32 devices in a mesh: ax: 4 (over z), circ: 8 (over y, x, core).
Axes of the slice: x: 2, y: 2, z: 4, core: 2. Of those that a mesh axis runs over, the one named last changes fastest.
Arguments:
- displacement: bfloat16 [64, 512, 6, 256], P('ax', 'circ'), may hold values from -6 to 6
- stiffness: bfloat16 [64, 512, 324], P('ax', 'circ'), may hold values from -0.875 to 0.875
- kernel: bfloat16 [128, 12, 2, 256, 256], P(('ax', 'circ')), may hold values from -0.109375 to 0.109375
- areas: float32 [32768], P(('ax', 'circ')), may hold values from 0.25 to 4
- near_cells: int32 [128, 12], P(('ax', 'circ')), may hold values from 0 to 15, all different within a row
- source_owner: int32 [131072, 1], P(('ax', 'circ')), may hold values from 0 to 7; in each aligned block of 4096 rows (0 to 4095, 4096 to 8191, ...) at most 1280 rows name the same one
- source_node: int32 [131072], P(('ax', 'circ')), may hold values from 0 to 1023
- target_owner: int32 [32768, 1], P(('ax', 'circ')), may hold values from 0 to 7; in each aligned block of 1024 rows (0 to 1023, 1024 to 2047, ...) at most 320 rows name the same one
- target_node: int32 [32768], P(('ax', 'circ')), may hold values from 0 to 1023
Outputs:
- shell_force: float32 [64, 512, 6, 256], P('ax', 'circ')
- pressure: float32 [2, 32768, 256], P(None, ('ax', 'circ'))
The draws below stay inside these ranges and needn't reach their ends.
Inputs may be any that keep to these rules, and one draw needn't show every extreme that they name: `source_owner`: in the rows of one device no sector is named by more than 1280 rows. `target_owner`: in the rows of one device no sector is named by more than 320 rows. `near_cells`: the 12 entries of a row are distinct.
All inputs are finite; a program needn't handle non-finite values.
Results may differ from the reference program's by a relative error of at most 0.0019.
Values may be sent and summed in bfloat16 or wider, within the bound.
No kernel may reach another device: no remote copies, remote signals or barrier semaphores. Data moves between devices by JAX's collectives and lax.ppermute only.
A program may use at most 256 MiB of HBM per device.

```python
import math
import jax
import jax.numpy as jnp
import numpy as np
from jax import lax

NODE_AX = 16
NODE_CIRC = 64
DOF = 6
VECS = 256
PANEL = 256
CELL_DEV = 4
NEAR = 12
SRC_CELLS = 16
SLOTS = 4096
TARGETS_DEV = 1024
CAP_V = 1280
CAP_L = 320
AXIAL = 64
CIRCUM = 512
CELLS_ALL = 128
SLOTS_ALL = 131072
TARGETS_ALL = 32768
N_AX = 4
N_CIRC = 8


def with_ends(drawn, stream_key, least, high):
    longest = drawn.shape.index(max(drawn.shape))
    spots = []
    for shift in (0, 1):
        where = [jax.random.randint(jax.random.fold_in(stream_key, axis), (), 0, length) for axis, length in enumerate(drawn.shape)]
        where[longest] = (where[longest] + shift) % drawn.shape[longest]
        spots.append(tuple(where))
    return drawn.at[spots[0]].set(least).at[spots[1]].set(high)


def level_of(own_key, shape, split, least, top_value):
    def one(position, parts):
        heights = jax.random.uniform(jax.random.fold_in(jax.random.fold_in(own_key, 6), position), (parts,), jnp.float32, least / len(split), top_value / len(split))
        return jnp.repeat(jnp.exp(heights), shape[position] // parts).reshape((-1,) + (1,) * (len(shape) - position - 1))

    factor_of = one(*split[0])
    for cut in split[1:]:
        factor_of = factor_of * one(*cut)
    return factor_of


def picks_of(rng, rows, count, top, lift):
    ranking = jax.random.permutation(jax.random.fold_in(rng, 1), count)
    boost = ranking
    for power in range(3):
        boost = boost * boost // count
    boost = boost * lift // count
    lots = jax.random.randint(jax.random.fold_in(rng, 2), (rows, count), 0, 4096) + boost
    fixed_rows = jax.random.permutation(jax.random.fold_in(rng, 3), rows)[jnp.arange(count) % rows]
    lots = jnp.where(jnp.arange(rows)[:, None] == fixed_rows[None, :], 1 << 14, lots)
    score = lots * count + jnp.arange(count)
    return lax.top_k(score.astype(jnp.int32), top)[1].astype(jnp.int32)


def assign_block(own_key, own, number, rows, count, top, reach, slope):
    order = jax.random.permutation(own_key, count)
    crowded, usual = load_shares(count, rows * top, reach, slope, True), load_shares(count, rows * top, reach, slope, False)
    places = jnp.arange(count)

    def named(lengths, offset_by):
        used = int((lengths > 0).sum())
        fixed = max(1, used // 4)
        moved = fixed + (places - fixed + offset_by * (used - fixed)) % max(1, count - fixed)
        return jnp.zeros((count,), jnp.int32).at[order[jnp.where(places < fixed, places, moved)]].set(jnp.asarray(lengths, jnp.int32))

    lengths = jnp.where(number % 4 == 0, named(crowded, number // 4), named(usual, number - number // 4 - 1))
    mixed = jax.random.permutation(jax.random.fold_in(own, 3), count)
    source_of, sink = mixed[0:count // 2 * 2:2], mixed[1:count // 2 * 2:2]
    slack = jnp.minimum(lengths[source_of] - 1, reach - lengths[sink]) // 2
    slack = jnp.where((source_of == order[0]) | (sink == order[0]) | (lengths[sink] == 0), 0, jnp.maximum(slack, 0))
    moved = jax.random.randint(jax.random.fold_in(own, 4), (count // 2,), 0, 1 << 20) % (slack + 1)
    lengths = lengths.at[source_of].add(-moved).at[sink].add(moved)
    items = jnp.searchsorted(jnp.cumsum(lengths), jnp.arange(rows * top), side="right").astype(jnp.int32)
    listing = items.reshape(top, rows).T
    listing = listing[jax.random.permutation(jax.random.fold_in(own, 1), rows)]
    offset_by = jax.random.randint(jax.random.fold_in(own, 2), (rows, 1), 0, top)
    return jnp.take_along_axis(listing, (jnp.arange(top)[None, :] + offset_by) % top, axis=1)


def load_shares(amount, total, bound, lean, full):
    loads = [(1 << 20) // math.isqrt(rank ** lean) + 1 for rank in range(1, amount + 1)]
    largest = bound if full else min(bound, max(-(-total // amount), total * loads[0] // sum(loads)))
    least = 1 if total - largest >= amount - 1 else 0
    given, surplus = [largest] + [least] * (amount - 1), total - largest - least * (amount - 1)
    while surplus > 0:
        free = [i for i in range(1, amount) if given[i] < largest] or [i for i in range(1, amount) if given[i] < bound]
        whole, budget = sum([loads[i] for i in free]), surplus
        for i in free:
            more = min(bound - given[i], max(1, budget * loads[i] // whole), surplus)
            given[i] = given[i] + more
            surplus = surplus - more
    return np.array(given)


def scatter_about(rng, extent, scale, most, shards=(), kind=jnp.bfloat16):
    result = scale * jax.random.normal(rng, extent, jnp.float32)
    if shards:
        result = result * level_of(rng, extent, shards, -0.22, 0.18)
    return jnp.clip(result, -most, most).astype(kind)


def setup_inputs(seed: int = 0) -> dict:
    keys = jax.random.split(jax.random.key(seed), 10)
    displacement = scatter_about(keys[0], (AXIAL, CIRCUM, DOF, VECS), 1.0, 6.0, ((0, 4), (1, 8)))
    stiffness = scatter_about(keys[1], (AXIAL, CIRCUM, 9 * DOF * DOF), (9 * DOF) ** -0.5, 0.875, ((0, 4), (1, 8)))
    kernel = scatter_about(keys[2], (CELLS_ALL, NEAR, 2, PANEL, PANEL), (NEAR * PANEL) ** -0.5, 0.109375, ((0, 32),))
    areas = jnp.clip(jnp.exp(math.log(4.0) - 2.7725887 * jax.random.uniform(keys[3], (TARGETS_ALL,), jnp.float32) ** level_of(keys[3], (TARGETS_ALL,), ((0, 32),), -0.2, 0.2)), 0.25, 4.0)
    near_cells = picks_of(keys[4], CELLS_ALL, SRC_CELLS, NEAR, 0)
    source_owner_keys = jax.random.split(jax.random.fold_in(keys[5], 1), SLOTS_ALL // SLOTS)
    source_owner_turns = jax.random.permutation(jax.random.fold_in(keys[5], 3), SLOTS_ALL // SLOTS)
    source_owner = jax.vmap(lambda own, number: assign_block(jax.random.fold_in(keys[5], 2), own, number, SLOTS, N_CIRC, 1, CAP_V, 1))(source_owner_keys, source_owner_turns).reshape((SLOTS_ALL, 1))
    source_node = with_ends(jax.random.randint(keys[6], (SLOTS_ALL,), 0, NODE_AX * NODE_CIRC), jax.random.fold_in(keys[6], 1), 0, (NODE_AX * NODE_CIRC) - 1).astype(jnp.int32)
    target_owner_keys = jax.random.split(jax.random.fold_in(keys[7], 1), TARGETS_ALL // TARGETS_DEV)
    target_owner_turns = jax.random.permutation(jax.random.fold_in(keys[7], 3), TARGETS_ALL // TARGETS_DEV)
    target_owner = jax.vmap(lambda own, number: assign_block(jax.random.fold_in(keys[7], 2), own, number, TARGETS_DEV, N_CIRC, 1, CAP_L, 1))(target_owner_keys, target_owner_turns).reshape((TARGETS_ALL, 1))
    target_node = with_ends(jax.random.randint(keys[8], (TARGETS_ALL,), 0, NODE_AX * NODE_CIRC), jax.random.fold_in(keys[8], 1), 0, (NODE_AX * NODE_CIRC) - 1).astype(jnp.int32)
    return dict(displacement=displacement, stiffness=stiffness, kernel=kernel, areas=areas, near_cells=near_cells, source_owner=source_owner, source_node=source_node, target_owner=target_owner, target_node=target_node)


def reference(displacement, stiffness, kernel, areas, near_cells, source_owner, source_node, target_owner, target_node):
    axial = NODE_AX * N_AX
    circum = NODE_CIRC * N_CIRC
    devices_all = N_AX * N_CIRC
    extended = jnp.pad(displacement.astype(jnp.float32), ((1, 1), (0, 0), (0, 0), (0, 0)))
    extended = jnp.concatenate([extended[:, -1:], extended, extended[:, :1]], axis=1)
    blocks = stiffness.reshape(axial, circum, 9, DOF, DOF)
    shell_force = jnp.zeros((axial, circum, DOF, VECS), jnp.float32)
    for offset in range(9):
        step_axial = offset // 3 - 1
        step_around = offset % 3 - 1
        source = extended[1 + step_axial:1 + step_axial + axial, 1 + step_around:1 + step_around + circum]
        shell_force = shell_force + jnp.einsum("acij,acjr->acir", blocks[:, :, offset].astype(jnp.float32), source, precision=lax.Precision.HIGHEST)
    radial = displacement[:, :, 0, :]
    slot_device = jnp.arange(SLOTS_ALL, dtype=jnp.int32) // SLOTS
    slot_axial = slot_device // N_CIRC
    row_index = slot_axial * NODE_AX + source_node // NODE_CIRC
    col_index = source_owner[:, 0] * NODE_CIRC + source_node % NODE_CIRC
    velocity = radial[row_index, col_index]
    cell_rows = velocity.reshape(devices_all, SRC_CELLS, PANEL, VECS)
    near_all = near_cells.reshape(devices_all, CELL_DEV, NEAR)
    kernel_all = kernel.reshape(devices_all, CELL_DEV, NEAR, 2, PANEL, PANEL)

    def one_device(item):
        kernel_dev, near_dev, cells_dev = item
        gathered = cells_dev[near_dev].astype(jnp.float32)
        return jnp.einsum("tnkij,tnjr->ktir", kernel_dev.astype(jnp.float32), gathered, precision=lax.Precision.HIGHEST)

    computed = lax.map(one_device, (kernel_all, near_all, cell_rows))
    pressure = jnp.transpose(computed, (1, 0, 2, 3, 4)).reshape(2, TARGETS_ALL, VECS)
    load_low = (areas[:, None] * pressure[0]).astype(jnp.bfloat16)
    load_value = lax.optimization_barrier(load_low).astype(jnp.float32)
    target_device = jnp.arange(TARGETS_ALL, dtype=jnp.int32) // TARGETS_DEV
    target_axial = target_device // N_CIRC
    load_row = target_axial * NODE_AX + target_node // NODE_CIRC
    load_col = target_owner[:, 0] * NODE_CIRC + target_node % NODE_CIRC
    shell_force = shell_force.at[load_row, load_col, 0].add(-load_value)
    return shell_force, pressure
```

```python
import jax
import jax.numpy as jnp
from jax import lax
from jax.experimental import pallas as pl
from jax.experimental.pallas import tpu as pltpu
from jax.sharding import PartitionSpec as P


def extended(cells, sides, width):
    for axis, dim in sides:
        count = lax.axis_size(axis)
        head = lax.slice_in_dim(cells, 0, width, axis=dim)
        tail = lax.slice_in_dim(cells, cells.shape[dim] - width, cells.shape[dim], axis=dim)
        cells = jnp.concatenate(
            [
                lax.ppermute(tail, axis, [(i, (i + 1) % count) for i in range(count)]),
                cells,
                lax.ppermute(head, axis, [((i + 1) % count, i) for i in range(count)]),
            ],
            axis=dim,
        )
    return cells


def slot_positions(owners, sectors, capacity):
    onehot = (owners[:, None] == jnp.arange(sectors, dtype=jnp.int32)[None, :]).astype(jnp.int32)
    before = jnp.cumsum(onehot, axis=0) - onehot
    ranking = jnp.sum(before * onehot, axis=1)
    return owners * capacity + ranking


def pressure_kernel(near_ref, kern_ref, vel_ref, area_ref, p_ref, load_ref):
    g = pl.program_id(0)
    near_count = kern_ref.shape[1]
    panel = kern_ref.shape[3]
    for n in range(near_count):
        m = near_ref[g, n]
        w = kern_ref[0, n].reshape(2 * panel, panel)
        prod = jnp.dot(w, vel_ref[m], preferred_element_type=jnp.float32)
        if n == 0:
            p_ref[...] = prod.reshape(p_ref.shape)
        else:
            p_ref[...] += prod.reshape(p_ref.shape)
    load_ref[...] = (area_ref[...] * p_ref[0]).astype(load_ref.dtype)


def near_field(kernel, source_cells, areas, near_cells):
    cells_dev, near_count, _, panel, _ = kernel.shape
    src_cells, _, vectors = source_cells.shape
    targets = cells_dev * panel
    grid_spec = pltpu.PrefetchScalarGridSpec(
        num_scalar_prefetch=1,
        grid=(cells_dev,),
        in_specs=[
            pl.BlockSpec((1, near_count, 2, panel, panel), lambda g, near: (g, 0, 0, 0, 0)),
            pl.BlockSpec((src_cells, panel, vectors), lambda g, near: (0, 0, 0)),
            pl.BlockSpec((panel, 1), lambda g, near: (g, 0)),
        ],
        out_specs=[
            pl.BlockSpec((2, panel, vectors), lambda g, near: (0, g, 0)),
            pl.BlockSpec((panel, vectors), lambda g, near: (g, 0)),
        ],
    )
    return pl.pallas_call(
        pressure_kernel,
        grid_spec=grid_spec,
        out_shape=[
            jax.ShapeDtypeStruct((2, targets, vectors), jnp.float32),
            jax.ShapeDtypeStruct((targets, vectors), jnp.bfloat16),
        ],
    )(near_cells, kernel, source_cells, areas.reshape(targets, 1))


def body(
    displacement,
    stiffness,
    kernel,
    areas,
    near_cells,
    source_owner,
    source_node,
    target_owner,
    target_node,
):
    axial_rows = displacement.shape[0]
    circum_rows = displacement.shape[1]
    degrees = displacement.shape[2]
    vectors = displacement.shape[3]
    sectors = lax.axis_size("circ")
    axial_total = axial_rows * lax.axis_size("ax")
    node_count = axial_rows * circum_rows

    radial = displacement[:, :, 0, :].reshape(node_count, vectors)
    table = lax.all_gather(radial, "circ", axis=0, tiled=True)
    slot_index = source_owner[:, 0] * node_count + source_node
    velocity = jnp.take(table, slot_index, axis=0, mode="clip")

    padded = extended(displacement, (("ax", 0), ("circ", 1)), 1)
    blocks = stiffness.reshape(axial_rows, circum_rows, 9, degrees, degrees)
    global_row = lax.axis_index("ax") * axial_rows + jnp.arange(axial_rows, dtype=jnp.int32)
    stiff = None
    for offset in range(9):
        step_axial = offset // 3 - 1
        step_around = offset % 3 - 1
        inside = ((global_row + step_axial >= 0) & (global_row + step_axial < axial_total)).astype(
            blocks.dtype
        )
        block_now = blocks[:, :, offset] * inside[:, None, None, None]
        source = padded[
            1 + step_axial : 1 + step_axial + axial_rows,
            1 + step_around : 1 + step_around + circum_rows,
        ]
        part = jnp.einsum(
            "acij,acjr->acir", block_now, source, preferred_element_type=jnp.float32
        )
        stiff = part if stiff is None else stiff + part

    panel_size = kernel.shape[3]
    source_cells = velocity.reshape(-1, panel_size, vectors)
    pressure, load_value = near_field(kernel, source_cells, areas, near_cells)

    load_owner = target_owner[:, 0]
    target_count = load_owner.shape[0]
    load_capacity = 5 * target_count // (2 * sectors)
    load_slot = slot_positions(load_owner, sectors, load_capacity)
    gather_slot = (
        load_slot[None, :] == jnp.arange(sectors * load_capacity, dtype=jnp.int32)[:, None]
    ).astype(jnp.bfloat16)
    outgoing = jnp.dot(gather_slot, load_value, preferred_element_type=jnp.float32).astype(
        jnp.bfloat16
    )
    outgoing = outgoing.reshape(sectors, load_capacity, vectors)
    node_slot = (
        jnp.full((sectors * load_capacity,), -1, jnp.int32)
        .at[load_slot]
        .set(target_node)
        .reshape(sectors, load_capacity)
    )
    arrived = lax.all_to_all(outgoing, "circ", split_axis=0, concat_axis=0, tiled=True)
    arrived_node = lax.all_to_all(node_slot, "circ", split_axis=0, concat_axis=0, tiled=True)
    selector = (
        arrived_node.reshape(-1)[None, :] == jnp.arange(node_count, dtype=jnp.int32)[:, None]
    ).astype(jnp.bfloat16)
    fluid = jnp.dot(selector, arrived.reshape(-1, vectors), preferred_element_type=jnp.float32)
    stiff = stiff.reshape(axial_rows, circum_rows, degrees, vectors)
    dof_first = (jnp.arange(degrees, dtype=jnp.int32) == 0).astype(jnp.float32)
    shell_force = stiff - dof_first[None, None, :, None] * fluid.reshape(
        axial_rows, circum_rows, 1, vectors
    )
    return (shell_force, pressure)


def solution(mesh):
    return jax.shard_map(
        body,
        mesh=mesh,
        in_specs=(
            P("ax", "circ", None, None),
            P("ax", "circ", None),
            P(("ax", "circ"), None, None, None, None),
            P(("ax", "circ")),
            P(("ax", "circ"), None),
            P(("ax", "circ"), None),
            P(("ax", "circ")),
            P(("ax", "circ"), None),
            P(("ax", "circ")),
        ),
        out_specs=(P("ax", "circ", None, None), P(None, ("ax", "circ"), None)),
        check_vma=False,
    )
```

```python
import functools

import jax
import jax.numpy as jnp
from jax import lax
from jax.experimental import pallas as pl
from jax.experimental.pallas import tpu as pltpu
from jax.sharding import PartitionSpec as P


def extended(cells, sides, width):
    for axis, dim in sides:
        count = lax.axis_size(axis)
        head = lax.slice_in_dim(cells, 0, width, axis=dim)
        tail = lax.slice_in_dim(cells, cells.shape[dim] - width, cells.shape[dim], axis=dim)
        cells = jnp.concatenate(
            [
                lax.ppermute(tail, axis, [(i, (i + 1) % count) for i in range(count)]),
                cells,
                lax.ppermute(head, axis, [((i + 1) % count, i) for i in range(count)]),
            ],
            axis=dim,
        )
    return cells


def slot_positions(owners, sectors, capacity):
    onehot = (owners[:, None] == jnp.arange(sectors, dtype=jnp.int32)[None, :]).astype(jnp.int32)
    before = jnp.cumsum(onehot, axis=0) - onehot
    ranking = jnp.sum(before * onehot, axis=1)
    return owners * capacity + ranking


def pressure_kernel(near_ref, kern_ref, vel_ref, area_ref, p_ref, load_ref):
    g = pl.program_id(0)
    near_count = kern_ref.shape[1]
    panel = kern_ref.shape[3]
    for n in range(near_count):
        m = near_ref[g, n]
        w = kern_ref[0, n].reshape(2 * panel, panel)
        prod = jnp.dot(w, vel_ref[m], preferred_element_type=jnp.float32)
        if n == 0:
            p_ref[...] = prod.reshape(p_ref.shape)
        else:
            p_ref[...] += prod.reshape(p_ref.shape)
    load_ref[...] = (area_ref[...] * p_ref[0]).astype(load_ref.dtype)


def near_field(kernel, source_cells, areas, near_cells):
    cells_dev, near_count, _, panel, _ = kernel.shape
    src_cells, _, vectors = source_cells.shape
    targets = cells_dev * panel
    grid_spec = pltpu.PrefetchScalarGridSpec(
        num_scalar_prefetch=1,
        grid=(cells_dev,),
        in_specs=[
            pl.BlockSpec((1, near_count, 2, panel, panel), lambda g, near: (g, 0, 0, 0, 0)),
            pl.BlockSpec((src_cells, panel, vectors), lambda g, near: (0, 0, 0)),
            pl.BlockSpec((panel, 1), lambda g, near: (g, 0)),
        ],
        out_specs=[
            pl.BlockSpec((2, panel, vectors), lambda g, near: (0, g, 0)),
            pl.BlockSpec((panel, vectors), lambda g, near: (g, 0)),
        ],
    )
    return pl.pallas_call(
        pressure_kernel,
        grid_spec=grid_spec,
        out_shape=[
            jax.ShapeDtypeStruct((2, targets, vectors), jnp.float32),
            jax.ShapeDtypeStruct((targets, vectors), jnp.bfloat16),
        ],
    )(near_cells, kernel, source_cells, areas.reshape(targets, 1))


def stiff_kernel(s_ref, rows_ref, fluid_ref, out_ref, sel_ref, band_ref, *, degrees):
    a = pl.program_id(0)
    nodes = s_ref.shape[1]
    offsets = band_ref.shape[0]
    group = 128
    span = offsets * degrees
    wide = ((band_ref.shape[2] + group - 1) // group) * group

    @pl.when(a == 0)
    def _():
        k = lax.broadcasted_iota(jnp.int32, sel_ref.shape, 0)
        y = lax.broadcasted_iota(jnp.int32, sel_ref.shape, 1)
        blk = y // group
        lane = y % group
        target = (
            (blk // degrees) * (offsets * degrees * degrees)
            + (lane // degrees) * (degrees * degrees)
            + (blk % degrees) * degrees
            + lane % degrees
        )
        sel_ref[...] = jnp.where((lane < span) & (k == target), 1.0, 0.0).astype(sel_ref.dtype)

    spread = jnp.dot(s_ref[0], sel_ref[...], preferred_element_type=jnp.float32)
    pad = jnp.zeros((nodes, wide - group), jnp.float32)
    for d in range(offsets):
        for i in range(degrees):
            blk = d * degrees + i
            piece = jnp.concatenate([spread[:, blk * group : (blk + 1) * group], pad], axis=1)
            parts = []
            for g in range(nodes // 8):
                rows = piece[g * 8 : (g + 1) * 8]
                if g:
                    rows = pltpu.roll(rows, g * 8 * degrees, 1)
                parts.append(pltpu.roll(rows, 0, 1, stride=degrees, stride_axis=0))
            skewed = jnp.concatenate(parts, axis=0)
            band_ref[d, i * nodes : (i + 1) * nodes, :] = skewed[:, : band_ref.shape[2]].astype(
                band_ref.dtype
            )
    acc = None
    for d in range(offsets):
        part = jnp.dot(band_ref[d], rows_ref[a + d], preferred_element_type=jnp.float32)
        acc = part if acc is None else acc + part
    out_ref[0, :nodes, :] = acc[:nodes] - fluid_ref[0]
    out_ref[0, nodes:, :] = acc[nodes:]


def banded_force(blocks, rows_in, fluid, degrees):
    axial_rows, nodes, width = blocks.shape
    offsets = 3
    band_cols = rows_in.shape[1]
    vectors = rows_in.shape[-1]
    band_rows = degrees * nodes
    return pl.pallas_call(
        functools.partial(stiff_kernel, degrees=degrees),
        grid=(axial_rows,),
        in_specs=[
            pl.BlockSpec((1, nodes, width), lambda a: (a, 0, 0)),
            pl.BlockSpec(rows_in.shape, lambda a: (0, 0, 0)),
            pl.BlockSpec((1, nodes, vectors), lambda a: (a, 0, 0)),
        ],
        out_specs=pl.BlockSpec((1, band_rows, vectors), lambda a: (a, 0, 0)),
        out_shape=jax.ShapeDtypeStruct((axial_rows, band_rows, vectors), jnp.float32),
        scratch_shapes=[
            pltpu.VMEM((width, offsets * degrees * 128), jnp.bfloat16),
            pltpu.VMEM((offsets, band_rows, band_cols), jnp.bfloat16),
        ],
    )(blocks, rows_in, fluid)


def body(
    displacement,
    stiffness,
    kernel,
    areas,
    near_cells,
    source_owner,
    source_node,
    target_owner,
    target_node,
):
    axial_rows = displacement.shape[0]
    circum_rows = displacement.shape[1]
    degrees = displacement.shape[2]
    vectors = displacement.shape[3]
    sectors = lax.axis_size("circ")
    axial_total = axial_rows * lax.axis_size("ax")
    node_count = axial_rows * circum_rows

    radial = displacement[:, :, 0, :].reshape(node_count, vectors)
    table = lax.all_gather(radial, "circ", axis=0, tiled=True)
    slot_index = source_owner[:, 0] * node_count + source_node
    velocity = jnp.take(table, slot_index, axis=0, mode="clip")

    padded = extended(displacement, (("ax", 0), ("circ", 1)), 1)
    rows_in = padded.reshape(axial_rows + 2, (circum_rows + 2) * degrees, vectors)
    global_row = lax.axis_index("ax") * axial_rows + jnp.arange(axial_rows, dtype=jnp.int32)
    lane_step = jnp.arange(stiffness.shape[2], dtype=jnp.int32) // (3 * degrees * degrees) - 1
    inside = (global_row[:, None] + lane_step[None, :] >= 0) & (
        global_row[:, None] + lane_step[None, :] < axial_total
    )
    blocks = jnp.where(inside[:, None, :], stiffness, jnp.zeros_like(stiffness))

    panel_size = kernel.shape[3]
    source_cells = velocity.reshape(-1, panel_size, vectors)
    pressure, load_value = near_field(kernel, source_cells, areas, near_cells)

    load_owner = target_owner[:, 0]
    target_count = load_owner.shape[0]
    load_capacity = 5 * target_count // (2 * sectors)
    load_slot = slot_positions(load_owner, sectors, load_capacity)
    gather_slot = (
        load_slot[None, :] == jnp.arange(sectors * load_capacity, dtype=jnp.int32)[:, None]
    ).astype(jnp.bfloat16)
    outgoing = jnp.dot(gather_slot, load_value, preferred_element_type=jnp.float32).astype(
        jnp.bfloat16
    )
    outgoing = outgoing.reshape(sectors, load_capacity, vectors)
    node_slot = (
        jnp.full((sectors * load_capacity,), -1, jnp.int32)
        .at[load_slot]
        .set(target_node)
        .reshape(sectors, load_capacity)
    )
    arrived = lax.all_to_all(outgoing, "circ", split_axis=0, concat_axis=0, tiled=True)
    arrived_node = lax.all_to_all(node_slot, "circ", split_axis=0, concat_axis=0, tiled=True)
    selector = (
        arrived_node.reshape(-1)[None, :] == jnp.arange(node_count, dtype=jnp.int32)[:, None]
    ).astype(jnp.bfloat16)
    fluid = jnp.dot(selector, arrived.reshape(-1, vectors), preferred_element_type=jnp.float32)
    fluid = fluid.reshape(axial_rows, circum_rows, vectors)
    force = banded_force(blocks, rows_in, fluid, degrees)
    shell_force = jnp.transpose(
        force.reshape(axial_rows, degrees, circum_rows, vectors), (0, 2, 1, 3)
    )
    return (shell_force, pressure)


def solution(mesh):
    return jax.shard_map(
        body,
        mesh=mesh,
        in_specs=(
            P("ax", "circ", None, None),
            P("ax", "circ", None),
            P(("ax", "circ"), None, None, None, None),
            P(("ax", "circ")),
            P(("ax", "circ"), None),
            P(("ax", "circ"), None),
            P(("ax", "circ")),
            P(("ax", "circ"), None),
            P(("ax", "circ")),
        ),
        out_specs=(P("ax", "circ", None, None), P(None, ("ax", "circ"), None)),
        check_vma=False,
    )
```

```python
import functools

import jax
import jax.numpy as jnp
from jax import lax
from jax.experimental import pallas as pl
from jax.experimental.pallas import tpu as pltpu
from jax.sharding import PartitionSpec as P


def extended(cells, sides, width):
    for axis, dim in sides:
        count = lax.axis_size(axis)
        head = lax.slice_in_dim(cells, 0, width, axis=dim)
        tail = lax.slice_in_dim(cells, cells.shape[dim] - width, cells.shape[dim], axis=dim)
        cells = jnp.concatenate(
            [
                lax.ppermute(tail, axis, [(i, (i + 1) % count) for i in range(count)]),
                cells,
                lax.ppermute(head, axis, [((i + 1) % count, i) for i in range(count)]),
            ],
            axis=dim,
        )
    return cells


def slot_positions(owners, sectors, capacity):
    onehot = (owners[:, None] == jnp.arange(sectors, dtype=jnp.int32)[None, :]).astype(jnp.int32)
    before = jnp.cumsum(onehot, axis=0) - onehot
    ranking = jnp.sum(before * onehot, axis=1)
    return owners * capacity + ranking


def pressure_kernel(near_ref, kern_ref, vel_ref, area_ref, p_ref, load_ref):
    g = pl.program_id(0)
    near_count = kern_ref.shape[1]
    panel = kern_ref.shape[3]
    for n in range(near_count):
        m = near_ref[g, n]
        w = kern_ref[0, n].reshape(2 * panel, panel)
        prod = jnp.dot(w, vel_ref[m], preferred_element_type=jnp.float32)
        if n == 0:
            p_ref[...] = prod.reshape(p_ref.shape)
        else:
            p_ref[...] += prod.reshape(p_ref.shape)
    load_ref[...] = (area_ref[...] * p_ref[0]).astype(load_ref.dtype)


def near_field(kernel, source_cells, areas, near_cells):
    cells_dev, near_count, _, panel, _ = kernel.shape
    src_cells, _, vectors = source_cells.shape
    targets = cells_dev * panel
    grid_spec = pltpu.PrefetchScalarGridSpec(
        num_scalar_prefetch=1,
        grid=(cells_dev,),
        in_specs=[
            pl.BlockSpec((1, near_count, 2, panel, panel), lambda g, near: (g, 0, 0, 0, 0)),
            pl.BlockSpec((src_cells, panel, vectors), lambda g, near: (0, 0, 0)),
            pl.BlockSpec((panel, 1), lambda g, near: (g, 0)),
        ],
        out_specs=[
            pl.BlockSpec((2, panel, vectors), lambda g, near: (0, g, 0)),
            pl.BlockSpec((panel, vectors), lambda g, near: (g, 0)),
        ],
    )
    return pl.pallas_call(
        pressure_kernel,
        grid_spec=grid_spec,
        out_shape=[
            jax.ShapeDtypeStruct((2, targets, vectors), jnp.float32),
            jax.ShapeDtypeStruct((targets, vectors), jnp.bfloat16),
        ],
    )(near_cells, kernel, source_cells, areas.reshape(targets, 1))


def stiff_kernel(s_ref, rows_ref, out_ref, sel_ref, band_ref, *, degrees):
    a = pl.program_id(0)
    nodes = s_ref.shape[1]
    offsets = band_ref.shape[0]
    group = 128
    span = offsets * degrees
    wide = ((band_ref.shape[2] + group - 1) // group) * group

    @pl.when(a == 0)
    def _():
        k = lax.broadcasted_iota(jnp.int32, sel_ref.shape, 0)
        y = lax.broadcasted_iota(jnp.int32, sel_ref.shape, 1)
        blk = y // group
        lane = y % group
        target = (
            (blk // degrees) * (offsets * degrees * degrees)
            + (lane // degrees) * (degrees * degrees)
            + (blk % degrees) * degrees
            + lane % degrees
        )
        sel_ref[...] = jnp.where((lane < span) & (k == target), 1.0, 0.0).astype(sel_ref.dtype)

    spread = jnp.dot(s_ref[0], sel_ref[...], preferred_element_type=jnp.float32)
    pad = jnp.zeros((nodes, wide - group), jnp.float32)
    for d in range(offsets):
        for i in range(degrees):
            blk = d * degrees + i
            piece = jnp.concatenate([spread[:, blk * group : (blk + 1) * group], pad], axis=1)
            parts = []
            for g in range(nodes // 8):
                rows = piece[g * 8 : (g + 1) * 8]
                if g:
                    rows = pltpu.roll(rows, g * 8 * degrees, 1)
                parts.append(pltpu.roll(rows, 0, 1, stride=degrees, stride_axis=0))
            skewed = jnp.concatenate(parts, axis=0)
            band_ref[d, i * nodes : (i + 1) * nodes, :] = skewed[:, : band_ref.shape[2]].astype(
                band_ref.dtype
            )
    acc = None
    for d in range(offsets):
        part = jnp.dot(band_ref[d], rows_ref[a + d], preferred_element_type=jnp.float32)
        acc = part if acc is None else acc + part
    out_ref[0] = acc


def banded_force(blocks, rows_in, degrees):
    axial_rows, nodes, width = blocks.shape
    offsets = 3
    band_cols = rows_in.shape[1]
    vectors = rows_in.shape[-1]
    band_rows = degrees * nodes
    return pl.pallas_call(
        functools.partial(stiff_kernel, degrees=degrees),
        grid=(axial_rows,),
        in_specs=[
            pl.BlockSpec((1, nodes, width), lambda a: (a, 0, 0)),
            pl.BlockSpec(rows_in.shape, lambda a: (0, 0, 0)),
        ],
        out_specs=pl.BlockSpec((1, band_rows, vectors), lambda a: (a, 0, 0)),
        out_shape=jax.ShapeDtypeStruct((axial_rows, band_rows, vectors), jnp.float32),
        scratch_shapes=[
            pltpu.VMEM((width, offsets * degrees * 128), jnp.bfloat16),
            pltpu.VMEM((offsets, band_rows, band_cols), jnp.bfloat16),
        ],
    )(blocks, rows_in)


def body(
    displacement,
    stiffness,
    kernel,
    areas,
    near_cells,
    source_owner,
    source_node,
    target_owner,
    target_node,
):
    axial_rows = displacement.shape[0]
    circum_rows = displacement.shape[1]
    degrees = displacement.shape[2]
    vectors = displacement.shape[3]
    sectors = lax.axis_size("circ")
    axial_total = axial_rows * lax.axis_size("ax")
    node_count = axial_rows * circum_rows

    radial = displacement[:, :, 0, :].reshape(node_count, vectors)
    table = lax.all_gather(radial, "circ", axis=0, tiled=True)

    padded = extended(displacement, (("ax", 0), ("circ", 1)), 1)
    rows_in = padded.reshape(axial_rows + 2, (circum_rows + 2) * degrees, vectors)
    global_row = lax.axis_index("ax") * axial_rows + jnp.arange(axial_rows, dtype=jnp.int32)
    lane_step = jnp.arange(stiffness.shape[2], dtype=jnp.int32) // (3 * degrees * degrees) - 1
    inside = (global_row[:, None] + lane_step[None, :] >= 0) & (
        global_row[:, None] + lane_step[None, :] < axial_total
    )
    blocks = jnp.where(inside[:, None, :], stiffness, jnp.zeros_like(stiffness))
    force = banded_force(blocks, rows_in, degrees)

    force, table = lax.optimization_barrier((force, table))
    slot_index = source_owner[:, 0] * node_count + source_node
    velocity = jnp.take(table, slot_index, axis=0, mode="clip")

    panel_size = kernel.shape[3]
    source_cells = velocity.reshape(-1, panel_size, vectors)
    pressure, load_value = near_field(kernel, source_cells, areas, near_cells)

    load_owner = target_owner[:, 0]
    target_count = load_owner.shape[0]
    load_capacity = 5 * target_count // (2 * sectors)
    load_slot = slot_positions(load_owner, sectors, load_capacity)
    gather_slot = (
        load_slot[None, :] == jnp.arange(sectors * load_capacity, dtype=jnp.int32)[:, None]
    ).astype(jnp.bfloat16)
    outgoing = jnp.dot(gather_slot, load_value, preferred_element_type=jnp.float32).astype(
        jnp.bfloat16
    )
    outgoing = outgoing.reshape(sectors, load_capacity, vectors)
    node_slot = (
        jnp.full((sectors * load_capacity,), -1, jnp.int32)
        .at[load_slot]
        .set(target_node)
        .reshape(sectors, load_capacity)
    )
    arrived = lax.all_to_all(outgoing, "circ", split_axis=0, concat_axis=0, tiled=True)
    arrived_node = lax.all_to_all(node_slot, "circ", split_axis=0, concat_axis=0, tiled=True)
    selector = (
        arrived_node.reshape(-1)[None, :] == jnp.arange(node_count, dtype=jnp.int32)[:, None]
    ).astype(jnp.bfloat16)
    fluid = jnp.dot(selector, arrived.reshape(-1, vectors), preferred_element_type=jnp.float32)
    fluid = fluid.reshape(axial_rows, circum_rows, vectors)
    force = force.at[:, :circum_rows, :].add(-fluid)
    shell_force = jnp.transpose(
        force.reshape(axial_rows, degrees, circum_rows, vectors), (0, 2, 1, 3)
    )
    return (shell_force, pressure)


def solution(mesh):
    return jax.shard_map(
        body,
        mesh=mesh,
        in_specs=(
            P("ax", "circ", None, None),
            P("ax", "circ", None),
            P(("ax", "circ"), None, None, None, None),
            P(("ax", "circ")),
            P(("ax", "circ"), None),
            P(("ax", "circ"), None),
            P(("ax", "circ")),
            P(("ax", "circ"), None),
            P(("ax", "circ")),
        ),
        out_specs=(P("ax", "circ", None, None), P(None, ("ax", "circ"), None)),
        check_vma=False,
    )
```

```python
import functools

import jax
import jax.numpy as jnp
from jax import lax
from jax.experimental import pallas as pl
from jax.experimental.pallas import tpu as pltpu
from jax.sharding import PartitionSpec as P


def extended(cells, sides, width):
    for axis, dim in sides:
        count = lax.axis_size(axis)
        head = lax.slice_in_dim(cells, 0, width, axis=dim)
        tail = lax.slice_in_dim(cells, cells.shape[dim] - width, cells.shape[dim], axis=dim)
        cells = jnp.concatenate(
            [
                lax.ppermute(tail, axis, [(i, (i + 1) % count) for i in range(count)]),
                cells,
                lax.ppermute(head, axis, [((i + 1) % count, i) for i in range(count)]),
            ],
            axis=dim,
        )
    return cells


def slot_positions(owners, sectors, capacity):
    onehot = (owners[:, None] == jnp.arange(sectors, dtype=jnp.int32)[None, :]).astype(jnp.int32)
    before = jnp.cumsum(onehot, axis=0) - onehot
    ranking = jnp.sum(before * onehot, axis=1)
    return owners * capacity + ranking


def pressure_kernel(near_ref, kern_ref, vel_ref, area_ref, p_ref, load_ref):
    g = pl.program_id(0)
    near_count = kern_ref.shape[1]
    panel = kern_ref.shape[3]
    for n in range(near_count):
        m = near_ref[g, n]
        w = kern_ref[0, n].reshape(2 * panel, panel)
        prod = jnp.dot(w, vel_ref[m], preferred_element_type=jnp.float32)
        if n == 0:
            p_ref[...] = prod.reshape(p_ref.shape)
        else:
            p_ref[...] += prod.reshape(p_ref.shape)
    load_ref[...] = (area_ref[...] * p_ref[0]).astype(load_ref.dtype)


def near_field(kernel, source_cells, areas, near_cells):
    cells_dev, near_count, _, panel, _ = kernel.shape
    src_cells, _, vectors = source_cells.shape
    targets = cells_dev * panel
    grid_spec = pltpu.PrefetchScalarGridSpec(
        num_scalar_prefetch=1,
        grid=(cells_dev,),
        in_specs=[
            pl.BlockSpec((1, near_count, 2, panel, panel), lambda g, near: (g, 0, 0, 0, 0)),
            pl.BlockSpec((src_cells, panel, vectors), lambda g, near: (0, 0, 0)),
            pl.BlockSpec((panel, 1), lambda g, near: (g, 0)),
        ],
        out_specs=[
            pl.BlockSpec((2, panel, vectors), lambda g, near: (0, g, 0)),
            pl.BlockSpec((panel, vectors), lambda g, near: (g, 0)),
        ],
    )
    return pl.pallas_call(
        pressure_kernel,
        grid_spec=grid_spec,
        out_shape=[
            jax.ShapeDtypeStruct((2, targets, vectors), jnp.float32),
            jax.ShapeDtypeStruct((targets, vectors), jnp.bfloat16),
        ],
    )(near_cells, kernel, source_cells, areas.reshape(targets, 1))


def stiff_kernel(s_ref, rows_ref, *rest, degrees, first):
    out_ref, sel_ref, band_ref = rest[-3:]
    step = pl.program_id(0)
    a = step + first
    nodes = s_ref.shape[1]
    offsets = band_ref.shape[0]
    group = 128
    span = offsets * degrees
    wide = ((band_ref.shape[2] + group - 1) // group) * group

    @pl.when(step == 0)
    def _():
        k = lax.broadcasted_iota(jnp.int32, sel_ref.shape, 0)
        y = lax.broadcasted_iota(jnp.int32, sel_ref.shape, 1)
        blk = y // group
        lane = y % group
        target = (
            (blk // degrees) * (offsets * degrees * degrees)
            + (lane // degrees) * (degrees * degrees)
            + (blk % degrees) * degrees
            + lane % degrees
        )
        sel_ref[...] = jnp.where((lane < span) & (k == target), 1.0, 0.0).astype(sel_ref.dtype)

    spread = jnp.dot(s_ref[0], sel_ref[...], preferred_element_type=jnp.float32)
    pad = jnp.zeros((nodes, wide - group), jnp.float32)
    for d in range(offsets):
        for i in range(degrees):
            blk = d * degrees + i
            piece = jnp.concatenate([spread[:, blk * group : (blk + 1) * group], pad], axis=1)
            parts = []
            for g in range(nodes // 8):
                rows = piece[g * 8 : (g + 1) * 8]
                if g:
                    rows = pltpu.roll(rows, g * 8 * degrees, 1)
                parts.append(pltpu.roll(rows, 0, 1, stride=degrees, stride_axis=0))
            skewed = jnp.concatenate(parts, axis=0)
            band_ref[d, i * nodes : (i + 1) * nodes, :] = skewed[:, : band_ref.shape[2]].astype(
                band_ref.dtype
            )
    acc = None
    for d in range(offsets):
        part = jnp.dot(band_ref[d], rows_ref[a + d], preferred_element_type=jnp.float32)
        acc = part if acc is None else acc + part
    out_ref[0] = acc


def banded_force(blocks, rows_in, degrees, first, count, previous=None):
    axial_rows, nodes, width = blocks.shape
    offsets = 3
    band_cols = rows_in.shape[1]
    vectors = rows_in.shape[-1]
    band_rows = degrees * nodes
    in_specs = [
        pl.BlockSpec((1, nodes, width), lambda a: (a + first, 0, 0)),
        pl.BlockSpec(rows_in.shape, lambda a: (0, 0, 0)),
    ]
    operands = [blocks, rows_in]
    aliases = {}
    if previous is not None:
        in_specs.append(pl.BlockSpec(memory_space=pl.ANY))
        operands.append(previous)
        aliases = {2: 0}
    return pl.pallas_call(
        functools.partial(stiff_kernel, degrees=degrees, first=first),
        grid=(count,),
        in_specs=in_specs,
        out_specs=pl.BlockSpec((1, band_rows, vectors), lambda a: (a + first, 0, 0)),
        out_shape=jax.ShapeDtypeStruct((axial_rows, band_rows, vectors), jnp.float32),
        scratch_shapes=[
            pltpu.VMEM((width, offsets * degrees * 128), jnp.bfloat16),
            pltpu.VMEM((offsets, band_rows, band_cols), jnp.bfloat16),
        ],
        input_output_aliases=aliases,
    )(*operands)


def body(
    displacement,
    stiffness,
    kernel,
    areas,
    near_cells,
    source_owner,
    source_node,
    target_owner,
    target_node,
):
    axial_rows = displacement.shape[0]
    circum_rows = displacement.shape[1]
    degrees = displacement.shape[2]
    vectors = displacement.shape[3]
    sectors = lax.axis_size("circ")
    axial_total = axial_rows * lax.axis_size("ax")
    node_count = axial_rows * circum_rows

    radial = displacement[:, :, 0, :].reshape(node_count, vectors)
    table = lax.all_gather(radial, "circ", axis=0, tiled=True)

    padded = extended(displacement, (("ax", 0), ("circ", 1)), 1)
    rows_in = padded.reshape(axial_rows + 2, (circum_rows + 2) * degrees, vectors)
    global_row = lax.axis_index("ax") * axial_rows + jnp.arange(axial_rows, dtype=jnp.int32)
    lane_step = jnp.arange(stiffness.shape[2], dtype=jnp.int32) // (3 * degrees * degrees) - 1
    inside = (global_row[:, None] + lane_step[None, :] >= 0) & (
        global_row[:, None] + lane_step[None, :] < axial_total
    )
    blocks = jnp.where(inside[:, None, :], stiffness, jnp.zeros_like(stiffness))
    half = axial_rows // 2
    force = banded_force(blocks, rows_in, degrees, 0, half)

    force, table = lax.optimization_barrier((force, table))
    slot_index = source_owner[:, 0] * node_count + source_node
    velocity = jnp.take(table, slot_index, axis=0, mode="clip")

    panel_size = kernel.shape[3]
    source_cells = velocity.reshape(-1, panel_size, vectors)
    pressure, load_value = near_field(kernel, source_cells, areas, near_cells)

    load_owner = target_owner[:, 0]
    target_count = load_owner.shape[0]
    load_capacity = 5 * target_count // (2 * sectors)
    load_slot = slot_positions(load_owner, sectors, load_capacity)
    gather_slot = (
        load_slot[None, :] == jnp.arange(sectors * load_capacity, dtype=jnp.int32)[:, None]
    ).astype(jnp.bfloat16)
    outgoing = jnp.dot(gather_slot, load_value, preferred_element_type=jnp.float32).astype(
        jnp.bfloat16
    )
    outgoing = outgoing.reshape(sectors, load_capacity, vectors)
    node_slot = (
        jnp.full((sectors * load_capacity,), -1, jnp.int32)
        .at[load_slot]
        .set(target_node)
        .reshape(sectors, load_capacity)
    )
    outgoing, force = lax.optimization_barrier((outgoing, force))
    arrived = lax.all_to_all(outgoing, "circ", split_axis=0, concat_axis=0, tiled=True)
    force = banded_force(blocks, rows_in, degrees, half, axial_rows - half, force)
    arrived_node = lax.all_to_all(node_slot, "circ", split_axis=0, concat_axis=0, tiled=True)
    selector = (
        arrived_node.reshape(-1)[None, :] == jnp.arange(node_count, dtype=jnp.int32)[:, None]
    ).astype(jnp.bfloat16)
    fluid = jnp.dot(selector, arrived.reshape(-1, vectors), preferred_element_type=jnp.float32)
    fluid = fluid.reshape(axial_rows, circum_rows, vectors)
    force = force.at[:, :circum_rows, :].add(-fluid)
    shell_force = jnp.transpose(
        force.reshape(axial_rows, degrees, circum_rows, vectors), (0, 2, 1, 3)
    )
    return (shell_force, pressure)


def solution(mesh):
    return jax.shard_map(
        body,
        mesh=mesh,
        in_specs=(
            P("ax", "circ", None, None),
            P("ax", "circ", None),
            P(("ax", "circ"), None, None, None, None),
            P(("ax", "circ")),
            P(("ax", "circ"), None),
            P(("ax", "circ"), None),
            P(("ax", "circ")),
            P(("ax", "circ"), None),
            P(("ax", "circ")),
        ),
        out_specs=(P("ax", "circ", None, None), P(None, ("ax", "circ"), None)),
        check_vma=False,
    )
```

```python
import functools

import jax
import jax.numpy as jnp
from jax import lax
from jax.experimental import pallas as pl
from jax.experimental.pallas import tpu as pltpu
from jax.sharding import PartitionSpec as P


def extended(cells, sides, width):
    for axis, dim in sides:
        count = lax.axis_size(axis)
        head = lax.slice_in_dim(cells, 0, width, axis=dim)
        tail = lax.slice_in_dim(cells, cells.shape[dim] - width, cells.shape[dim], axis=dim)
        cells = jnp.concatenate(
            [
                lax.ppermute(tail, axis, [(i, (i + 1) % count) for i in range(count)]),
                cells,
                lax.ppermute(head, axis, [((i + 1) % count, i) for i in range(count)]),
            ],
            axis=dim,
        )
    return cells


def slot_positions(owners, sectors, capacity):
    onehot = (owners[:, None] == jnp.arange(sectors, dtype=jnp.int32)[None, :]).astype(jnp.int32)
    before = jnp.cumsum(onehot, axis=0) - onehot
    ranking = jnp.sum(before * onehot, axis=1)
    return owners * capacity + ranking


def pressure_kernel(near_ref, kern_ref, vel_ref, area_ref, p_ref, load_ref):
    g = pl.program_id(0)
    near_count = kern_ref.shape[1]
    panel = kern_ref.shape[3]
    for n in range(near_count):
        m = near_ref[g, n]
        w = kern_ref[0, n].reshape(2 * panel, panel)
        prod = jnp.dot(w, vel_ref[m], preferred_element_type=jnp.float32)
        if n == 0:
            p_ref[...] = prod.reshape(p_ref.shape)
        else:
            p_ref[...] += prod.reshape(p_ref.shape)
    load_ref[...] = (area_ref[...] * p_ref[0]).astype(load_ref.dtype)


def near_field(kernel, source_cells, areas, near_cells):
    cells_dev, near_count, _, panel, _ = kernel.shape
    src_cells, _, vectors = source_cells.shape
    targets = cells_dev * panel
    grid_spec = pltpu.PrefetchScalarGridSpec(
        num_scalar_prefetch=1,
        grid=(cells_dev,),
        in_specs=[
            pl.BlockSpec((1, near_count, 2, panel, panel), lambda g, near: (g, 0, 0, 0, 0)),
            pl.BlockSpec((src_cells, panel, vectors), lambda g, near: (0, 0, 0)),
            pl.BlockSpec((panel, 1), lambda g, near: (g, 0)),
        ],
        out_specs=[
            pl.BlockSpec((2, panel, vectors), lambda g, near: (0, g, 0)),
            pl.BlockSpec((panel, vectors), lambda g, near: (g, 0)),
        ],
    )
    return pl.pallas_call(
        pressure_kernel,
        grid_spec=grid_spec,
        out_shape=[
            jax.ShapeDtypeStruct((2, targets, vectors), jnp.float32),
            jax.ShapeDtypeStruct((targets, vectors), jnp.bfloat16),
        ],
    )(near_cells, kernel, source_cells, areas.reshape(targets, 1))


def stiff_kernel(s_ref, rows_ref, top_ref, bottom_ref, halo_ref, *rest, degrees, first):
    out_ref, sel_ref, band_ref = rest[-3:]
    step = pl.program_id(0)
    a = step + first
    last = rows_ref.shape[0] - 1
    nodes = s_ref.shape[1]
    offsets = band_ref.shape[0]
    group = 128
    span = offsets * degrees
    wide = band_ref.shape[2]
    inner = nodes * degrees

    @pl.when(step == 0)
    def _():
        k = lax.broadcasted_iota(jnp.int32, sel_ref.shape, 0)
        y = lax.broadcasted_iota(jnp.int32, sel_ref.shape, 1)
        blk = y // group
        lane = y % group
        target = (
            (blk // degrees) * (offsets * degrees * degrees)
            + (lane // degrees) * (degrees * degrees)
            + (blk % degrees) * degrees
            + lane % degrees
        )
        sel_ref[...] = jnp.where((lane < span) & (k == target), 1.0, 0.0).astype(sel_ref.dtype)

    spread = jnp.dot(s_ref[0], sel_ref[...], preferred_element_type=jnp.float32)
    pad = jnp.zeros((nodes, wide - group), jnp.float32)
    for d in range(offsets):
        for i in range(degrees):
            blk = d * degrees + i
            piece = jnp.concatenate([spread[:, blk * group : (blk + 1) * group], pad], axis=1)
            parts = []
            for g in range(nodes // 8):
                rows = pltpu.roll(piece[g * 8 : (g + 1) * 8], (g * 8 * degrees - degrees) % wide, 1)
                parts.append(pltpu.roll(rows, 0, 1, stride=degrees, stride_axis=0))
            skewed = jnp.concatenate(parts, axis=0)
            band_ref[d, i * nodes : (i + 1) * nodes, :] = skewed.astype(band_ref.dtype)
    above = jnp.where(a == 0, top_ref[0], rows_ref[jnp.maximum(a - 1, 0)])
    below = jnp.where(a == last, bottom_ref[0], rows_ref[jnp.minimum(a + 1, last)])
    acc = None
    for d, rows in enumerate((above, rows_ref[a], below)):
        part = jnp.dot(band_ref[d, :, :inner], rows, preferred_element_type=jnp.float32)
        part += jnp.dot(band_ref[d, :, inner:], halo_ref[a + d], preferred_element_type=jnp.float32)
        acc = part if acc is None else acc + part
    out_ref[0] = acc


def banded_force(blocks, rows, top, bottom, halo, degrees, first, count, previous=None):
    axial_rows, nodes, width = blocks.shape
    offsets = 3
    vectors = rows.shape[-1]
    band_rows = degrees * nodes
    band_cols = band_rows + halo.shape[1]
    in_specs = [
        pl.BlockSpec((1, nodes, width), lambda a: (a + first, 0, 0)),
        pl.BlockSpec(rows.shape, lambda a: (0, 0, 0)),
        pl.BlockSpec(top.shape, lambda a: (0, 0, 0)),
        pl.BlockSpec(bottom.shape, lambda a: (0, 0, 0)),
        pl.BlockSpec(halo.shape, lambda a: (0, 0, 0)),
    ]
    operands = [blocks, rows, top, bottom, halo]
    aliases = {}
    if previous is not None:
        in_specs.append(pl.BlockSpec(memory_space=pl.ANY))
        operands.append(previous)
        aliases = {len(operands) - 1: 0}
    return pl.pallas_call(
        functools.partial(stiff_kernel, degrees=degrees, first=first),
        grid=(count,),
        in_specs=in_specs,
        out_specs=pl.BlockSpec((1, band_rows, vectors), lambda a: (a + first, 0, 0)),
        out_shape=jax.ShapeDtypeStruct((axial_rows, band_rows, vectors), jnp.float32),
        scratch_shapes=[
            pltpu.VMEM((width, offsets * degrees * 128), jnp.bfloat16),
            pltpu.VMEM((offsets, band_rows, band_cols), jnp.bfloat16),
        ],
        input_output_aliases=aliases,
    )(*operands)


def body(
    displacement,
    stiffness,
    kernel,
    areas,
    near_cells,
    source_owner,
    source_node,
    target_owner,
    target_node,
):
    axial_rows = displacement.shape[0]
    circum_rows = displacement.shape[1]
    degrees = displacement.shape[2]
    vectors = displacement.shape[3]
    sectors = lax.axis_size("circ")
    axial_total = axial_rows * lax.axis_size("ax")
    node_count = axial_rows * circum_rows

    radial = displacement[:, :, 0, :].reshape(node_count, vectors)
    table = lax.all_gather(radial, "circ", axis=0, tiled=True)

    node_rows = displacement.reshape(axial_rows, circum_rows * degrees, vectors)
    count_ax = lax.axis_size("ax")
    top = lax.ppermute(node_rows[-1:], "ax", [(i, (i + 1) % count_ax) for i in range(count_ax)])
    bottom = lax.ppermute(node_rows[:1], "ax", [((i + 1) % count_ax, i) for i in range(count_ax)])
    first_nodes = jnp.concatenate(
        [top[:, :degrees], node_rows[:, :degrees], bottom[:, :degrees]], axis=0
    )
    last_nodes = jnp.concatenate(
        [top[:, -degrees:], node_rows[:, -degrees:], bottom[:, -degrees:]], axis=0
    )
    left = lax.ppermute(last_nodes, "circ", [(i, (i + 1) % sectors) for i in range(sectors)])
    right = lax.ppermute(first_nodes, "circ", [((i + 1) % sectors, i) for i in range(sectors)])
    gap = jnp.zeros((axial_rows + 2, 128 - 2 * degrees, vectors), displacement.dtype)
    halo = jnp.concatenate([right, gap, left], axis=1)
    global_row = lax.axis_index("ax") * axial_rows + jnp.arange(axial_rows, dtype=jnp.int32)
    lane_step = jnp.arange(stiffness.shape[2], dtype=jnp.int32) // (3 * degrees * degrees) - 1
    inside = (global_row[:, None] + lane_step[None, :] >= 0) & (
        global_row[:, None] + lane_step[None, :] < axial_total
    )
    blocks = jnp.where(inside[:, None, :], stiffness, jnp.zeros_like(stiffness))
    half = axial_rows // 2
    force = banded_force(blocks, node_rows, top, bottom, halo, degrees, 0, half)

    force, table = lax.optimization_barrier((force, table))
    slot_index = source_owner[:, 0] * node_count + source_node
    velocity = jnp.take(table, slot_index, axis=0, mode="clip")

    panel_size = kernel.shape[3]
    source_cells = velocity.reshape(-1, panel_size, vectors)
    pressure, load_value = near_field(kernel, source_cells, areas, near_cells)

    load_owner = target_owner[:, 0]
    target_count = load_owner.shape[0]
    load_capacity = 5 * target_count // (2 * sectors)
    load_slot = slot_positions(load_owner, sectors, load_capacity)
    gather_slot = (
        load_slot[None, :] == jnp.arange(sectors * load_capacity, dtype=jnp.int32)[:, None]
    ).astype(jnp.bfloat16)
    outgoing = jnp.dot(gather_slot, load_value, preferred_element_type=jnp.float32).astype(
        jnp.bfloat16
    )
    outgoing = outgoing.reshape(sectors, load_capacity, vectors)
    node_slot = (
        jnp.full((sectors * load_capacity,), -1, jnp.int32)
        .at[load_slot]
        .set(target_node)
        .reshape(sectors, load_capacity)
    )
    outgoing, force = lax.optimization_barrier((outgoing, force))
    arrived = lax.all_to_all(outgoing, "circ", split_axis=0, concat_axis=0, tiled=True)
    force = banded_force(
        blocks, node_rows, top, bottom, halo, degrees, half, axial_rows - half, force
    )
    arrived_node = lax.all_to_all(node_slot, "circ", split_axis=0, concat_axis=0, tiled=True)
    selector = (
        arrived_node.reshape(-1)[None, :] == jnp.arange(node_count, dtype=jnp.int32)[:, None]
    ).astype(jnp.bfloat16)
    fluid = jnp.dot(selector, arrived.reshape(-1, vectors), preferred_element_type=jnp.float32)
    fluid = fluid.reshape(axial_rows, circum_rows, vectors)
    force = force.at[:, :circum_rows, :].add(-fluid)
    shell_force = jnp.transpose(
        force.reshape(axial_rows, degrees, circum_rows, vectors), (0, 2, 1, 3)
    )
    return (shell_force, pressure)


def solution(mesh):
    return jax.shard_map(
        body,
        mesh=mesh,
        in_specs=(
            P("ax", "circ", None, None),
            P("ax", "circ", None),
            P(("ax", "circ"), None, None, None, None),
            P(("ax", "circ")),
            P(("ax", "circ"), None),
            P(("ax", "circ"), None),
            P(("ax", "circ")),
            P(("ax", "circ"), None),
            P(("ax", "circ")),
        ),
        out_specs=(P("ax", "circ", None, None), P(None, ("ax", "circ"), None)),
        check_vma=False,
    )
```

```python
import functools

import jax
import jax.numpy as jnp
from jax import lax
from jax.experimental import pallas as pl
from jax.experimental.pallas import tpu as pltpu
from jax.sharding import PartitionSpec as P


def extended(cells, sides, width):
    for axis, dim in sides:
        count = lax.axis_size(axis)
        head = lax.slice_in_dim(cells, 0, width, axis=dim)
        tail = lax.slice_in_dim(cells, cells.shape[dim] - width, cells.shape[dim], axis=dim)
        cells = jnp.concatenate(
            [
                lax.ppermute(tail, axis, [(i, (i + 1) % count) for i in range(count)]),
                cells,
                lax.ppermute(head, axis, [((i + 1) % count, i) for i in range(count)]),
            ],
            axis=dim,
        )
    return cells


def slot_positions(owners, sectors, capacity):
    onehot = (owners[:, None] == jnp.arange(sectors, dtype=jnp.int32)[None, :]).astype(jnp.int32)
    before = jnp.cumsum(onehot, axis=0) - onehot
    ranking = jnp.sum(before * onehot, axis=1)
    return owners * capacity + ranking


def pressure_kernel(near_ref, kern_ref, vel_ref, area_ref, p_ref, load_ref):
    g = pl.program_id(0)
    near_count = kern_ref.shape[1]
    panel = kern_ref.shape[3]
    for n in range(near_count):
        m = near_ref[g, n]
        w = kern_ref[0, n].reshape(2 * panel, panel)
        prod = jnp.dot(w, vel_ref[m], preferred_element_type=jnp.float32)
        if n == 0:
            p_ref[...] = prod.reshape(p_ref.shape)
        else:
            p_ref[...] += prod.reshape(p_ref.shape)
    load_ref[...] = (area_ref[...] * p_ref[0]).astype(load_ref.dtype)


def near_field(kernel, source_cells, areas, near_cells):
    cells_dev, near_count, _, panel, _ = kernel.shape
    src_cells, _, vectors = source_cells.shape
    targets = cells_dev * panel
    grid_spec = pltpu.PrefetchScalarGridSpec(
        num_scalar_prefetch=1,
        grid=(cells_dev,),
        in_specs=[
            pl.BlockSpec((1, near_count, 2, panel, panel), lambda g, near: (g, 0, 0, 0, 0)),
            pl.BlockSpec((src_cells, panel, vectors), lambda g, near: (0, 0, 0)),
            pl.BlockSpec((panel, 1), lambda g, near: (g, 0)),
        ],
        out_specs=[
            pl.BlockSpec((2, panel, vectors), lambda g, near: (0, g, 0)),
            pl.BlockSpec((panel, vectors), lambda g, near: (g, 0)),
        ],
    )
    return pl.pallas_call(
        pressure_kernel,
        grid_spec=grid_spec,
        out_shape=[
            jax.ShapeDtypeStruct((2, targets, vectors), jnp.float32),
            jax.ShapeDtypeStruct((targets, vectors), jnp.bfloat16),
        ],
    )(near_cells, kernel, source_cells, areas.reshape(targets, 1))


def stiff_kernel(s_ref, rows_ref, top_ref, bottom_ref, halo_ref, *rest, degrees, first):
    out_ref, sel_ref, band_ref = rest[-3:]
    step = pl.program_id(0)
    a = step + first
    last = rows_ref.shape[0] - 1
    nodes = s_ref.shape[1]
    offsets = band_ref.shape[0]
    group = 128
    span = offsets * degrees
    wide = band_ref.shape[2]
    inner = nodes * degrees

    @pl.when(step == 0)
    def _():
        k = lax.broadcasted_iota(jnp.int32, sel_ref.shape, 0)
        y = lax.broadcasted_iota(jnp.int32, sel_ref.shape, 1)
        blk = y // group
        lane = y % group
        target = (
            (blk // degrees) * (offsets * degrees * degrees)
            + (lane // degrees) * (degrees * degrees)
            + (blk % degrees) * degrees
            + lane % degrees
        )
        sel_ref[...] = jnp.where((lane < span) & (k == target), 1.0, 0.0).astype(sel_ref.dtype)

    spread = jnp.dot(s_ref[0], sel_ref[...], preferred_element_type=jnp.float32)
    pad = jnp.zeros((nodes, wide - group), jnp.float32)
    for d in range(offsets):
        for i in range(degrees):
            blk = d * degrees + i
            piece = jnp.concatenate([spread[:, blk * group : (blk + 1) * group], pad], axis=1)
            parts = []
            for g in range(nodes // 8):
                rows = pltpu.roll(piece[g * 8 : (g + 1) * 8], (g * 8 * degrees - degrees) % wide, 1)
                parts.append(pltpu.roll(rows, 0, 1, stride=degrees, stride_axis=0))
            skewed = jnp.concatenate(parts, axis=0)
            band_ref[d, i * nodes : (i + 1) * nodes, :] = skewed.astype(band_ref.dtype)
    above = jnp.where(a == 0, top_ref[0], rows_ref[jnp.maximum(a - 1, 0)])
    below = jnp.where(a == last, bottom_ref[0], rows_ref[jnp.minimum(a + 1, last)])
    acc = None
    for d, rows in enumerate((above, rows_ref[a], below)):
        part = jnp.dot(band_ref[d, :, :inner], rows, preferred_element_type=jnp.float32)
        part += jnp.dot(band_ref[d, :, inner:], halo_ref[a + d], preferred_element_type=jnp.float32)
        acc = part if acc is None else acc + part
    out_ref[0] = acc


def banded_force(blocks, rows, top, bottom, halo, degrees, first, count, previous=None):
    axial_rows, nodes, width = blocks.shape
    offsets = 3
    vectors = rows.shape[-1]
    band_rows = degrees * nodes
    band_cols = band_rows + halo.shape[1]
    in_specs = [
        pl.BlockSpec((1, nodes, width), lambda a: (a + first, 0, 0)),
        pl.BlockSpec(rows.shape, lambda a: (0, 0, 0)),
        pl.BlockSpec(top.shape, lambda a: (0, 0, 0)),
        pl.BlockSpec(bottom.shape, lambda a: (0, 0, 0)),
        pl.BlockSpec(halo.shape, lambda a: (0, 0, 0)),
    ]
    operands = [blocks, rows, top, bottom, halo]
    aliases = {}
    if previous is not None:
        in_specs.append(pl.BlockSpec(memory_space=pl.ANY))
        operands.append(previous)
        aliases = {len(operands) - 1: 0}
    return pl.pallas_call(
        functools.partial(stiff_kernel, degrees=degrees, first=first),
        grid=(count,),
        in_specs=in_specs,
        out_specs=pl.BlockSpec((1, band_rows, vectors), lambda a: (a + first, 0, 0)),
        out_shape=jax.ShapeDtypeStruct((axial_rows, band_rows, vectors), jnp.float32),
        scratch_shapes=[
            pltpu.VMEM((width, offsets * degrees * 128), jnp.bfloat16),
            pltpu.VMEM((offsets, band_rows, band_cols), jnp.bfloat16),
        ],
        input_output_aliases=aliases,
    )(*operands)


def body(
    displacement,
    stiffness,
    kernel,
    areas,
    near_cells,
    source_owner,
    source_node,
    target_owner,
    target_node,
):
    axial_rows = displacement.shape[0]
    circum_rows = displacement.shape[1]
    degrees = displacement.shape[2]
    vectors = displacement.shape[3]
    sectors = lax.axis_size("circ")
    node_count = axial_rows * circum_rows

    radial = displacement[:, :, 0, :].reshape(node_count, vectors)
    table = lax.all_gather(radial, "circ", axis=0, tiled=True)

    node_rows = displacement.reshape(axial_rows, circum_rows * degrees, vectors)
    count_ax = lax.axis_size("ax")
    top = lax.ppermute(node_rows[-1:], "ax", [(i, (i + 1) % count_ax) for i in range(count_ax)])
    bottom = lax.ppermute(node_rows[:1], "ax", [((i + 1) % count_ax, i) for i in range(count_ax)])
    ax_index = lax.axis_index("ax")
    top = jnp.where(ax_index == 0, jnp.zeros_like(top), top)
    bottom = jnp.where(ax_index == count_ax - 1, jnp.zeros_like(bottom), bottom)
    first_nodes = jnp.concatenate(
        [top[:, :degrees], node_rows[:, :degrees], bottom[:, :degrees]], axis=0
    )
    last_nodes = jnp.concatenate(
        [top[:, -degrees:], node_rows[:, -degrees:], bottom[:, -degrees:]], axis=0
    )
    left = lax.ppermute(last_nodes, "circ", [(i, (i + 1) % sectors) for i in range(sectors)])
    right = lax.ppermute(first_nodes, "circ", [((i + 1) % sectors, i) for i in range(sectors)])
    gap = jnp.zeros((axial_rows + 2, 128 - 2 * degrees, vectors), displacement.dtype)
    halo = jnp.concatenate([right, gap, left], axis=1)
    blocks = stiffness
    half = axial_rows // 2
    force = banded_force(blocks, node_rows, top, bottom, halo, degrees, 0, half)

    force, table = lax.optimization_barrier((force, table))
    slot_index = source_owner[:, 0] * node_count + source_node
    velocity = jnp.take(table, slot_index, axis=0, mode="clip")

    panel_size = kernel.shape[3]
    source_cells = velocity.reshape(-1, panel_size, vectors)
    pressure, load_value = near_field(kernel, source_cells, areas, near_cells)

    load_owner = target_owner[:, 0]
    target_count = load_owner.shape[0]
    load_capacity = 5 * target_count // (2 * sectors)
    load_slot = slot_positions(load_owner, sectors, load_capacity)
    gather_slot = (
        load_slot[None, :] == jnp.arange(sectors * load_capacity, dtype=jnp.int32)[:, None]
    ).astype(jnp.bfloat16)
    outgoing = jnp.dot(gather_slot, load_value, preferred_element_type=jnp.float32).astype(
        jnp.bfloat16
    )
    outgoing = outgoing.reshape(sectors, load_capacity, vectors)
    node_slot = jnp.dot(
        gather_slot.astype(jnp.float32),
        target_node.astype(jnp.float32),
        precision=lax.Precision.HIGHEST,
    )
    node_slot = jnp.round(node_slot).astype(jnp.int32).reshape(sectors, load_capacity)
    outgoing, force = lax.optimization_barrier((outgoing, force))
    arrived = lax.all_to_all(outgoing, "circ", split_axis=0, concat_axis=0, tiled=True)
    force = banded_force(
        blocks, node_rows, top, bottom, halo, degrees, half, axial_rows - half, force
    )
    arrived_node = lax.all_to_all(node_slot, "circ", split_axis=0, concat_axis=0, tiled=True)
    selector = (
        arrived_node.reshape(-1)[None, :] == jnp.arange(node_count, dtype=jnp.int32)[:, None]
    ).astype(jnp.bfloat16)
    fluid = jnp.dot(selector, arrived.reshape(-1, vectors), preferred_element_type=jnp.float32)
    fluid = fluid.reshape(axial_rows, circum_rows, vectors)
    force = force.at[:, :circum_rows, :].add(-fluid)
    shell_force = jnp.transpose(
        force.reshape(axial_rows, degrees, circum_rows, vectors), (0, 2, 1, 3)
    )
    return (shell_force, pressure)


def solution(mesh):
    return jax.shard_map(
        body,
        mesh=mesh,
        in_specs=(
            P("ax", "circ", None, None),
            P("ax", "circ", None),
            P(("ax", "circ"), None, None, None, None),
            P(("ax", "circ")),
            P(("ax", "circ"), None),
            P(("ax", "circ"), None),
            P(("ax", "circ")),
            P(("ax", "circ"), None),
            P(("ax", "circ")),
        ),
        out_specs=(P("ax", "circ", None, None), P(None, ("ax", "circ"), None)),
        check_vma=False,
    )
```

```python
import functools

import jax
import jax.numpy as jnp
from jax import lax
from jax.experimental import pallas as pl
from jax.experimental.pallas import tpu as pltpu
from jax.sharding import PartitionSpec as P


def extended(cells, sides, width):
    for axis, dim in sides:
        count = lax.axis_size(axis)
        head = lax.slice_in_dim(cells, 0, width, axis=dim)
        tail = lax.slice_in_dim(cells, cells.shape[dim] - width, cells.shape[dim], axis=dim)
        cells = jnp.concatenate(
            [
                lax.ppermute(tail, axis, [(i, (i + 1) % count) for i in range(count)]),
                cells,
                lax.ppermute(head, axis, [((i + 1) % count, i) for i in range(count)]),
            ],
            axis=dim,
        )
    return cells


def slot_positions(owners, sectors, capacity):
    onehot = (owners[:, None] == jnp.arange(sectors, dtype=jnp.int32)[None, :]).astype(jnp.int32)
    before = jnp.cumsum(onehot, axis=0) - onehot
    ranking = jnp.sum(before * onehot, axis=1)
    return owners * capacity + ranking


def pressure_kernel(near_ref, kern_ref, vel_ref, area_ref, p_ref, load_ref):
    g = pl.program_id(0)
    near_count = kern_ref.shape[1]
    panel = kern_ref.shape[3]
    for n in range(near_count):
        m = near_ref[g, n]
        w = kern_ref[0, n].reshape(2 * panel, panel)
        prod = jnp.dot(w, vel_ref[m], preferred_element_type=jnp.float32)
        if n == 0:
            p_ref[...] = prod.reshape(p_ref.shape)
        else:
            p_ref[...] += prod.reshape(p_ref.shape)
    load_ref[...] = (area_ref[...] * p_ref[0]).astype(load_ref.dtype)


def near_field(kernel, source_cells, areas, near_cells):
    cells_dev, near_count, _, panel, _ = kernel.shape
    src_cells, _, vectors = source_cells.shape
    targets = cells_dev * panel
    grid_spec = pltpu.PrefetchScalarGridSpec(
        num_scalar_prefetch=1,
        grid=(cells_dev,),
        in_specs=[
            pl.BlockSpec((1, near_count, 2, panel, panel), lambda g, near: (g, 0, 0, 0, 0)),
            pl.BlockSpec((src_cells, panel, vectors), lambda g, near: (0, 0, 0)),
            pl.BlockSpec((panel, 1), lambda g, near: (g, 0)),
        ],
        out_specs=[
            pl.BlockSpec((2, panel, vectors), lambda g, near: (0, g, 0)),
            pl.BlockSpec((panel, vectors), lambda g, near: (g, 0)),
        ],
    )
    return pl.pallas_call(
        pressure_kernel,
        grid_spec=grid_spec,
        out_shape=[
            jax.ShapeDtypeStruct((2, targets, vectors), jnp.float32),
            jax.ShapeDtypeStruct((targets, vectors), jnp.bfloat16),
        ],
    )(near_cells, kernel, source_cells, areas.reshape(targets, 1))


def stiff_kernel(s_ref, rows_ref, top_ref, bottom_ref, halo_ref, *rest, degrees, first):
    out_ref, sel_ref, band_ref = rest[-3:]
    step = pl.program_id(0)
    a = step + first
    last = rows_ref.shape[0] - 1
    nodes = s_ref.shape[1]
    offsets = band_ref.shape[0]
    group = 128
    span = offsets * degrees
    wide = band_ref.shape[2]

    @pl.when(step == 0)
    def _():
        k = lax.broadcasted_iota(jnp.int32, sel_ref.shape, 0)
        y = lax.broadcasted_iota(jnp.int32, sel_ref.shape, 1)
        blk = y // group
        lane = y % group
        target = (
            (blk // degrees) * (offsets * degrees * degrees)
            + (lane // degrees) * (degrees * degrees)
            + (blk % degrees) * degrees
            + lane % degrees
        )
        sel_ref[...] = jnp.where((lane < span) & (k == target), 1.0, 0.0).astype(sel_ref.dtype)

    spread = jnp.dot(s_ref[0], sel_ref[...], preferred_element_type=jnp.float32)
    pad = jnp.zeros((nodes, wide - group), jnp.float32)
    for d in range(offsets):
        for i in range(degrees):
            blk = d * degrees + i
            piece = jnp.concatenate([spread[:, blk * group : (blk + 1) * group], pad], axis=1)
            parts = []
            for g in range(nodes // 8):
                rows = pltpu.roll(piece[g * 8 : (g + 1) * 8], (g * 8 * degrees - degrees) % wide, 1)
                parts.append(pltpu.roll(rows, 0, 1, stride=degrees, stride_axis=0))
            skewed = jnp.concatenate(parts, axis=0)
            band_ref[d, i * nodes : (i + 1) * nodes, :] = skewed.astype(band_ref.dtype)
    above = jnp.where(a == 0, top_ref[0], rows_ref[jnp.maximum(a - 1, 0)])
    below = jnp.where(a == last, bottom_ref[0], rows_ref[jnp.minimum(a + 1, last)])
    acc = None
    for d, rows in enumerate((above, rows_ref[a], below)):
        both = jnp.concatenate([rows, halo_ref[a + d]], axis=0)
        part = jnp.dot(band_ref[d], both, preferred_element_type=jnp.float32)
        acc = part if acc is None else acc + part
    out_ref[0] = acc


def banded_force(blocks, rows, top, bottom, halo, degrees, first, count, previous=None):
    axial_rows, nodes, width = blocks.shape
    offsets = 3
    vectors = rows.shape[-1]
    band_rows = degrees * nodes
    band_cols = band_rows + halo.shape[1]
    in_specs = [
        pl.BlockSpec((1, nodes, width), lambda a: (a + first, 0, 0)),
        pl.BlockSpec(rows.shape, lambda a: (0, 0, 0)),
        pl.BlockSpec(top.shape, lambda a: (0, 0, 0)),
        pl.BlockSpec(bottom.shape, lambda a: (0, 0, 0)),
        pl.BlockSpec(halo.shape, lambda a: (0, 0, 0)),
    ]
    operands = [blocks, rows, top, bottom, halo]
    aliases = {}
    if previous is not None:
        in_specs.append(pl.BlockSpec(memory_space=pl.ANY))
        operands.append(previous)
        aliases = {len(operands) - 1: 0}
    return pl.pallas_call(
        functools.partial(stiff_kernel, degrees=degrees, first=first),
        grid=(count,),
        in_specs=in_specs,
        out_specs=pl.BlockSpec((1, band_rows, vectors), lambda a: (a + first, 0, 0)),
        out_shape=jax.ShapeDtypeStruct((axial_rows, band_rows, vectors), jnp.float32),
        scratch_shapes=[
            pltpu.VMEM((width, offsets * degrees * 128), jnp.bfloat16),
            pltpu.VMEM((offsets, band_rows, band_cols), jnp.bfloat16),
        ],
        input_output_aliases=aliases,
    )(*operands)


def body(
    displacement,
    stiffness,
    kernel,
    areas,
    near_cells,
    source_owner,
    source_node,
    target_owner,
    target_node,
):
    axial_rows = displacement.shape[0]
    circum_rows = displacement.shape[1]
    degrees = displacement.shape[2]
    vectors = displacement.shape[3]
    sectors = lax.axis_size("circ")
    axial_total = axial_rows * lax.axis_size("ax")
    node_count = axial_rows * circum_rows

    radial = displacement[:, :, 0, :].reshape(node_count, vectors)
    table = lax.all_gather(radial, "circ", axis=0, tiled=True)

    node_rows = displacement.reshape(axial_rows, circum_rows * degrees, vectors)
    count_ax = lax.axis_size("ax")
    top = lax.ppermute(node_rows[-1:], "ax", [(i, (i + 1) % count_ax) for i in range(count_ax)])
    bottom = lax.ppermute(node_rows[:1], "ax", [((i + 1) % count_ax, i) for i in range(count_ax)])
    first_nodes = jnp.concatenate(
        [top[:, :degrees], node_rows[:, :degrees], bottom[:, :degrees]], axis=0
    )
    last_nodes = jnp.concatenate(
        [top[:, -degrees:], node_rows[:, -degrees:], bottom[:, -degrees:]], axis=0
    )
    left = lax.ppermute(last_nodes, "circ", [(i, (i + 1) % sectors) for i in range(sectors)])
    right = lax.ppermute(first_nodes, "circ", [((i + 1) % sectors, i) for i in range(sectors)])
    gap = jnp.zeros((axial_rows + 2, 128 - 2 * degrees, vectors), displacement.dtype)
    halo = jnp.concatenate([right, gap, left], axis=1)
    global_row = lax.axis_index("ax") * axial_rows + jnp.arange(axial_rows, dtype=jnp.int32)
    lane_step = jnp.arange(stiffness.shape[2], dtype=jnp.int32) // (3 * degrees * degrees) - 1
    inside = (global_row[:, None] + lane_step[None, :] >= 0) & (
        global_row[:, None] + lane_step[None, :] < axial_total
    )
    blocks = jnp.where(inside[:, None, :], stiffness, jnp.zeros_like(stiffness))
    half = axial_rows // 2
    force = banded_force(blocks, node_rows, top, bottom, halo, degrees, 0, half)

    force, table = lax.optimization_barrier((force, table))
    slot_index = source_owner[:, 0] * node_count + source_node
    velocity = jnp.take(table, slot_index, axis=0, mode="clip")

    panel_size = kernel.shape[3]
    source_cells = velocity.reshape(-1, panel_size, vectors)
    pressure, load_value = near_field(kernel, source_cells, areas, near_cells)

    load_owner = target_owner[:, 0]
    target_count = load_owner.shape[0]
    load_capacity = 5 * target_count // (2 * sectors)
    load_slot = slot_positions(load_owner, sectors, load_capacity)
    gather_slot = (
        load_slot[None, :] == jnp.arange(sectors * load_capacity, dtype=jnp.int32)[:, None]
    ).astype(jnp.bfloat16)
    outgoing = jnp.dot(gather_slot, load_value, preferred_element_type=jnp.float32).astype(
        jnp.bfloat16
    )
    outgoing = outgoing.reshape(sectors, load_capacity, vectors)
    node_slot = (
        jnp.full((sectors * load_capacity,), -1, jnp.int32)
        .at[load_slot]
        .set(target_node)
        .reshape(sectors, load_capacity)
    )
    outgoing, force = lax.optimization_barrier((outgoing, force))
    arrived = lax.all_to_all(outgoing, "circ", split_axis=0, concat_axis=0, tiled=True)
    force = banded_force(
        blocks, node_rows, top, bottom, halo, degrees, half, axial_rows - half, force
    )
    arrived_node = lax.all_to_all(node_slot, "circ", split_axis=0, concat_axis=0, tiled=True)
    selector = (
        arrived_node.reshape(-1)[None, :] == jnp.arange(node_count, dtype=jnp.int32)[:, None]
    ).astype(jnp.bfloat16)
    fluid = jnp.dot(selector, arrived.reshape(-1, vectors), preferred_element_type=jnp.float32)
    fluid = fluid.reshape(axial_rows, circum_rows, vectors)
    force = force.at[:, :circum_rows, :].add(-fluid)
    shell_force = jnp.transpose(
        force.reshape(axial_rows, degrees, circum_rows, vectors), (0, 2, 1, 3)
    )
    return (shell_force, pressure)


def solution(mesh):
    return jax.shard_map(
        body,
        mesh=mesh,
        in_specs=(
            P("ax", "circ", None, None),
            P("ax", "circ", None),
            P(("ax", "circ"), None, None, None, None),
            P(("ax", "circ")),
            P(("ax", "circ"), None),
            P(("ax", "circ"), None),
            P(("ax", "circ")),
            P(("ax", "circ"), None),
            P(("ax", "circ")),
        ),
        out_specs=(P("ax", "circ", None, None), P(None, ("ax", "circ"), None)),
        check_vma=False,
    )
```

```python
import functools

import jax
import jax.numpy as jnp
from jax import lax
from jax.experimental import pallas as pl
from jax.experimental.pallas import tpu as pltpu
from jax.sharding import PartitionSpec as P


def extended(cells, sides, width):
    for axis, dim in sides:
        count = lax.axis_size(axis)
        head = lax.slice_in_dim(cells, 0, width, axis=dim)
        tail = lax.slice_in_dim(cells, cells.shape[dim] - width, cells.shape[dim], axis=dim)
        cells = jnp.concatenate(
            [
                lax.ppermute(tail, axis, [(i, (i + 1) % count) for i in range(count)]),
                cells,
                lax.ppermute(head, axis, [((i + 1) % count, i) for i in range(count)]),
            ],
            axis=dim,
        )
    return cells


def slot_positions(owners, sectors, capacity):
    onehot = (owners[:, None] == jnp.arange(sectors, dtype=jnp.int32)[None, :]).astype(jnp.int32)
    before = jnp.cumsum(onehot, axis=0) - onehot
    ranking = jnp.sum(before * onehot, axis=1)
    return owners * capacity + ranking


def pressure_kernel(near_ref, kern_ref, vel_ref, area_ref, p_ref, load_ref):
    g = pl.program_id(0)
    chunk = pl.program_id(1)
    per_chunk = kern_ref.shape[1]
    panel = kern_ref.shape[3]
    acc = None
    for n in range(per_chunk):
        m = near_ref[g, chunk * per_chunk + n]
        w = kern_ref[0, n].reshape(2 * panel, panel)
        prod = jnp.dot(w, vel_ref[m], preferred_element_type=jnp.float32)
        acc = prod if acc is None else acc + prod
    acc = acc.reshape(p_ref.shape)

    @pl.when(chunk == 0)
    def _():
        p_ref[...] = acc

    @pl.when(chunk > 0)
    def _():
        p_ref[...] += acc

    @pl.when(chunk == pl.num_programs(1) - 1)
    def _():
        load_ref[...] = (area_ref[...] * p_ref[0]).astype(load_ref.dtype)


def near_field(kernel, source_cells, areas, near_cells):
    cells_dev, near_count, _, panel, _ = kernel.shape
    src_cells, _, vectors = source_cells.shape
    targets = cells_dev * panel
    per_chunk = 4 if near_count % 4 == 0 else near_count
    grid_spec = pltpu.PrefetchScalarGridSpec(
        num_scalar_prefetch=1,
        grid=(cells_dev, near_count // per_chunk),
        in_specs=[
            pl.BlockSpec((1, per_chunk, 2, panel, panel), lambda g, c, near: (g, c, 0, 0, 0)),
            pl.BlockSpec((src_cells, panel, vectors), lambda g, c, near: (0, 0, 0)),
            pl.BlockSpec((panel, 1), lambda g, c, near: (g, 0)),
        ],
        out_specs=[
            pl.BlockSpec((2, panel, vectors), lambda g, c, near: (0, g, 0)),
            pl.BlockSpec((panel, vectors), lambda g, c, near: (g, 0)),
        ],
    )
    return pl.pallas_call(
        pressure_kernel,
        grid_spec=grid_spec,
        out_shape=[
            jax.ShapeDtypeStruct((2, targets, vectors), jnp.float32),
            jax.ShapeDtypeStruct((targets, vectors), jnp.bfloat16),
        ],
    )(near_cells, kernel, source_cells, areas.reshape(targets, 1))


def stiff_kernel(s_ref, rows_ref, top_ref, bottom_ref, halo_ref, *rest, degrees, first):
    out_ref, sel_ref, band_ref = rest[-3:]
    step = pl.program_id(0)
    a = step + first
    last = rows_ref.shape[0] - 1
    nodes = s_ref.shape[1]
    offsets = band_ref.shape[0]
    group = 128
    span = offsets * degrees
    wide = band_ref.shape[2]

    @pl.when(step == 0)
    def _():
        k = lax.broadcasted_iota(jnp.int32, sel_ref.shape, 0)
        y = lax.broadcasted_iota(jnp.int32, sel_ref.shape, 1)
        blk = y // group
        lane = y % group
        target = (
            (blk // degrees) * (offsets * degrees * degrees)
            + (lane // degrees) * (degrees * degrees)
            + (blk % degrees) * degrees
            + lane % degrees
        )
        sel_ref[...] = jnp.where((lane < span) & (k == target), 1.0, 0.0).astype(sel_ref.dtype)

    spread = jnp.dot(s_ref[0], sel_ref[...], preferred_element_type=jnp.float32)
    pad = jnp.zeros((nodes, wide - group), jnp.float32)
    for d in range(offsets):
        for i in range(degrees):
            blk = d * degrees + i
            piece = jnp.concatenate([spread[:, blk * group : (blk + 1) * group], pad], axis=1)
            parts = []
            for g in range(nodes // 8):
                rows = pltpu.roll(piece[g * 8 : (g + 1) * 8], (g * 8 * degrees - degrees) % wide, 1)
                parts.append(pltpu.roll(rows, 0, 1, stride=degrees, stride_axis=0))
            skewed = jnp.concatenate(parts, axis=0)
            band_ref[d, i * nodes : (i + 1) * nodes, :] = skewed.astype(band_ref.dtype)
    above = jnp.where(a == 0, top_ref[0], rows_ref[jnp.maximum(a - 1, 0)])
    below = jnp.where(a == last, bottom_ref[0], rows_ref[jnp.minimum(a + 1, last)])
    acc = None
    for d, rows in enumerate((above, rows_ref[a], below)):
        both = jnp.concatenate([rows, halo_ref[a + d]], axis=0)
        part = jnp.dot(band_ref[d], both, preferred_element_type=jnp.float32)
        acc = part if acc is None else acc + part
    out_ref[0] = acc


def banded_force(blocks, rows, top, bottom, halo, degrees, first, count, previous=None):
    axial_rows, nodes, width = blocks.shape
    offsets = 3
    vectors = rows.shape[-1]
    band_rows = degrees * nodes
    band_cols = band_rows + halo.shape[1]
    in_specs = [
        pl.BlockSpec((1, nodes, width), lambda a: (a + first, 0, 0)),
        pl.BlockSpec(rows.shape, lambda a: (0, 0, 0)),
        pl.BlockSpec(top.shape, lambda a: (0, 0, 0)),
        pl.BlockSpec(bottom.shape, lambda a: (0, 0, 0)),
        pl.BlockSpec(halo.shape, lambda a: (0, 0, 0)),
    ]
    operands = [blocks, rows, top, bottom, halo]
    aliases = {}
    if previous is not None:
        in_specs.append(pl.BlockSpec(memory_space=pl.ANY))
        operands.append(previous)
        aliases = {len(operands) - 1: 0}
    return pl.pallas_call(
        functools.partial(stiff_kernel, degrees=degrees, first=first),
        grid=(count,),
        in_specs=in_specs,
        out_specs=pl.BlockSpec((1, band_rows, vectors), lambda a: (a + first, 0, 0)),
        out_shape=jax.ShapeDtypeStruct((axial_rows, band_rows, vectors), jnp.float32),
        scratch_shapes=[
            pltpu.VMEM((width, offsets * degrees * 128), jnp.bfloat16),
            pltpu.VMEM((offsets, band_rows, band_cols), jnp.bfloat16),
        ],
        input_output_aliases=aliases,
    )(*operands)


def body(
    displacement,
    stiffness,
    kernel,
    areas,
    near_cells,
    source_owner,
    source_node,
    target_owner,
    target_node,
):
    axial_rows = displacement.shape[0]
    circum_rows = displacement.shape[1]
    degrees = displacement.shape[2]
    vectors = displacement.shape[3]
    sectors = lax.axis_size("circ")
    axial_total = axial_rows * lax.axis_size("ax")
    node_count = axial_rows * circum_rows

    radial = displacement[:, :, 0, :].reshape(node_count, vectors)
    table = lax.all_gather(radial, "circ", axis=0, tiled=True)

    node_rows = displacement.reshape(axial_rows, circum_rows * degrees, vectors)
    count_ax = lax.axis_size("ax")
    top = lax.ppermute(node_rows[-1:], "ax", [(i, (i + 1) % count_ax) for i in range(count_ax)])
    bottom = lax.ppermute(node_rows[:1], "ax", [((i + 1) % count_ax, i) for i in range(count_ax)])
    first_nodes = jnp.concatenate(
        [top[:, :degrees], node_rows[:, :degrees], bottom[:, :degrees]], axis=0
    )
    last_nodes = jnp.concatenate(
        [top[:, -degrees:], node_rows[:, -degrees:], bottom[:, -degrees:]], axis=0
    )
    left = lax.ppermute(last_nodes, "circ", [(i, (i + 1) % sectors) for i in range(sectors)])
    right = lax.ppermute(first_nodes, "circ", [((i + 1) % sectors, i) for i in range(sectors)])
    gap = jnp.zeros((axial_rows + 2, 128 - 2 * degrees, vectors), displacement.dtype)
    halo = jnp.concatenate([right, gap, left], axis=1)
    global_row = lax.axis_index("ax") * axial_rows + jnp.arange(axial_rows, dtype=jnp.int32)
    lane_step = jnp.arange(stiffness.shape[2], dtype=jnp.int32) // (3 * degrees * degrees) - 1
    inside = (global_row[:, None] + lane_step[None, :] >= 0) & (
        global_row[:, None] + lane_step[None, :] < axial_total
    )
    blocks = jnp.where(inside[:, None, :], stiffness, jnp.zeros_like(stiffness))
    half = axial_rows // 2
    force = banded_force(blocks, node_rows, top, bottom, halo, degrees, 0, half)

    force, table = lax.optimization_barrier((force, table))
    slot_index = source_owner[:, 0] * node_count + source_node
    velocity = jnp.take(table, slot_index, axis=0, mode="clip")

    panel_size = kernel.shape[3]
    source_cells = velocity.reshape(-1, panel_size, vectors)
    pressure, load_value = near_field(kernel, source_cells, areas, near_cells)

    load_owner = target_owner[:, 0]
    target_count = load_owner.shape[0]
    load_capacity = 5 * target_count // (2 * sectors)
    load_slot = slot_positions(load_owner, sectors, load_capacity)
    gather_slot = (
        load_slot[None, :] == jnp.arange(sectors * load_capacity, dtype=jnp.int32)[:, None]
    ).astype(jnp.bfloat16)
    outgoing = jnp.dot(gather_slot, load_value, preferred_element_type=jnp.float32).astype(
        jnp.bfloat16
    )
    outgoing = outgoing.reshape(sectors, load_capacity, vectors)
    node_slot = (
        jnp.full((sectors * load_capacity,), -1, jnp.int32)
        .at[load_slot]
        .set(target_node)
        .reshape(sectors, load_capacity)
    )
    outgoing, force = lax.optimization_barrier((outgoing, force))
    arrived = lax.all_to_all(outgoing, "circ", split_axis=0, concat_axis=0, tiled=True)
    force = banded_force(
        blocks, node_rows, top, bottom, halo, degrees, half, axial_rows - half, force
    )
    arrived_node = lax.all_to_all(node_slot, "circ", split_axis=0, concat_axis=0, tiled=True)
    selector = (
        arrived_node.reshape(-1)[None, :] == jnp.arange(node_count, dtype=jnp.int32)[:, None]
    ).astype(jnp.bfloat16)
    fluid = jnp.dot(selector, arrived.reshape(-1, vectors), preferred_element_type=jnp.float32)
    fluid = fluid.reshape(axial_rows, circum_rows, vectors)
    force = force.at[:, :circum_rows, :].add(-fluid)
    shell_force = jnp.transpose(
        force.reshape(axial_rows, degrees, circum_rows, vectors), (0, 2, 1, 3)
    )
    return (shell_force, pressure)


def solution(mesh):
    return jax.shard_map(
        body,
        mesh=mesh,
        in_specs=(
            P("ax", "circ", None, None),
            P("ax", "circ", None),
            P(("ax", "circ"), None, None, None, None),
            P(("ax", "circ")),
            P(("ax", "circ"), None),
            P(("ax", "circ"), None),
            P(("ax", "circ")),
            P(("ax", "circ"), None),
            P(("ax", "circ")),
        ),
        out_specs=(P("ax", "circ", None, None), P(None, ("ax", "circ"), None)),
        check_vma=False,
    )
```

```python
import functools

import jax
import jax.numpy as jnp
from jax import lax
from jax.experimental import pallas as pl
from jax.experimental.pallas import tpu as pltpu
from jax.sharding import PartitionSpec as P


def extended(cells, sides, width):
    for axis, dim in sides:
        count = lax.axis_size(axis)
        head = lax.slice_in_dim(cells, 0, width, axis=dim)
        tail = lax.slice_in_dim(cells, cells.shape[dim] - width, cells.shape[dim], axis=dim)
        cells = jnp.concatenate(
            [
                lax.ppermute(tail, axis, [(i, (i + 1) % count) for i in range(count)]),
                cells,
                lax.ppermute(head, axis, [((i + 1) % count, i) for i in range(count)]),
            ],
            axis=dim,
        )
    return cells


def slot_positions(owners, sectors, capacity):
    onehot = owners[:, None] == jnp.arange(sectors, dtype=jnp.int32)[None, :]
    count = owners.shape[0]
    order = jnp.arange(count, dtype=jnp.int32)
    earlier = (order[None, :] < order[:, None]).astype(jnp.bfloat16)
    before = jnp.dot(earlier, onehot.astype(jnp.bfloat16), preferred_element_type=jnp.float32)
    ranking = jnp.sum(jnp.where(onehot, before, 0.0), axis=1).astype(jnp.int32)
    return owners * capacity + ranking


def pressure_kernel(near_ref, kern_ref, vel_ref, area_ref, p_ref, load_ref):
    g = pl.program_id(0)
    near_count = kern_ref.shape[1]
    panel = kern_ref.shape[3]
    for n in range(near_count):
        m = near_ref[g, n]
        w = kern_ref[0, n].reshape(2 * panel, panel)
        prod = jnp.dot(w, vel_ref[m], preferred_element_type=jnp.float32)
        if n == 0:
            p_ref[...] = prod.reshape(p_ref.shape)
        else:
            p_ref[...] += prod.reshape(p_ref.shape)
    load_ref[...] = (area_ref[...] * p_ref[0]).astype(load_ref.dtype)


def near_field(kernel, source_cells, areas, near_cells):
    cells_dev, near_count, _, panel, _ = kernel.shape
    src_cells, _, vectors = source_cells.shape
    targets = cells_dev * panel
    grid_spec = pltpu.PrefetchScalarGridSpec(
        num_scalar_prefetch=1,
        grid=(cells_dev,),
        in_specs=[
            pl.BlockSpec((1, near_count, 2, panel, panel), lambda g, near: (g, 0, 0, 0, 0)),
            pl.BlockSpec((src_cells, panel, vectors), lambda g, near: (0, 0, 0)),
            pl.BlockSpec((panel, 1), lambda g, near: (g, 0)),
        ],
        out_specs=[
            pl.BlockSpec((2, panel, vectors), lambda g, near: (0, g, 0)),
            pl.BlockSpec((panel, vectors), lambda g, near: (g, 0)),
        ],
    )
    return pl.pallas_call(
        pressure_kernel,
        grid_spec=grid_spec,
        out_shape=[
            jax.ShapeDtypeStruct((2, targets, vectors), jnp.float32),
            jax.ShapeDtypeStruct((targets, vectors), jnp.bfloat16),
        ],
    )(near_cells, kernel, source_cells, areas.reshape(targets, 1))


def stiff_kernel(s_ref, rows_ref, top_ref, bottom_ref, halo_ref, *rest, degrees, first):
    out_ref, sel_ref, band_ref = rest[-3:]
    step = pl.program_id(0)
    a = step + first
    last = rows_ref.shape[0] - 1
    nodes = s_ref.shape[1]
    offsets = band_ref.shape[0]
    group = 128
    span = offsets * degrees
    wide = band_ref.shape[2]

    @pl.when(step == 0)
    def _():
        k = lax.broadcasted_iota(jnp.int32, sel_ref.shape, 0)
        y = lax.broadcasted_iota(jnp.int32, sel_ref.shape, 1)
        blk = y // group
        lane = y % group
        target = (
            (blk // degrees) * (offsets * degrees * degrees)
            + (lane // degrees) * (degrees * degrees)
            + (blk % degrees) * degrees
            + lane % degrees
        )
        sel_ref[...] = jnp.where((lane < span) & (k == target), 1.0, 0.0).astype(sel_ref.dtype)

    spread = jnp.dot(s_ref[0], sel_ref[...], preferred_element_type=jnp.float32)
    pad = jnp.zeros((nodes, wide - group), jnp.float32)
    for d in range(offsets):
        for i in range(degrees):
            blk = d * degrees + i
            piece = jnp.concatenate([spread[:, blk * group : (blk + 1) * group], pad], axis=1)
            parts = []
            for g in range(nodes // 8):
                rows = pltpu.roll(piece[g * 8 : (g + 1) * 8], (g * 8 * degrees - degrees) % wide, 1)
                parts.append(pltpu.roll(rows, 0, 1, stride=degrees, stride_axis=0))
            skewed = jnp.concatenate(parts, axis=0)
            band_ref[d, i * nodes : (i + 1) * nodes, :] = skewed.astype(band_ref.dtype)
    above = jnp.where(a == 0, top_ref[0], rows_ref[jnp.maximum(a - 1, 0)])
    below = jnp.where(a == last, bottom_ref[0], rows_ref[jnp.minimum(a + 1, last)])
    acc = None
    for d, rows in enumerate((above, rows_ref[a], below)):
        both = jnp.concatenate([rows, halo_ref[a + d]], axis=0)
        part = jnp.dot(band_ref[d], both, preferred_element_type=jnp.float32)
        acc = part if acc is None else acc + part
    out_ref[0] = acc


def banded_force(blocks, rows, top, bottom, halo, degrees, first, count, previous=None):
    axial_rows, nodes, width = blocks.shape
    offsets = 3
    vectors = rows.shape[-1]
    band_rows = degrees * nodes
    band_cols = band_rows + halo.shape[1]
    in_specs = [
        pl.BlockSpec((1, nodes, width), lambda a: (a + first, 0, 0)),
        pl.BlockSpec(rows.shape, lambda a: (0, 0, 0)),
        pl.BlockSpec(top.shape, lambda a: (0, 0, 0)),
        pl.BlockSpec(bottom.shape, lambda a: (0, 0, 0)),
        pl.BlockSpec(halo.shape, lambda a: (0, 0, 0)),
    ]
    operands = [blocks, rows, top, bottom, halo]
    aliases = {}
    if previous is not None:
        in_specs.append(pl.BlockSpec(memory_space=pl.ANY))
        operands.append(previous)
        aliases = {len(operands) - 1: 0}
    return pl.pallas_call(
        functools.partial(stiff_kernel, degrees=degrees, first=first),
        grid=(count,),
        in_specs=in_specs,
        out_specs=pl.BlockSpec((1, band_rows, vectors), lambda a: (a + first, 0, 0)),
        out_shape=jax.ShapeDtypeStruct((axial_rows, band_rows, vectors), jnp.float32),
        scratch_shapes=[
            pltpu.VMEM((width, offsets * degrees * 128), jnp.bfloat16),
            pltpu.VMEM((offsets, band_rows, band_cols), jnp.bfloat16),
        ],
        input_output_aliases=aliases,
    )(*operands)


def body(
    displacement,
    stiffness,
    kernel,
    areas,
    near_cells,
    source_owner,
    source_node,
    target_owner,
    target_node,
):
    axial_rows = displacement.shape[0]
    circum_rows = displacement.shape[1]
    degrees = displacement.shape[2]
    vectors = displacement.shape[3]
    sectors = lax.axis_size("circ")
    node_count = axial_rows * circum_rows

    radial = displacement[:, :, 0, :].reshape(node_count, vectors)
    table = lax.all_gather(radial, "circ", axis=0, tiled=True)

    node_rows = displacement.reshape(axial_rows, circum_rows * degrees, vectors)
    count_ax = lax.axis_size("ax")
    top = lax.ppermute(node_rows[-1:], "ax", [(i, (i + 1) % count_ax) for i in range(count_ax)])
    bottom = lax.ppermute(node_rows[:1], "ax", [((i + 1) % count_ax, i) for i in range(count_ax)])
    ax_index = lax.axis_index("ax")
    top = jnp.where(ax_index == 0, jnp.zeros_like(top), top)
    bottom = jnp.where(ax_index == count_ax - 1, jnp.zeros_like(bottom), bottom)
    first_nodes = jnp.concatenate(
        [top[:, :degrees], node_rows[:, :degrees], bottom[:, :degrees]], axis=0
    )
    last_nodes = jnp.concatenate(
        [top[:, -degrees:], node_rows[:, -degrees:], bottom[:, -degrees:]], axis=0
    )
    left = lax.ppermute(last_nodes, "circ", [(i, (i + 1) % sectors) for i in range(sectors)])
    right = lax.ppermute(first_nodes, "circ", [((i + 1) % sectors, i) for i in range(sectors)])
    gap = jnp.zeros((axial_rows + 2, 128 - 2 * degrees, vectors), displacement.dtype)
    halo = jnp.concatenate([right, gap, left], axis=1)
    blocks = stiffness
    half = axial_rows // 2
    force = banded_force(blocks, node_rows, top, bottom, halo, degrees, 0, half)

    force, table = lax.optimization_barrier((force, table))
    slot_index = source_owner[:, 0] * node_count + source_node
    velocity = jnp.take(table, slot_index, axis=0, mode="clip")

    panel_size = kernel.shape[3]
    source_cells = velocity.reshape(-1, panel_size, vectors)
    pressure, load_value = near_field(kernel, source_cells, areas, near_cells)

    load_owner = target_owner[:, 0]
    target_count = load_owner.shape[0]
    load_capacity = 5 * target_count // (2 * sectors)
    load_slot = slot_positions(load_owner, sectors, load_capacity)
    gather_slot = (
        load_slot[None, :] == jnp.arange(sectors * load_capacity, dtype=jnp.int32)[:, None]
    ).astype(jnp.bfloat16)
    outgoing = jnp.dot(gather_slot, load_value, preferred_element_type=jnp.float32).astype(
        jnp.bfloat16
    )
    outgoing = outgoing.reshape(sectors, load_capacity, vectors)
    node_slot = (
        jnp.full((sectors * load_capacity,), -1, jnp.int32)
        .at[load_slot]
        .set(target_node)
        .reshape(sectors, load_capacity)
    )
    outgoing, force = lax.optimization_barrier((outgoing, force))
    arrived = lax.all_to_all(outgoing, "circ", split_axis=0, concat_axis=0, tiled=True)
    force = banded_force(
        blocks, node_rows, top, bottom, halo, degrees, half, axial_rows - half, force
    )
    arrived_node = lax.all_to_all(node_slot, "circ", split_axis=0, concat_axis=0, tiled=True)
    selector = (
        arrived_node.reshape(-1)[None, :] == jnp.arange(node_count, dtype=jnp.int32)[:, None]
    ).astype(jnp.bfloat16)
    fluid = jnp.dot(selector, arrived.reshape(-1, vectors), preferred_element_type=jnp.float32)
    fluid = fluid.reshape(axial_rows, circum_rows, vectors)
    force = force.at[:, :circum_rows, :].add(-fluid)
    shell_force = jnp.transpose(
        force.reshape(axial_rows, degrees, circum_rows, vectors), (0, 2, 1, 3)
    )
    return (shell_force, pressure)


def solution(mesh):
    return jax.shard_map(
        body,
        mesh=mesh,
        in_specs=(
            P("ax", "circ", None, None),
            P("ax", "circ", None),
            P(("ax", "circ"), None, None, None, None),
            P(("ax", "circ")),
            P(("ax", "circ"), None),
            P(("ax", "circ"), None),
            P(("ax", "circ")),
            P(("ax", "circ"), None),
            P(("ax", "circ")),
        ),
        out_specs=(P("ax", "circ", None, None), P(None, ("ax", "circ"), None)),
        check_vma=False,
    )
```

```python
import functools

import jax
import jax.numpy as jnp
from jax import lax
from jax.experimental import pallas as pl
from jax.experimental.pallas import tpu as pltpu
from jax.sharding import PartitionSpec as P


def extended(cells, sides, width):
    for axis, dim in sides:
        count = lax.axis_size(axis)
        head = lax.slice_in_dim(cells, 0, width, axis=dim)
        tail = lax.slice_in_dim(cells, cells.shape[dim] - width, cells.shape[dim], axis=dim)
        cells = jnp.concatenate(
            [
                lax.ppermute(tail, axis, [(i, (i + 1) % count) for i in range(count)]),
                cells,
                lax.ppermute(head, axis, [((i + 1) % count, i) for i in range(count)]),
            ],
            axis=dim,
        )
    return cells


def slot_positions(owners, sectors, capacity):
    onehot = (owners[:, None] == jnp.arange(sectors, dtype=jnp.int32)[None, :]).astype(jnp.int32)
    before = jnp.cumsum(onehot, axis=0) - onehot
    ranking = jnp.sum(before * onehot, axis=1)
    return owners * capacity + ranking


def pressure_kernel(near_ref, kern_ref, vel_ref, area_ref, p_ref, load_ref):
    g = pl.program_id(0)
    near_count = kern_ref.shape[1]
    panel = kern_ref.shape[3]
    for n in range(near_count):
        m = near_ref[g, n]
        w = kern_ref[0, n].reshape(2 * panel, panel)
        prod = jnp.dot(w, vel_ref[m], preferred_element_type=jnp.float32)
        if n == 0:
            p_ref[...] = prod.reshape(p_ref.shape)
        else:
            p_ref[...] += prod.reshape(p_ref.shape)
    load_ref[...] = (area_ref[...] * p_ref[0]).astype(load_ref.dtype)


def near_field(kernel, source_cells, areas, near_cells):
    cells_dev, near_count, _, panel, _ = kernel.shape
    src_cells, _, vectors = source_cells.shape
    targets = cells_dev * panel
    grid_spec = pltpu.PrefetchScalarGridSpec(
        num_scalar_prefetch=1,
        grid=(cells_dev,),
        in_specs=[
            pl.BlockSpec((1, near_count, 2, panel, panel), lambda g, near: (g, 0, 0, 0, 0)),
            pl.BlockSpec((src_cells, panel, vectors), lambda g, near: (0, 0, 0)),
            pl.BlockSpec((panel, 1), lambda g, near: (g, 0)),
        ],
        out_specs=[
            pl.BlockSpec((2, panel, vectors), lambda g, near: (0, g, 0)),
            pl.BlockSpec((panel, vectors), lambda g, near: (g, 0)),
        ],
    )
    return pl.pallas_call(
        pressure_kernel,
        grid_spec=grid_spec,
        out_shape=[
            jax.ShapeDtypeStruct((2, targets, vectors), jnp.float32),
            jax.ShapeDtypeStruct((targets, vectors), jnp.bfloat16),
        ],
    )(near_cells, kernel, source_cells, areas.reshape(targets, 1))


def stiff_kernel(s_ref, rows_ref, top_ref, bottom_ref, halo_ref, *rest, degrees, first):
    out_ref, sel_ref, band_ref = rest[-3:]
    step = pl.program_id(0)
    a = step + first
    last = rows_ref.shape[0] - 1
    nodes = s_ref.shape[1]
    offsets = band_ref.shape[0]
    group = 128
    span = offsets * degrees
    wide = band_ref.shape[2]

    @pl.when(step == 0)
    def _():
        k = lax.broadcasted_iota(jnp.int32, sel_ref.shape, 0)
        y = lax.broadcasted_iota(jnp.int32, sel_ref.shape, 1)
        blk = y // group
        lane = y % group
        target = (
            (blk // degrees) * (offsets * degrees * degrees)
            + (lane // degrees) * (degrees * degrees)
            + (blk % degrees) * degrees
            + lane % degrees
        )
        sel_ref[...] = jnp.where((lane < span) & (k == target), 1.0, 0.0).astype(sel_ref.dtype)

    spread = jnp.dot(s_ref[0], sel_ref[...], preferred_element_type=jnp.float32)
    pad = jnp.zeros((nodes, wide - group), jnp.float32)
    for d in range(offsets):
        for i in range(degrees):
            blk = d * degrees + i
            piece = jnp.concatenate([spread[:, blk * group : (blk + 1) * group], pad], axis=1)
            parts = []
            for g in range(nodes // 8):
                rows = pltpu.roll(piece[g * 8 : (g + 1) * 8], (g * 8 * degrees - degrees) % wide, 1)
                parts.append(pltpu.roll(rows, 0, 1, stride=degrees, stride_axis=0))
            skewed = jnp.concatenate(parts, axis=0)
            band_ref[d, i * nodes : (i + 1) * nodes, :] = skewed.astype(band_ref.dtype)
    above = jnp.where(a == 0, top_ref[0], rows_ref[jnp.maximum(a - 1, 0)])
    below = jnp.where(a == last, bottom_ref[0], rows_ref[jnp.minimum(a + 1, last)])
    acc = None
    for d, rows in enumerate((above, rows_ref[a], below)):
        both = jnp.concatenate([rows, halo_ref[a + d]], axis=0)
        part = jnp.dot(band_ref[d], both, preferred_element_type=jnp.float32)
        acc = part if acc is None else acc + part
    out_ref[0] = acc


def banded_force(blocks, rows, top, bottom, halo, degrees, first, count, previous=None):
    axial_rows, nodes, width = blocks.shape
    offsets = 3
    vectors = rows.shape[-1]
    band_rows = degrees * nodes
    band_cols = band_rows + halo.shape[1]
    in_specs = [
        pl.BlockSpec((1, nodes, width), lambda a: (a + first, 0, 0)),
        pl.BlockSpec(rows.shape, lambda a: (0, 0, 0)),
        pl.BlockSpec(top.shape, lambda a: (0, 0, 0)),
        pl.BlockSpec(bottom.shape, lambda a: (0, 0, 0)),
        pl.BlockSpec(halo.shape, lambda a: (0, 0, 0)),
    ]
    operands = [blocks, rows, top, bottom, halo]
    aliases = {}
    if previous is not None:
        in_specs.append(pl.BlockSpec(memory_space=pl.ANY))
        operands.append(previous)
        aliases = {len(operands) - 1: 0}
    return pl.pallas_call(
        functools.partial(stiff_kernel, degrees=degrees, first=first),
        grid=(count,),
        in_specs=in_specs,
        out_specs=pl.BlockSpec((1, band_rows, vectors), lambda a: (a + first, 0, 0)),
        out_shape=jax.ShapeDtypeStruct((axial_rows, band_rows, vectors), jnp.float32),
        scratch_shapes=[
            pltpu.VMEM((width, offsets * degrees * 128), jnp.bfloat16),
            pltpu.VMEM((offsets, band_rows, band_cols), jnp.bfloat16),
        ],
        input_output_aliases=aliases,
    )(*operands)


def body(
    displacement,
    stiffness,
    kernel,
    areas,
    near_cells,
    source_owner,
    source_node,
    target_owner,
    target_node,
):
    axial_rows = displacement.shape[0]
    circum_rows = displacement.shape[1]
    degrees = displacement.shape[2]
    vectors = displacement.shape[3]
    sectors = lax.axis_size("circ")
    axial_total = axial_rows * lax.axis_size("ax")
    node_count = axial_rows * circum_rows

    radial = displacement[:, :, 0, :].reshape(node_count, vectors)
    table = lax.all_gather(radial, "circ", axis=0, tiled=True)

    node_rows = displacement.reshape(axial_rows, circum_rows * degrees, vectors)
    count_ax = lax.axis_size("ax")
    top = lax.ppermute(node_rows[-1:], "ax", [(i, (i + 1) % count_ax) for i in range(count_ax)])
    bottom = lax.ppermute(node_rows[:1], "ax", [((i + 1) % count_ax, i) for i in range(count_ax)])
    first_nodes = jnp.concatenate(
        [top[:, :degrees], node_rows[:, :degrees], bottom[:, :degrees]], axis=0
    )
    last_nodes = jnp.concatenate(
        [top[:, -degrees:], node_rows[:, -degrees:], bottom[:, -degrees:]], axis=0
    )
    left = lax.ppermute(last_nodes, "circ", [(i, (i + 1) % sectors) for i in range(sectors)])
    right = lax.ppermute(first_nodes, "circ", [((i + 1) % sectors, i) for i in range(sectors)])
    gap = jnp.zeros((axial_rows + 2, 128 - 2 * degrees, vectors), displacement.dtype)
    halo = jnp.concatenate([right, gap, left], axis=1)
    global_row = lax.axis_index("ax") * axial_rows + jnp.arange(axial_rows, dtype=jnp.int32)
    lane_step = jnp.arange(stiffness.shape[2], dtype=jnp.int32) // (3 * degrees * degrees) - 1
    inside = (global_row[:, None] + lane_step[None, :] >= 0) & (
        global_row[:, None] + lane_step[None, :] < axial_total
    )
    blocks = jnp.where(inside[:, None, :], stiffness, jnp.zeros_like(stiffness))
    half = axial_rows // 2
    force = banded_force(blocks, node_rows, top, bottom, halo, degrees, 0, half)

    force, table = lax.optimization_barrier((force, table))
    slot_index = source_owner[:, 0] * node_count + source_node
    velocity = jnp.take(table, slot_index, axis=0, mode="clip")

    panel_size = kernel.shape[3]
    source_cells = velocity.reshape(-1, panel_size, vectors)
    pressure, load_value = near_field(kernel, source_cells, areas, near_cells)

    load_owner = target_owner[:, 0]
    target_count = load_owner.shape[0]
    load_capacity = 5 * target_count // (2 * sectors)
    load_slot = slot_positions(load_owner, sectors, load_capacity)
    gather_slot = (
        load_slot[None, :] == jnp.arange(sectors * load_capacity, dtype=jnp.int32)[:, None]
    ).astype(jnp.bfloat16)
    outgoing = jnp.dot(gather_slot, load_value, preferred_element_type=jnp.float32).astype(
        jnp.bfloat16
    )
    outgoing = outgoing.reshape(sectors, load_capacity, vectors)
    radix = 32
    digits = jnp.stack([target_node // radix, target_node % radix], axis=0).astype(jnp.bfloat16)
    slot_digits = lax.dot_general(
        digits, gather_slot, (((1,), (1,)), ((), ())), preferred_element_type=jnp.float32
    ).astype(jnp.bfloat16)
    slot_digits = jnp.transpose(slot_digits.reshape(2, sectors, load_capacity), (1, 0, 2))
    digit_rows = -(-2 * load_capacity // vectors)
    slot_digits = jnp.pad(
        slot_digits.reshape(sectors, 2 * load_capacity),
        ((0, 0), (0, digit_rows * vectors - 2 * load_capacity)),
    ).reshape(sectors, digit_rows, vectors)
    packet = jnp.concatenate([outgoing, slot_digits], axis=1)
    packet, force = lax.optimization_barrier((packet, force))
    arrived = lax.all_to_all(packet, "circ", split_axis=0, concat_axis=0, tiled=True)
    force = banded_force(
        blocks, node_rows, top, bottom, halo, degrees, half, axial_rows - half, force
    )
    arrived_load = arrived[:, :load_capacity].reshape(-1, vectors)
    arrived_digits = (
        arrived[:, load_capacity:]
        .reshape(sectors, digit_rows * vectors)[:, : 2 * load_capacity]
        .reshape(sectors, 2, load_capacity)
        .astype(jnp.float32)
    )
    arrived_node = (arrived_digits[:, 0] * radix + arrived_digits[:, 1]).astype(jnp.int32)
    selector = (
        arrived_node.reshape(-1)[None, :] == jnp.arange(node_count, dtype=jnp.int32)[:, None]
    ).astype(jnp.bfloat16)
    fluid = jnp.dot(selector, arrived_load, preferred_element_type=jnp.float32)
    fluid = fluid.reshape(axial_rows, circum_rows, vectors)
    force = force.at[:, :circum_rows, :].add(-fluid)
    shell_force = jnp.transpose(
        force.reshape(axial_rows, degrees, circum_rows, vectors), (0, 2, 1, 3)
    )
    return (shell_force, pressure)


def solution(mesh):
    return jax.shard_map(
        body,
        mesh=mesh,
        in_specs=(
            P("ax", "circ", None, None),
            P("ax", "circ", None),
            P(("ax", "circ"), None, None, None, None),
            P(("ax", "circ")),
            P(("ax", "circ"), None),
            P(("ax", "circ"), None),
            P(("ax", "circ")),
            P(("ax", "circ"), None),
            P(("ax", "circ")),
        ),
        out_specs=(P("ax", "circ", None, None), P(None, ("ax", "circ"), None)),
        check_vma=False,
    )
```

```python
import functools

import jax
import jax.numpy as jnp
from jax import lax
from jax.experimental import pallas as pl
from jax.experimental.pallas import tpu as pltpu
from jax.sharding import PartitionSpec as P


def extended(cells, sides, width):
    for axis, dim in sides:
        count = lax.axis_size(axis)
        head = lax.slice_in_dim(cells, 0, width, axis=dim)
        tail = lax.slice_in_dim(cells, cells.shape[dim] - width, cells.shape[dim], axis=dim)
        cells = jnp.concatenate(
            [
                lax.ppermute(tail, axis, [(i, (i + 1) % count) for i in range(count)]),
                cells,
                lax.ppermute(head, axis, [((i + 1) % count, i) for i in range(count)]),
            ],
            axis=dim,
        )
    return cells


def slot_positions(owners, sectors, capacity):
    onehot = owners[:, None] == jnp.arange(sectors, dtype=jnp.int32)[None, :]
    count = owners.shape[0]
    order = jnp.arange(count, dtype=jnp.int32)
    earlier = (order[None, :] < order[:, None]).astype(jnp.bfloat16)
    before = jnp.dot(earlier, onehot.astype(jnp.bfloat16), preferred_element_type=jnp.float32)
    ranking = jnp.sum(jnp.where(onehot, before, 0.0), axis=1).astype(jnp.int32)
    return owners * capacity + ranking


def pressure_kernel(near_ref, kern_ref, vel_ref, area_ref, p_ref, load_ref):
    g = pl.program_id(0)
    near_count = kern_ref.shape[1]
    panel = kern_ref.shape[3]
    for n in range(near_count):
        m = near_ref[g, n]
        w = kern_ref[0, n].reshape(2 * panel, panel)
        prod = jnp.dot(w, vel_ref[m], preferred_element_type=jnp.float32)
        if n == 0:
            p_ref[...] = prod.reshape(p_ref.shape)
        else:
            p_ref[...] += prod.reshape(p_ref.shape)
    load_ref[...] = (area_ref[...] * p_ref[0]).astype(load_ref.dtype)


def near_field(kernel, source_cells, areas, near_cells):
    cells_dev, near_count, _, panel, _ = kernel.shape
    src_cells, _, vectors = source_cells.shape
    targets = cells_dev * panel
    grid_spec = pltpu.PrefetchScalarGridSpec(
        num_scalar_prefetch=1,
        grid=(cells_dev,),
        in_specs=[
            pl.BlockSpec((1, near_count, 2, panel, panel), lambda g, near: (g, 0, 0, 0, 0)),
            pl.BlockSpec((src_cells, panel, vectors), lambda g, near: (0, 0, 0)),
            pl.BlockSpec((panel, 1), lambda g, near: (g, 0)),
        ],
        out_specs=[
            pl.BlockSpec((2, panel, vectors), lambda g, near: (0, g, 0)),
            pl.BlockSpec((panel, vectors), lambda g, near: (g, 0)),
        ],
    )
    return pl.pallas_call(
        pressure_kernel,
        grid_spec=grid_spec,
        out_shape=[
            jax.ShapeDtypeStruct((2, targets, vectors), jnp.float32),
            jax.ShapeDtypeStruct((targets, vectors), jnp.bfloat16),
        ],
    )(near_cells, kernel, source_cells, areas.reshape(targets, 1))


def stiff_kernel(s_ref, rows_ref, top_ref, bottom_ref, halo_ref, *rest, degrees, first):
    out_ref, sel_ref, band_ref = rest[-3:]
    step = pl.program_id(0)
    a = step + first
    last = rows_ref.shape[0] - 1
    nodes = s_ref.shape[1]
    offsets = band_ref.shape[0]
    group = 128
    span = offsets * degrees
    wide = band_ref.shape[2]

    @pl.when(step == 0)
    def _():
        k = lax.broadcasted_iota(jnp.int32, sel_ref.shape, 0)
        y = lax.broadcasted_iota(jnp.int32, sel_ref.shape, 1)
        blk = y // group
        lane = y % group
        target = (
            (blk // degrees) * (offsets * degrees * degrees)
            + (lane // degrees) * (degrees * degrees)
            + (blk % degrees) * degrees
            + lane % degrees
        )
        sel_ref[...] = jnp.where((lane < span) & (k == target), 1.0, 0.0).astype(sel_ref.dtype)

    spread = jnp.dot(s_ref[0], sel_ref[...], preferred_element_type=jnp.float32)
    pad = jnp.zeros((nodes, wide - group), jnp.float32)
    for d in range(offsets):
        for i in range(degrees):
            blk = d * degrees + i
            piece = jnp.concatenate([spread[:, blk * group : (blk + 1) * group], pad], axis=1)
            parts = []
            for g in range(nodes // 8):
                rows = pltpu.roll(piece[g * 8 : (g + 1) * 8], (g * 8 * degrees - degrees) % wide, 1)
                parts.append(pltpu.roll(rows, 0, 1, stride=degrees, stride_axis=0))
            skewed = jnp.concatenate(parts, axis=0)
            band_ref[d, i * nodes : (i + 1) * nodes, :] = skewed.astype(band_ref.dtype)
    above = jnp.where(a == 0, top_ref[0], rows_ref[jnp.maximum(a - 1, 0)])
    below = jnp.where(a == last, bottom_ref[0], rows_ref[jnp.minimum(a + 1, last)])
    acc = None
    for d, rows in enumerate((above, rows_ref[a], below)):
        both = jnp.concatenate([rows, halo_ref[a + d]], axis=0)
        part = jnp.dot(band_ref[d], both, preferred_element_type=jnp.float32)
        acc = part if acc is None else acc + part
    out_ref[0] = acc


def banded_force(blocks, rows, top, bottom, halo, degrees, first, count, previous=None):
    axial_rows, nodes, width = blocks.shape
    offsets = 3
    vectors = rows.shape[-1]
    band_rows = degrees * nodes
    band_cols = band_rows + halo.shape[1]
    in_specs = [
        pl.BlockSpec((1, nodes, width), lambda a: (a + first, 0, 0)),
        pl.BlockSpec(rows.shape, lambda a: (0, 0, 0)),
        pl.BlockSpec(top.shape, lambda a: (0, 0, 0)),
        pl.BlockSpec(bottom.shape, lambda a: (0, 0, 0)),
        pl.BlockSpec(halo.shape, lambda a: (0, 0, 0)),
    ]
    operands = [blocks, rows, top, bottom, halo]
    aliases = {}
    if previous is not None:
        in_specs.append(pl.BlockSpec(memory_space=pl.ANY))
        operands.append(previous)
        aliases = {len(operands) - 1: 0}
    return pl.pallas_call(
        functools.partial(stiff_kernel, degrees=degrees, first=first),
        grid=(count,),
        in_specs=in_specs,
        out_specs=pl.BlockSpec((1, band_rows, vectors), lambda a: (a + first, 0, 0)),
        out_shape=jax.ShapeDtypeStruct((axial_rows, band_rows, vectors), jnp.float32),
        scratch_shapes=[
            pltpu.VMEM((width, offsets * degrees * 128), jnp.bfloat16),
            pltpu.VMEM((offsets, band_rows, band_cols), jnp.bfloat16),
        ],
        input_output_aliases=aliases,
    )(*operands)


def body(
    displacement,
    stiffness,
    kernel,
    areas,
    near_cells,
    source_owner,
    source_node,
    target_owner,
    target_node,
):
    axial_rows = displacement.shape[0]
    circum_rows = displacement.shape[1]
    degrees = displacement.shape[2]
    vectors = displacement.shape[3]
    sectors = lax.axis_size("circ")
    axial_total = axial_rows * lax.axis_size("ax")
    node_count = axial_rows * circum_rows

    radial = displacement[:, :, 0, :].reshape(node_count, vectors)
    table = lax.all_gather(radial, "circ", axis=0, tiled=True)

    node_rows = displacement.reshape(axial_rows, circum_rows * degrees, vectors)
    count_ax = lax.axis_size("ax")
    top = lax.ppermute(node_rows[-1:], "ax", [(i, (i + 1) % count_ax) for i in range(count_ax)])
    bottom = lax.ppermute(node_rows[:1], "ax", [((i + 1) % count_ax, i) for i in range(count_ax)])
    first_nodes = jnp.concatenate(
        [top[:, :degrees], node_rows[:, :degrees], bottom[:, :degrees]], axis=0
    )
    last_nodes = jnp.concatenate(
        [top[:, -degrees:], node_rows[:, -degrees:], bottom[:, -degrees:]], axis=0
    )
    left = lax.ppermute(last_nodes, "circ", [(i, (i + 1) % sectors) for i in range(sectors)])
    right = lax.ppermute(first_nodes, "circ", [((i + 1) % sectors, i) for i in range(sectors)])
    gap = jnp.zeros((axial_rows + 2, 128 - 2 * degrees, vectors), displacement.dtype)
    halo = jnp.concatenate([right, gap, left], axis=1)
    global_row = lax.axis_index("ax") * axial_rows + jnp.arange(axial_rows, dtype=jnp.int32)
    lane_step = jnp.arange(stiffness.shape[2], dtype=jnp.int32) // (3 * degrees * degrees) - 1
    inside = (global_row[:, None] + lane_step[None, :] >= 0) & (
        global_row[:, None] + lane_step[None, :] < axial_total
    )
    blocks = jnp.where(inside[:, None, :], stiffness, jnp.zeros_like(stiffness))
    half = (axial_rows * 7) // 16
    force = banded_force(blocks, node_rows, top, bottom, halo, degrees, 0, half)

    force, table = lax.optimization_barrier((force, table))
    slot_index = source_owner[:, 0] * node_count + source_node
    velocity = jnp.take(table, slot_index, axis=0, mode="clip")

    panel_size = kernel.shape[3]
    source_cells = velocity.reshape(-1, panel_size, vectors)
    pressure, load_value = near_field(kernel, source_cells, areas, near_cells)

    load_owner = target_owner[:, 0]
    target_count = load_owner.shape[0]
    load_capacity = 5 * target_count // (2 * sectors)
    load_slot = slot_positions(load_owner, sectors, load_capacity)
    gather_slot = (
        load_slot[None, :] == jnp.arange(sectors * load_capacity, dtype=jnp.int32)[:, None]
    ).astype(jnp.bfloat16)
    outgoing = jnp.dot(gather_slot, load_value, preferred_element_type=jnp.float32).astype(
        jnp.bfloat16
    )
    outgoing = outgoing.reshape(sectors, load_capacity, vectors)
    radix = 32
    digits = jnp.stack([target_node // radix, target_node % radix], axis=0).astype(jnp.bfloat16)
    slot_digits = lax.dot_general(
        digits, gather_slot, (((1,), (1,)), ((), ())), preferred_element_type=jnp.float32
    ).astype(jnp.bfloat16)
    slot_digits = jnp.transpose(slot_digits.reshape(2, sectors, load_capacity), (1, 0, 2))
    digit_rows = -(-2 * load_capacity // vectors)
    slot_digits = jnp.pad(
        slot_digits.reshape(sectors, 2 * load_capacity),
        ((0, 0), (0, digit_rows * vectors - 2 * load_capacity)),
    ).reshape(sectors, digit_rows, vectors)
    packet = jnp.concatenate([outgoing, slot_digits], axis=1)
    packet, force = lax.optimization_barrier((packet, force))
    arrived = lax.all_to_all(packet, "circ", split_axis=0, concat_axis=0, tiled=True)
    force = banded_force(
        blocks, node_rows, top, bottom, halo, degrees, half, axial_rows - half, force
    )
    arrived_load = arrived[:, :load_capacity].reshape(-1, vectors)
    arrived_digits = (
        arrived[:, load_capacity:]
        .reshape(sectors, digit_rows * vectors)[:, : 2 * load_capacity]
        .reshape(sectors, 2, load_capacity)
        .astype(jnp.float32)
    )
    arrived_node = (arrived_digits[:, 0] * radix + arrived_digits[:, 1]).astype(jnp.int32)
    selector = (
        arrived_node.reshape(-1)[None, :] == jnp.arange(node_count, dtype=jnp.int32)[:, None]
    ).astype(jnp.bfloat16)
    fluid = jnp.dot(selector, arrived_load, preferred_element_type=jnp.float32)
    fluid = fluid.reshape(axial_rows, circum_rows, vectors)
    force = force.at[:, :circum_rows, :].add(-fluid)
    shell_force = jnp.transpose(
        force.reshape(axial_rows, degrees, circum_rows, vectors), (0, 2, 1, 3)
    )
    return (shell_force, pressure)


def solution(mesh):
    return jax.shard_map(
        body,
        mesh=mesh,
        in_specs=(
            P("ax", "circ", None, None),
            P("ax", "circ", None),
            P(("ax", "circ"), None, None, None, None),
            P(("ax", "circ")),
            P(("ax", "circ"), None),
            P(("ax", "circ"), None),
            P(("ax", "circ")),
            P(("ax", "circ"), None),
            P(("ax", "circ")),
        ),
        out_specs=(P("ax", "circ", None, None), P(None, ("ax", "circ"), None)),
        check_vma=False,
    )
```

```python
import functools

import jax
import jax.numpy as jnp
from jax import lax
from jax.experimental import pallas as pl
from jax.experimental.pallas import tpu as pltpu
from jax.sharding import PartitionSpec as P


def extended(cells, sides, width):
    for axis, dim in sides:
        count = lax.axis_size(axis)
        head = lax.slice_in_dim(cells, 0, width, axis=dim)
        tail = lax.slice_in_dim(cells, cells.shape[dim] - width, cells.shape[dim], axis=dim)
        cells = jnp.concatenate(
            [
                lax.ppermute(tail, axis, [(i, (i + 1) % count) for i in range(count)]),
                cells,
                lax.ppermute(head, axis, [((i + 1) % count, i) for i in range(count)]),
            ],
            axis=dim,
        )
    return cells


def slot_positions(owners, sectors, capacity):
    onehot = owners[:, None] == jnp.arange(sectors, dtype=jnp.int32)[None, :]
    count = owners.shape[0]
    order = jnp.arange(count, dtype=jnp.int32)
    earlier = (order[None, :] < order[:, None]).astype(jnp.bfloat16)
    before = jnp.dot(earlier, onehot.astype(jnp.bfloat16), preferred_element_type=jnp.float32)
    ranking = jnp.sum(jnp.where(onehot, before, 0.0), axis=1).astype(jnp.int32)
    return owners * capacity + ranking


def pressure_kernel(near_ref, kern_ref, vel_ref, area_ref, p_ref, load_ref):
    g = pl.program_id(0)
    near_count = kern_ref.shape[1]
    panel = kern_ref.shape[3]
    for n in range(near_count):
        m = near_ref[g, n]
        w = kern_ref[0, n].reshape(2 * panel, panel)
        prod = jnp.dot(w, vel_ref[m], preferred_element_type=jnp.float32)
        if n == 0:
            p_ref[...] = prod.reshape(p_ref.shape)
        else:
            p_ref[...] += prod.reshape(p_ref.shape)
    load_ref[...] = (area_ref[...] * p_ref[0]).astype(load_ref.dtype)


def near_field(kernel, source_cells, areas, near_cells):
    cells_dev, near_count, _, panel, _ = kernel.shape
    src_cells, _, vectors = source_cells.shape
    targets = cells_dev * panel
    grid_spec = pltpu.PrefetchScalarGridSpec(
        num_scalar_prefetch=1,
        grid=(cells_dev,),
        in_specs=[
            pl.BlockSpec((1, near_count, 2, panel, panel), lambda g, near: (g, 0, 0, 0, 0)),
            pl.BlockSpec((src_cells, panel, vectors), lambda g, near: (0, 0, 0)),
            pl.BlockSpec((panel, 1), lambda g, near: (g, 0)),
        ],
        out_specs=[
            pl.BlockSpec((2, panel, vectors), lambda g, near: (0, g, 0)),
            pl.BlockSpec((panel, vectors), lambda g, near: (g, 0)),
        ],
    )
    return pl.pallas_call(
        pressure_kernel,
        grid_spec=grid_spec,
        out_shape=[
            jax.ShapeDtypeStruct((2, targets, vectors), jnp.float32),
            jax.ShapeDtypeStruct((targets, vectors), jnp.bfloat16),
        ],
    )(near_cells, kernel, source_cells, areas.reshape(targets, 1))


def stiff_kernel(s_ref, rows_ref, top_ref, bottom_ref, halo_ref, *rest, degrees, first):
    out_ref, sel_ref, band_ref = rest[-3:]
    step = pl.program_id(0)
    a = step + first
    last = rows_ref.shape[0] - 1
    nodes = s_ref.shape[1]
    offsets = band_ref.shape[0]
    group = 128
    span = offsets * degrees
    wide = band_ref.shape[2]

    @pl.when(step == 0)
    def _():
        k = lax.broadcasted_iota(jnp.int32, sel_ref.shape, 0)
        y = lax.broadcasted_iota(jnp.int32, sel_ref.shape, 1)
        blk = y // group
        lane = y % group
        target = (
            (blk // degrees) * (offsets * degrees * degrees)
            + (lane // degrees) * (degrees * degrees)
            + (blk % degrees) * degrees
            + lane % degrees
        )
        sel_ref[...] = jnp.where((lane < span) & (k == target), 1.0, 0.0).astype(sel_ref.dtype)

        band_ref[...] = jnp.zeros(band_ref.shape, band_ref.dtype)

    spread = jnp.dot(s_ref[0], sel_ref[...], preferred_element_type=jnp.float32)
    pad = jnp.zeros((8, group), jnp.float32)
    tiles = wide // group
    for d in range(offsets):
        for i in range(degrees):
            blk = d * degrees + i
            piece = spread[:, blk * group : (blk + 1) * group]
            for h in range(nodes // 16):
                base = 16 * h * degrees - degrees
                tile = base // group
                parts = []
                for g in (2 * h, 2 * h + 1):
                    rows = jnp.concatenate([piece[g * 8 : (g + 1) * 8], pad], axis=1)
                    shift = 8 * g * degrees - degrees - tile * group
                    rows = pltpu.roll(rows, shift, 1)
                    parts.append(pltpu.roll(rows, 0, 1, stride=degrees, stride_axis=0))
                window = jnp.concatenate(parts, axis=0).astype(band_ref.dtype)
                top_row = i * nodes + 16 * h
                for t in range(2):
                    lane = ((tile + t) % tiles) * group
                    band_ref[d, top_row : top_row + 16, lane : lane + group] = window[
                        :, t * group : (t + 1) * group
                    ]
    above = jnp.where(a == 0, top_ref[0], rows_ref[jnp.maximum(a - 1, 0)])
    below = jnp.where(a == last, bottom_ref[0], rows_ref[jnp.minimum(a + 1, last)])
    acc = None
    for d, rows in enumerate((above, rows_ref[a], below)):
        both = jnp.concatenate([rows, halo_ref[a + d]], axis=0)
        part = jnp.dot(band_ref[d], both, preferred_element_type=jnp.float32)
        acc = part if acc is None else acc + part
    out_ref[0] = acc


def banded_force(blocks, rows, top, bottom, halo, degrees, first, count, previous=None):
    axial_rows, nodes, width = blocks.shape
    offsets = 3
    vectors = rows.shape[-1]
    band_rows = degrees * nodes
    band_cols = band_rows + halo.shape[1]
    in_specs = [
        pl.BlockSpec((1, nodes, width), lambda a: (a + first, 0, 0)),
        pl.BlockSpec(rows.shape, lambda a: (0, 0, 0)),
        pl.BlockSpec(top.shape, lambda a: (0, 0, 0)),
        pl.BlockSpec(bottom.shape, lambda a: (0, 0, 0)),
        pl.BlockSpec(halo.shape, lambda a: (0, 0, 0)),
    ]
    operands = [blocks, rows, top, bottom, halo]
    aliases = {}
    if previous is not None:
        in_specs.append(pl.BlockSpec(memory_space=pl.ANY))
        operands.append(previous)
        aliases = {len(operands) - 1: 0}
    return pl.pallas_call(
        functools.partial(stiff_kernel, degrees=degrees, first=first),
        grid=(count,),
        in_specs=in_specs,
        out_specs=pl.BlockSpec((1, band_rows, vectors), lambda a: (a + first, 0, 0)),
        out_shape=jax.ShapeDtypeStruct((axial_rows, band_rows, vectors), jnp.float32),
        scratch_shapes=[
            pltpu.VMEM((width, offsets * degrees * 128), jnp.bfloat16),
            pltpu.VMEM((offsets, band_rows, band_cols), jnp.bfloat16),
        ],
        input_output_aliases=aliases,
    )(*operands)


def body(
    displacement,
    stiffness,
    kernel,
    areas,
    near_cells,
    source_owner,
    source_node,
    target_owner,
    target_node,
):
    axial_rows = displacement.shape[0]
    circum_rows = displacement.shape[1]
    degrees = displacement.shape[2]
    vectors = displacement.shape[3]
    sectors = lax.axis_size("circ")
    axial_total = axial_rows * lax.axis_size("ax")
    node_count = axial_rows * circum_rows

    radial = displacement[:, :, 0, :].reshape(node_count, vectors)
    table = lax.all_gather(radial, "circ", axis=0, tiled=True)

    node_rows = displacement.reshape(axial_rows, circum_rows * degrees, vectors)
    count_ax = lax.axis_size("ax")
    top = lax.ppermute(node_rows[-1:], "ax", [(i, (i + 1) % count_ax) for i in range(count_ax)])
    bottom = lax.ppermute(node_rows[:1], "ax", [((i + 1) % count_ax, i) for i in range(count_ax)])
    first_nodes = jnp.concatenate(
        [top[:, :degrees], node_rows[:, :degrees], bottom[:, :degrees]], axis=0
    )
    last_nodes = jnp.concatenate(
        [top[:, -degrees:], node_rows[:, -degrees:], bottom[:, -degrees:]], axis=0
    )
    left = lax.ppermute(last_nodes, "circ", [(i, (i + 1) % sectors) for i in range(sectors)])
    right = lax.ppermute(first_nodes, "circ", [((i + 1) % sectors, i) for i in range(sectors)])
    gap = jnp.zeros((axial_rows + 2, 128 - 2 * degrees, vectors), displacement.dtype)
    halo = jnp.concatenate([right, gap, left], axis=1)
    global_row = lax.axis_index("ax") * axial_rows + jnp.arange(axial_rows, dtype=jnp.int32)
    lane_step = jnp.arange(stiffness.shape[2], dtype=jnp.int32) // (3 * degrees * degrees) - 1
    inside = (global_row[:, None] + lane_step[None, :] >= 0) & (
        global_row[:, None] + lane_step[None, :] < axial_total
    )
    blocks = jnp.where(inside[:, None, :], stiffness, jnp.zeros_like(stiffness))
    half = (axial_rows * 7) // 16
    force = banded_force(blocks, node_rows, top, bottom, halo, degrees, 0, half)

    force, table = lax.optimization_barrier((force, table))
    slot_index = source_owner[:, 0] * node_count + source_node
    velocity = jnp.take(table, slot_index, axis=0, mode="clip")

    panel_size = kernel.shape[3]
    source_cells = velocity.reshape(-1, panel_size, vectors)
    pressure, load_value = near_field(kernel, source_cells, areas, near_cells)

    load_owner = target_owner[:, 0]
    target_count = load_owner.shape[0]
    load_capacity = 5 * target_count // (2 * sectors)
    load_slot = slot_positions(load_owner, sectors, load_capacity)
    gather_slot = (
        load_slot[None, :] == jnp.arange(sectors * load_capacity, dtype=jnp.int32)[:, None]
    ).astype(jnp.bfloat16)
    outgoing = jnp.dot(gather_slot, load_value, preferred_element_type=jnp.float32).astype(
        jnp.bfloat16
    )
    outgoing = outgoing.reshape(sectors, load_capacity, vectors)
    radix = 32
    digits = jnp.stack([target_node // radix, target_node % radix], axis=0).astype(jnp.bfloat16)
    slot_digits = lax.dot_general(
        digits, gather_slot, (((1,), (1,)), ((), ())), preferred_element_type=jnp.float32
    ).astype(jnp.bfloat16)
    slot_digits = jnp.transpose(slot_digits.reshape(2, sectors, load_capacity), (1, 0, 2))
    digit_rows = -(-2 * load_capacity // vectors)
    slot_digits = jnp.pad(
        slot_digits.reshape(sectors, 2 * load_capacity),
        ((0, 0), (0, digit_rows * vectors - 2 * load_capacity)),
    ).reshape(sectors, digit_rows, vectors)
    packet = jnp.concatenate([outgoing, slot_digits], axis=1)
    packet, force = lax.optimization_barrier((packet, force))
    arrived = lax.all_to_all(packet, "circ", split_axis=0, concat_axis=0, tiled=True)
    force = banded_force(
        blocks, node_rows, top, bottom, halo, degrees, half, axial_rows - half, force
    )
    arrived_load = arrived[:, :load_capacity].reshape(-1, vectors)
    arrived_digits = (
        arrived[:, load_capacity:]
        .reshape(sectors, digit_rows * vectors)[:, : 2 * load_capacity]
        .reshape(sectors, 2, load_capacity)
        .astype(jnp.float32)
    )
    arrived_node = (arrived_digits[:, 0] * radix + arrived_digits[:, 1]).astype(jnp.int32)
    selector = (
        arrived_node.reshape(-1)[None, :] == jnp.arange(node_count, dtype=jnp.int32)[:, None]
    ).astype(jnp.bfloat16)
    fluid = jnp.dot(selector, arrived_load, preferred_element_type=jnp.float32)
    fluid = fluid.reshape(axial_rows, circum_rows, vectors)
    force = force.at[:, :circum_rows, :].add(-fluid)
    shell_force = jnp.transpose(
        force.reshape(axial_rows, degrees, circum_rows, vectors), (0, 2, 1, 3)
    )
    return (shell_force, pressure)


def solution(mesh):
    return jax.shard_map(
        body,
        mesh=mesh,
        in_specs=(
            P("ax", "circ", None, None),
            P("ax", "circ", None),
            P(("ax", "circ"), None, None, None, None),
            P(("ax", "circ")),
            P(("ax", "circ"), None),
            P(("ax", "circ"), None),
            P(("ax", "circ")),
            P(("ax", "circ"), None),
            P(("ax", "circ")),
        ),
        out_specs=(P("ax", "circ", None, None), P(None, ("ax", "circ"), None)),
        check_vma=False,
    )
```

```python
import functools

import jax
import jax.numpy as jnp
from jax import lax
from jax.experimental import pallas as pl
from jax.experimental.pallas import tpu as pltpu
from jax.sharding import PartitionSpec as P


def extended(cells, sides, width):
    for axis, dim in sides:
        count = lax.axis_size(axis)
        head = lax.slice_in_dim(cells, 0, width, axis=dim)
        tail = lax.slice_in_dim(cells, cells.shape[dim] - width, cells.shape[dim], axis=dim)
        cells = jnp.concatenate(
            [
                lax.ppermute(tail, axis, [(i, (i + 1) % count) for i in range(count)]),
                cells,
                lax.ppermute(head, axis, [((i + 1) % count, i) for i in range(count)]),
            ],
            axis=dim,
        )
    return cells


def slot_positions(owners, sectors, capacity):
    onehot = owners[:, None] == jnp.arange(sectors, dtype=jnp.int32)[None, :]
    count = owners.shape[0]
    order = jnp.arange(count, dtype=jnp.int32)
    earlier = (order[None, :] < order[:, None]).astype(jnp.bfloat16)
    before = jnp.dot(earlier, onehot.astype(jnp.bfloat16), preferred_element_type=jnp.float32)
    ranking = jnp.sum(jnp.where(onehot, before, 0.0), axis=1).astype(jnp.int32)
    return owners * capacity + ranking


def pressure_kernel(near_ref, kern_ref, vel_ref, area_ref, p_ref, load_ref):
    g = pl.program_id(0)
    near_count = kern_ref.shape[1]
    panel = kern_ref.shape[3]
    for n in range(near_count):
        m = near_ref[g, n]
        w = kern_ref[0, n].reshape(2 * panel, panel)
        prod = jnp.dot(w, vel_ref[m], preferred_element_type=jnp.float32)
        if n == 0:
            p_ref[...] = prod.reshape(p_ref.shape)
        else:
            p_ref[...] += prod.reshape(p_ref.shape)
    load_ref[...] = (area_ref[...] * p_ref[0]).astype(load_ref.dtype)


def near_field(kernel, source_cells, areas, near_cells):
    cells_dev, near_count, _, panel, _ = kernel.shape
    src_cells, _, vectors = source_cells.shape
    targets = cells_dev * panel
    grid_spec = pltpu.PrefetchScalarGridSpec(
        num_scalar_prefetch=1,
        grid=(cells_dev,),
        in_specs=[
            pl.BlockSpec((1, near_count, 2, panel, panel), lambda g, near: (g, 0, 0, 0, 0)),
            pl.BlockSpec((src_cells, panel, vectors), lambda g, near: (0, 0, 0)),
            pl.BlockSpec((panel, 1), lambda g, near: (g, 0)),
        ],
        out_specs=[
            pl.BlockSpec((2, panel, vectors), lambda g, near: (0, g, 0)),
            pl.BlockSpec((panel, vectors), lambda g, near: (g, 0)),
        ],
    )
    return pl.pallas_call(
        pressure_kernel,
        grid_spec=grid_spec,
        out_shape=[
            jax.ShapeDtypeStruct((2, targets, vectors), jnp.float32),
            jax.ShapeDtypeStruct((targets, vectors), jnp.bfloat16),
        ],
    )(near_cells, kernel, source_cells, areas.reshape(targets, 1))


def stiff_kernel(s_ref, rows_ref, top_ref, bottom_ref, halo_ref, *rest, degrees, first):
    out_ref, sel_ref, band_ref = rest[-3:]
    step = pl.program_id(0)
    a = step + first
    last = rows_ref.shape[0] - 1
    nodes = s_ref.shape[1]
    offsets = band_ref.shape[0]
    group = 128
    span = offsets * degrees
    wide = band_ref.shape[2]

    per_tile = group // span

    @pl.when(step == 0)
    def _():
        k = lax.broadcasted_iota(jnp.int32, sel_ref.shape, 0)
        y = lax.broadcasted_iota(jnp.int32, sel_ref.shape, 1)
        lane = y % group
        blk = (y // group) * per_tile + lane // span
        inner = lane % span
        target = (
            (blk // degrees) * (offsets * degrees * degrees)
            + (inner // degrees) * (degrees * degrees)
            + (blk % degrees) * degrees
            + inner % degrees
        )
        valid = (lane < per_tile * span) & (blk < offsets * degrees)
        sel_ref[...] = jnp.where(valid & (k == target), 1.0, 0.0).astype(sel_ref.dtype)
        band_ref[...] = jnp.zeros(band_ref.shape, band_ref.dtype)

    spread = jnp.dot(s_ref[0], sel_ref[...], preferred_element_type=jnp.float32)
    pad = jnp.zeros((8, group), jnp.float32)
    tiles = wide // group
    lane_id = lax.broadcasted_iota(jnp.int32, (nodes, group), 1)
    for d in range(offsets):
        for i in range(degrees):
            blk = d * degrees + i
            b, q = blk // per_tile, blk % per_tile
            piece = spread[:, b * group : (b + 1) * group]
            piece = jnp.where(
                (lane_id >= q * span) & (lane_id < (q + 1) * span), piece, jnp.zeros_like(piece)
            )
            for h in range(nodes // 16):
                base = 16 * h * degrees - degrees
                tile = base // group
                parts = []
                for g in (2 * h, 2 * h + 1):
                    rows = jnp.concatenate([piece[g * 8 : (g + 1) * 8], pad], axis=1)
                    shift = (8 * g * degrees - degrees - tile * group - q * span) % (2 * group)
                    rows = pltpu.roll(rows, shift, 1)
                    parts.append(pltpu.roll(rows, 0, 1, stride=degrees, stride_axis=0))
                window = jnp.concatenate(parts, axis=0).astype(band_ref.dtype)
                top_row = i * nodes + 16 * h
                for t in range(2):
                    lane = ((tile + t) % tiles) * group
                    band_ref[d, top_row : top_row + 16, lane : lane + group] = window[
                        :, t * group : (t + 1) * group
                    ]
    above = jnp.where(a == 0, top_ref[0], rows_ref[jnp.maximum(a - 1, 0)])
    below = jnp.where(a == last, bottom_ref[0], rows_ref[jnp.minimum(a + 1, last)])
    acc = None
    for d, rows in enumerate((above, rows_ref[a], below)):
        both = jnp.concatenate([rows, halo_ref[a + d]], axis=0)
        part = jnp.dot(band_ref[d], both, preferred_element_type=jnp.float32)
        acc = part if acc is None else acc + part
    out_ref[0] = acc


def banded_force(blocks, rows, top, bottom, halo, degrees, first, count, previous=None):
    axial_rows, nodes, width = blocks.shape
    offsets = 3
    vectors = rows.shape[-1]
    band_rows = degrees * nodes
    band_cols = band_rows + halo.shape[1]
    sel_cols = -(-offsets * degrees // (128 // (offsets * degrees))) * 128
    in_specs = [
        pl.BlockSpec((1, nodes, width), lambda a: (a + first, 0, 0)),
        pl.BlockSpec(rows.shape, lambda a: (0, 0, 0)),
        pl.BlockSpec(top.shape, lambda a: (0, 0, 0)),
        pl.BlockSpec(bottom.shape, lambda a: (0, 0, 0)),
        pl.BlockSpec(halo.shape, lambda a: (0, 0, 0)),
    ]
    operands = [blocks, rows, top, bottom, halo]
    aliases = {}
    if previous is not None:
        in_specs.append(pl.BlockSpec(memory_space=pl.ANY))
        operands.append(previous)
        aliases = {len(operands) - 1: 0}
    return pl.pallas_call(
        functools.partial(stiff_kernel, degrees=degrees, first=first),
        grid=(count,),
        in_specs=in_specs,
        out_specs=pl.BlockSpec((1, band_rows, vectors), lambda a: (a + first, 0, 0)),
        out_shape=jax.ShapeDtypeStruct((axial_rows, band_rows, vectors), jnp.float32),
        scratch_shapes=[
            pltpu.VMEM((width, sel_cols), jnp.bfloat16),
            pltpu.VMEM((offsets, band_rows, band_cols), jnp.bfloat16),
        ],
        input_output_aliases=aliases,
    )(*operands)


def body(
    displacement,
    stiffness,
    kernel,
    areas,
    near_cells,
    source_owner,
    source_node,
    target_owner,
    target_node,
):
    axial_rows = displacement.shape[0]
    circum_rows = displacement.shape[1]
    degrees = displacement.shape[2]
    vectors = displacement.shape[3]
    sectors = lax.axis_size("circ")
    axial_total = axial_rows * lax.axis_size("ax")
    node_count = axial_rows * circum_rows

    radial = displacement[:, :, 0, :].reshape(node_count, vectors)
    table = lax.all_gather(radial, "circ", axis=0, tiled=True)

    node_rows = displacement.reshape(axial_rows, circum_rows * degrees, vectors)
    count_ax = lax.axis_size("ax")
    top = lax.ppermute(node_rows[-1:], "ax", [(i, (i + 1) % count_ax) for i in range(count_ax)])
    bottom = lax.ppermute(node_rows[:1], "ax", [((i + 1) % count_ax, i) for i in range(count_ax)])
    first_nodes = jnp.concatenate(
        [top[:, :degrees], node_rows[:, :degrees], bottom[:, :degrees]], axis=0
    )
    last_nodes = jnp.concatenate(
        [top[:, -degrees:], node_rows[:, -degrees:], bottom[:, -degrees:]], axis=0
    )
    left = lax.ppermute(last_nodes, "circ", [(i, (i + 1) % sectors) for i in range(sectors)])
    right = lax.ppermute(first_nodes, "circ", [((i + 1) % sectors, i) for i in range(sectors)])
    gap = jnp.zeros((axial_rows + 2, 128 - 2 * degrees, vectors), displacement.dtype)
    halo = jnp.concatenate([right, gap, left], axis=1)
    global_row = lax.axis_index("ax") * axial_rows + jnp.arange(axial_rows, dtype=jnp.int32)
    lane_step = jnp.arange(stiffness.shape[2], dtype=jnp.int32) // (3 * degrees * degrees) - 1
    inside = (global_row[:, None] + lane_step[None, :] >= 0) & (
        global_row[:, None] + lane_step[None, :] < axial_total
    )
    blocks = jnp.where(inside[:, None, :], stiffness, jnp.zeros_like(stiffness))
    half = (axial_rows * 7) // 16
    force = banded_force(blocks, node_rows, top, bottom, halo, degrees, 0, half)

    force, table = lax.optimization_barrier((force, table))
    slot_index = source_owner[:, 0] * node_count + source_node
    velocity = jnp.take(table, slot_index, axis=0, mode="clip")

    panel_size = kernel.shape[3]
    source_cells = velocity.reshape(-1, panel_size, vectors)
    pressure, load_value = near_field(kernel, source_cells, areas, near_cells)

    load_owner = target_owner[:, 0]
    target_count = load_owner.shape[0]
    load_capacity = 5 * target_count // (2 * sectors)
    load_slot = slot_positions(load_owner, sectors, load_capacity)
    gather_slot = (
        load_slot[None, :] == jnp.arange(sectors * load_capacity, dtype=jnp.int32)[:, None]
    ).astype(jnp.bfloat16)
    outgoing = jnp.dot(gather_slot, load_value, preferred_element_type=jnp.float32).astype(
        jnp.bfloat16
    )
    outgoing = outgoing.reshape(sectors, load_capacity, vectors)
    radix = 32
    digits = jnp.stack([target_node // radix, target_node % radix], axis=0).astype(jnp.bfloat16)
    slot_digits = lax.dot_general(
        digits, gather_slot, (((1,), (1,)), ((), ())), preferred_element_type=jnp.float32
    ).astype(jnp.bfloat16)
    slot_digits = jnp.transpose(slot_digits.reshape(2, sectors, load_capacity), (1, 0, 2))
    digit_rows = -(-2 * load_capacity // vectors)
    slot_digits = jnp.pad(
        slot_digits.reshape(sectors, 2 * load_capacity),
        ((0, 0), (0, digit_rows * vectors - 2 * load_capacity)),
    ).reshape(sectors, digit_rows, vectors)
    packet = jnp.concatenate([outgoing, slot_digits], axis=1)
    packet, force = lax.optimization_barrier((packet, force))
    arrived = lax.all_to_all(packet, "circ", split_axis=0, concat_axis=0, tiled=True)
    force = banded_force(
        blocks, node_rows, top, bottom, halo, degrees, half, axial_rows - half, force
    )
    arrived_load = arrived[:, :load_capacity].reshape(-1, vectors)
    arrived_digits = (
        arrived[:, load_capacity:]
        .reshape(sectors, digit_rows * vectors)[:, : 2 * load_capacity]
        .reshape(sectors, 2, load_capacity)
        .astype(jnp.float32)
    )
    arrived_node = (arrived_digits[:, 0] * radix + arrived_digits[:, 1]).astype(jnp.int32)
    selector = (
        arrived_node.reshape(-1)[None, :] == jnp.arange(node_count, dtype=jnp.int32)[:, None]
    ).astype(jnp.bfloat16)
    fluid = jnp.dot(selector, arrived_load, preferred_element_type=jnp.float32)
    fluid = fluid.reshape(axial_rows, circum_rows, vectors)
    force = force.at[:, :circum_rows, :].add(-fluid)
    shell_force = jnp.transpose(
        force.reshape(axial_rows, degrees, circum_rows, vectors), (0, 2, 1, 3)
    )
    return (shell_force, pressure)


def solution(mesh):
    return jax.shard_map(
        body,
        mesh=mesh,
        in_specs=(
            P("ax", "circ", None, None),
            P("ax", "circ", None),
            P(("ax", "circ"), None, None, None, None),
            P(("ax", "circ")),
            P(("ax", "circ"), None),
            P(("ax", "circ"), None),
            P(("ax", "circ")),
            P(("ax", "circ"), None),
            P(("ax", "circ")),
        ),
        out_specs=(P("ax", "circ", None, None), P(None, ("ax", "circ"), None)),
        check_vma=False,
    )
```

```python
import functools

import jax
import jax.numpy as jnp
from jax import lax
from jax.experimental import pallas as pl
from jax.experimental.pallas import tpu as pltpu
from jax.sharding import PartitionSpec as P


def extended(cells, sides, width):
    for axis, dim in sides:
        count = lax.axis_size(axis)
        head = lax.slice_in_dim(cells, 0, width, axis=dim)
        tail = lax.slice_in_dim(cells, cells.shape[dim] - width, cells.shape[dim], axis=dim)
        cells = jnp.concatenate(
            [
                lax.ppermute(tail, axis, [(i, (i + 1) % count) for i in range(count)]),
                cells,
                lax.ppermute(head, axis, [((i + 1) % count, i) for i in range(count)]),
            ],
            axis=dim,
        )
    return cells


def slot_positions(owners, sectors, capacity):
    onehot = owners[:, None] == jnp.arange(sectors, dtype=jnp.int32)[None, :]
    count = owners.shape[0]
    order = jnp.arange(count, dtype=jnp.int32)
    earlier = (order[None, :] < order[:, None]).astype(jnp.bfloat16)
    before = jnp.dot(earlier, onehot.astype(jnp.bfloat16), preferred_element_type=jnp.float32)
    ranking = jnp.sum(jnp.where(onehot, before, 0.0), axis=1).astype(jnp.int32)
    return owners * capacity + ranking


def pressure_kernel(near_ref, kern_ref, vel_ref, area_ref, *rest, with_load):
    p_ref = rest[-2] if with_load else rest[-1]
    g = pl.program_id(0)
    near_count = kern_ref.shape[1]
    for n in range(near_count):
        m = near_ref[g, n]
        prod = jnp.dot(kern_ref[0, n, 0], vel_ref[m], preferred_element_type=jnp.float32)
        if n == 0:
            p_ref[0] = prod
        else:
            p_ref[0] += prod
    if with_load:
        load_ref = rest[-1]
        load_ref[...] = (area_ref[...] * p_ref[0]).astype(load_ref.dtype)


def near_field(kernel, source_cells, areas, near_cells, part, previous=None):
    cells_dev, near_count, _, panel, _ = kernel.shape
    src_cells, _, vectors = source_cells.shape
    targets = cells_dev * panel
    with_load = previous is None
    in_specs = [
        pl.BlockSpec((1, near_count, 1, panel, panel), lambda g, near: (g, 0, part, 0, 0)),
        pl.BlockSpec((src_cells, panel, vectors), lambda g, near: (0, 0, 0)),
        pl.BlockSpec((panel, 1), lambda g, near: (g, 0)),
    ]
    operands = [near_cells, kernel, source_cells, areas.reshape(targets, 1)]
    out_specs = [pl.BlockSpec((1, panel, vectors), lambda g, near: (part, g, 0))]
    out_shape = [jax.ShapeDtypeStruct((2, targets, vectors), jnp.float32)]
    aliases = {}
    if with_load:
        out_specs.append(pl.BlockSpec((panel, vectors), lambda g, near: (g, 0)))
        out_shape.append(jax.ShapeDtypeStruct((targets, vectors), jnp.bfloat16))
    else:
        in_specs.append(pl.BlockSpec(memory_space=pl.ANY))
        operands.append(previous)
        aliases = {len(operands) - 1: 0}
    grid_spec = pltpu.PrefetchScalarGridSpec(
        num_scalar_prefetch=1, grid=(cells_dev,), in_specs=in_specs, out_specs=out_specs
    )
    return pl.pallas_call(
        functools.partial(pressure_kernel, with_load=with_load),
        grid_spec=grid_spec,
        out_shape=out_shape,
        input_output_aliases=aliases,
    )(*operands)


def stiff_kernel(s_ref, rows_ref, top_ref, bottom_ref, halo_ref, *rest, degrees, first):
    out_ref, sel_ref, band_ref = rest[-3:]
    step = pl.program_id(0)
    a = step + first
    last = rows_ref.shape[0] - 1
    nodes = s_ref.shape[1]
    offsets = band_ref.shape[0]
    group = 128
    span = offsets * degrees
    wide = band_ref.shape[2]

    per_tile = group // span

    @pl.when(step == 0)
    def _():
        k = lax.broadcasted_iota(jnp.int32, sel_ref.shape, 0)
        y = lax.broadcasted_iota(jnp.int32, sel_ref.shape, 1)
        lane = y % group
        blk = (y // group) * per_tile + lane // span
        inner = lane % span
        target = (
            (blk // degrees) * (offsets * degrees * degrees)
            + (inner // degrees) * (degrees * degrees)
            + (blk % degrees) * degrees
            + inner % degrees
        )
        valid = (lane < per_tile * span) & (blk < offsets * degrees)
        sel_ref[...] = jnp.where(valid & (k == target), 1.0, 0.0).astype(sel_ref.dtype)
        band_ref[...] = jnp.zeros(band_ref.shape, band_ref.dtype)

    spread = jnp.dot(s_ref[0], sel_ref[...], preferred_element_type=jnp.float32)
    pad = jnp.zeros((8, group), jnp.float32)
    tiles = wide // group
    lane_id = lax.broadcasted_iota(jnp.int32, (nodes, group), 1)
    for d in range(offsets):
        for i in range(degrees):
            blk = d * degrees + i
            b, q = blk // per_tile, blk % per_tile
            piece = spread[:, b * group : (b + 1) * group]
            piece = jnp.where(
                (lane_id >= q * span) & (lane_id < (q + 1) * span), piece, jnp.zeros_like(piece)
            )
            for h in range(nodes // 16):
                base = 16 * h * degrees - degrees
                tile = base // group
                parts = []
                for g in (2 * h, 2 * h + 1):
                    rows = jnp.concatenate([piece[g * 8 : (g + 1) * 8], pad], axis=1)
                    shift = (8 * g * degrees - degrees - tile * group - q * span) % (2 * group)
                    rows = pltpu.roll(rows, shift, 1)
                    parts.append(pltpu.roll(rows, 0, 1, stride=degrees, stride_axis=0))
                window = jnp.concatenate(parts, axis=0).astype(band_ref.dtype)
                top_row = i * nodes + 16 * h
                for t in range(2):
                    lane = ((tile + t) % tiles) * group
                    band_ref[d, top_row : top_row + 16, lane : lane + group] = window[
                        :, t * group : (t + 1) * group
                    ]
    above = jnp.where(a == 0, top_ref[0], rows_ref[jnp.maximum(a - 1, 0)])
    below = jnp.where(a == last, bottom_ref[0], rows_ref[jnp.minimum(a + 1, last)])
    acc = None
    for d, rows in enumerate((above, rows_ref[a], below)):
        both = jnp.concatenate([rows, halo_ref[a + d]], axis=0)
        part = jnp.dot(band_ref[d], both, preferred_element_type=jnp.float32)
        acc = part if acc is None else acc + part
    out_ref[0] = acc


def banded_force(blocks, rows, top, bottom, halo, degrees, first, count, previous=None):
    axial_rows, nodes, width = blocks.shape
    offsets = 3
    vectors = rows.shape[-1]
    band_rows = degrees * nodes
    band_cols = band_rows + halo.shape[1]
    sel_cols = -(-offsets * degrees // (128 // (offsets * degrees))) * 128
    in_specs = [
        pl.BlockSpec((1, nodes, width), lambda a: (a + first, 0, 0)),
        pl.BlockSpec(rows.shape, lambda a: (0, 0, 0)),
        pl.BlockSpec(top.shape, lambda a: (0, 0, 0)),
        pl.BlockSpec(bottom.shape, lambda a: (0, 0, 0)),
        pl.BlockSpec(halo.shape, lambda a: (0, 0, 0)),
    ]
    operands = [blocks, rows, top, bottom, halo]
    aliases = {}
    if previous is not None:
        in_specs.append(pl.BlockSpec(memory_space=pl.ANY))
        operands.append(previous)
        aliases = {len(operands) - 1: 0}
    return pl.pallas_call(
        functools.partial(stiff_kernel, degrees=degrees, first=first),
        grid=(count,),
        in_specs=in_specs,
        out_specs=pl.BlockSpec((1, band_rows, vectors), lambda a: (a + first, 0, 0)),
        out_shape=jax.ShapeDtypeStruct((axial_rows, band_rows, vectors), jnp.float32),
        scratch_shapes=[
            pltpu.VMEM((width, sel_cols), jnp.bfloat16),
            pltpu.VMEM((offsets, band_rows, band_cols), jnp.bfloat16),
        ],
        input_output_aliases=aliases,
    )(*operands)


def body(
    displacement,
    stiffness,
    kernel,
    areas,
    near_cells,
    source_owner,
    source_node,
    target_owner,
    target_node,
):
    axial_rows = displacement.shape[0]
    circum_rows = displacement.shape[1]
    degrees = displacement.shape[2]
    vectors = displacement.shape[3]
    sectors = lax.axis_size("circ")
    axial_total = axial_rows * lax.axis_size("ax")
    node_count = axial_rows * circum_rows

    radial = displacement[:, :, 0, :].reshape(node_count, vectors)
    table = lax.all_gather(radial, "circ", axis=0, tiled=True)

    node_rows = displacement.reshape(axial_rows, circum_rows * degrees, vectors)
    count_ax = lax.axis_size("ax")
    top = lax.ppermute(node_rows[-1:], "ax", [(i, (i + 1) % count_ax) for i in range(count_ax)])
    bottom = lax.ppermute(node_rows[:1], "ax", [((i + 1) % count_ax, i) for i in range(count_ax)])
    first_nodes = jnp.concatenate(
        [top[:, :degrees], node_rows[:, :degrees], bottom[:, :degrees]], axis=0
    )
    last_nodes = jnp.concatenate(
        [top[:, -degrees:], node_rows[:, -degrees:], bottom[:, -degrees:]], axis=0
    )
    left = lax.ppermute(last_nodes, "circ", [(i, (i + 1) % sectors) for i in range(sectors)])
    right = lax.ppermute(first_nodes, "circ", [((i + 1) % sectors, i) for i in range(sectors)])
    gap = jnp.zeros((axial_rows + 2, 128 - 2 * degrees, vectors), displacement.dtype)
    halo = jnp.concatenate([right, gap, left], axis=1)
    global_row = lax.axis_index("ax") * axial_rows + jnp.arange(axial_rows, dtype=jnp.int32)
    lane_step = jnp.arange(stiffness.shape[2], dtype=jnp.int32) // (3 * degrees * degrees) - 1
    inside = (global_row[:, None] + lane_step[None, :] >= 0) & (
        global_row[:, None] + lane_step[None, :] < axial_total
    )
    blocks = jnp.where(inside[:, None, :], stiffness, jnp.zeros_like(stiffness))
    half = (axial_rows * 7) // 16
    force = banded_force(blocks, node_rows, top, bottom, halo, degrees, 0, half)

    force, table = lax.optimization_barrier((force, table))
    slot_index = source_owner[:, 0] * node_count + source_node
    velocity = jnp.take(table, slot_index, axis=0, mode="clip")

    panel_size = kernel.shape[3]
    source_cells = velocity.reshape(-1, panel_size, vectors)
    pressure, load_value = near_field(kernel, source_cells, areas, near_cells, 0)

    load_owner = target_owner[:, 0]
    target_count = load_owner.shape[0]
    load_capacity = 5 * target_count // (2 * sectors)
    load_slot = slot_positions(load_owner, sectors, load_capacity)
    gather_slot = (
        load_slot[None, :] == jnp.arange(sectors * load_capacity, dtype=jnp.int32)[:, None]
    ).astype(jnp.bfloat16)
    outgoing = jnp.dot(gather_slot, load_value, preferred_element_type=jnp.float32).astype(
        jnp.bfloat16
    )
    outgoing = outgoing.reshape(sectors, load_capacity, vectors)
    radix = 32
    digits = jnp.stack([target_node // radix, target_node % radix], axis=0).astype(jnp.bfloat16)
    slot_digits = lax.dot_general(
        digits, gather_slot, (((1,), (1,)), ((), ())), preferred_element_type=jnp.float32
    ).astype(jnp.bfloat16)
    slot_digits = jnp.transpose(slot_digits.reshape(2, sectors, load_capacity), (1, 0, 2))
    digit_rows = -(-2 * load_capacity // vectors)
    slot_digits = jnp.pad(
        slot_digits.reshape(sectors, 2 * load_capacity),
        ((0, 0), (0, digit_rows * vectors - 2 * load_capacity)),
    ).reshape(sectors, digit_rows, vectors)
    packet = jnp.concatenate([outgoing, slot_digits], axis=1)
    packet, force, pressure = lax.optimization_barrier((packet, force, pressure))
    arrived = lax.all_to_all(packet, "circ", split_axis=0, concat_axis=0, tiled=True)
    force = banded_force(
        blocks, node_rows, top, bottom, halo, degrees, half, axial_rows - half, force
    )
    pressure = near_field(kernel, source_cells, areas, near_cells, 1, pressure)[0]
    arrived_load = arrived[:, :load_capacity].reshape(-1, vectors)
    arrived_digits = (
        arrived[:, load_capacity:]
        .reshape(sectors, digit_rows * vectors)[:, : 2 * load_capacity]
        .reshape(sectors, 2, load_capacity)
        .astype(jnp.float32)
    )
    arrived_node = (arrived_digits[:, 0] * radix + arrived_digits[:, 1]).astype(jnp.int32)
    selector = (
        arrived_node.reshape(-1)[None, :] == jnp.arange(node_count, dtype=jnp.int32)[:, None]
    ).astype(jnp.bfloat16)
    fluid = jnp.dot(selector, arrived_load, preferred_element_type=jnp.float32)
    fluid = fluid.reshape(axial_rows, circum_rows, vectors)
    force = force.at[:, :circum_rows, :].add(-fluid)
    shell_force = jnp.transpose(
        force.reshape(axial_rows, degrees, circum_rows, vectors), (0, 2, 1, 3)
    )
    return (shell_force, pressure)


def solution(mesh):
    return jax.shard_map(
        body,
        mesh=mesh,
        in_specs=(
            P("ax", "circ", None, None),
            P("ax", "circ", None),
            P(("ax", "circ"), None, None, None, None),
            P(("ax", "circ")),
            P(("ax", "circ"), None),
            P(("ax", "circ"), None),
            P(("ax", "circ")),
            P(("ax", "circ"), None),
            P(("ax", "circ")),
        ),
        out_specs=(P("ax", "circ", None, None), P(None, ("ax", "circ"), None)),
        check_vma=False,
    )
```

```python
import functools

import jax
import jax.numpy as jnp
from jax import lax
from jax.experimental import pallas as pl
from jax.experimental.pallas import tpu as pltpu
from jax.sharding import PartitionSpec as P


def extended(cells, sides, width):
    for axis, dim in sides:
        count = lax.axis_size(axis)
        head = lax.slice_in_dim(cells, 0, width, axis=dim)
        tail = lax.slice_in_dim(cells, cells.shape[dim] - width, cells.shape[dim], axis=dim)
        cells = jnp.concatenate(
            [
                lax.ppermute(tail, axis, [(i, (i + 1) % count) for i in range(count)]),
                cells,
                lax.ppermute(head, axis, [((i + 1) % count, i) for i in range(count)]),
            ],
            axis=dim,
        )
    return cells


def slot_positions(owners, sectors, capacity):
    onehot = owners[:, None] == jnp.arange(sectors, dtype=jnp.int32)[None, :]
    count = owners.shape[0]
    order = jnp.arange(count, dtype=jnp.int32)
    earlier = (order[None, :] < order[:, None]).astype(jnp.bfloat16)
    before = jnp.dot(earlier, onehot.astype(jnp.bfloat16), preferred_element_type=jnp.float32)
    ranking = jnp.sum(jnp.where(onehot, before, 0.0), axis=1).astype(jnp.int32)
    return owners * capacity + ranking


def pressure_kernel(near_ref, kern_ref, vel_ref, area_ref, *rest, with_load):
    p_ref = rest[-2] if with_load else rest[-1]
    g = pl.program_id(0)
    near_count = kern_ref.shape[1]
    for n in range(near_count):
        m = near_ref[g, n]
        prod = jnp.dot(kern_ref[0, n, 0], vel_ref[m], preferred_element_type=jnp.float32)
        if n == 0:
            p_ref[0] = prod
        else:
            p_ref[0] += prod
    if with_load:
        load_ref = rest[-1]
        load_ref[...] = (area_ref[...] * p_ref[0]).astype(load_ref.dtype)


def near_field(kernel, source_cells, areas, near_cells, part, previous=None):
    cells_dev, near_count, _, panel, _ = kernel.shape
    src_cells, _, vectors = source_cells.shape
    targets = cells_dev * panel
    with_load = previous is None
    in_specs = [
        pl.BlockSpec((1, near_count, 1, panel, panel), lambda g, near: (g, 0, part, 0, 0)),
        pl.BlockSpec((src_cells, panel, vectors), lambda g, near: (0, 0, 0)),
        pl.BlockSpec((panel, 1), lambda g, near: (g, 0)),
    ]
    operands = [near_cells, kernel, source_cells, areas.reshape(targets, 1)]
    out_specs = [pl.BlockSpec((1, panel, vectors), lambda g, near: (part, g, 0))]
    out_shape = [jax.ShapeDtypeStruct((2, targets, vectors), jnp.float32)]
    aliases = {}
    if with_load:
        out_specs.append(pl.BlockSpec((panel, vectors), lambda g, near: (g, 0)))
        out_shape.append(jax.ShapeDtypeStruct((targets, vectors), jnp.bfloat16))
    else:
        in_specs.append(pl.BlockSpec(memory_space=pl.ANY))
        operands.append(previous)
        aliases = {len(operands) - 1: 0}
    grid_spec = pltpu.PrefetchScalarGridSpec(
        num_scalar_prefetch=1, grid=(cells_dev,), in_specs=in_specs, out_specs=out_specs
    )
    return pl.pallas_call(
        functools.partial(pressure_kernel, with_load=with_load),
        grid_spec=grid_spec,
        out_shape=out_shape,
        input_output_aliases=aliases,
    )(*operands)


def stiff_kernel(s_ref, rows_ref, top_ref, bottom_ref, halo_ref, *rest, degrees, first):
    out_ref, sel_ref, band_ref = rest[-3:]
    step = pl.program_id(0)
    a = step + first
    last = rows_ref.shape[0] - 1
    nodes = s_ref.shape[1]
    offsets = band_ref.shape[0]
    group = 128
    span = offsets * degrees
    wide = band_ref.shape[2]

    per_tile = group // span

    @pl.when(step == 0)
    def _():
        k = lax.broadcasted_iota(jnp.int32, sel_ref.shape, 0)
        y = lax.broadcasted_iota(jnp.int32, sel_ref.shape, 1)
        lane = y % group
        blk = (y // group) * per_tile + lane // span
        inner = lane % span
        target = (
            (blk // degrees) * (offsets * degrees * degrees)
            + (inner // degrees) * (degrees * degrees)
            + (blk % degrees) * degrees
            + inner % degrees
        )
        valid = (lane < per_tile * span) & (blk < offsets * degrees)
        sel_ref[...] = jnp.where(valid & (k == target), 1.0, 0.0).astype(sel_ref.dtype)
        band_ref[...] = jnp.zeros(band_ref.shape, band_ref.dtype)

    spread = jnp.dot(s_ref[0], sel_ref[...], preferred_element_type=jnp.float32)
    pad = jnp.zeros((8, group), jnp.float32)
    tiles = wide // group
    lane_id = lax.broadcasted_iota(jnp.int32, (nodes, group), 1)
    for d in range(offsets):
        for i in range(degrees):
            blk = d * degrees + i
            b, q = blk // per_tile, blk % per_tile
            piece = spread[:, b * group : (b + 1) * group]
            piece = jnp.where(
                (lane_id >= q * span) & (lane_id < (q + 1) * span), piece, jnp.zeros_like(piece)
            )
            for h in range(nodes // 16):
                base = 16 * h * degrees - degrees
                tile = base // group
                parts = []
                for g in (2 * h, 2 * h + 1):
                    rows = jnp.concatenate([piece[g * 8 : (g + 1) * 8], pad], axis=1)
                    shift = (8 * g * degrees - degrees - tile * group - q * span) % (2 * group)
                    rows = pltpu.roll(rows, shift, 1)
                    parts.append(pltpu.roll(rows, 0, 1, stride=degrees, stride_axis=0))
                window = jnp.concatenate(parts, axis=0).astype(band_ref.dtype)
                top_row = i * nodes + 16 * h
                for t in range(2):
                    lane = ((tile + t) % tiles) * group
                    band_ref[d, top_row : top_row + 16, lane : lane + group] = window[
                        :, t * group : (t + 1) * group
                    ]
    above = jnp.where(a == 0, top_ref[0], rows_ref[jnp.maximum(a - 1, 0)])
    below = jnp.where(a == last, bottom_ref[0], rows_ref[jnp.minimum(a + 1, last)])
    acc = None
    for d, rows in enumerate((above, rows_ref[a], below)):
        both = jnp.concatenate([rows, halo_ref[a + d]], axis=0)
        part = jnp.dot(band_ref[d], both, preferred_element_type=jnp.float32)
        acc = part if acc is None else acc + part
    out_ref[0] = acc


def banded_force(blocks, rows, top, bottom, halo, degrees, first, count, previous=None):
    axial_rows, nodes, width = blocks.shape
    offsets = 3
    vectors = rows.shape[-1]
    band_rows = degrees * nodes
    band_cols = band_rows + halo.shape[1]
    sel_cols = -(-offsets * degrees // (128 // (offsets * degrees))) * 128
    in_specs = [
        pl.BlockSpec((1, nodes, width), lambda a: (a + first, 0, 0)),
        pl.BlockSpec(rows.shape, lambda a: (0, 0, 0)),
        pl.BlockSpec(top.shape, lambda a: (0, 0, 0)),
        pl.BlockSpec(bottom.shape, lambda a: (0, 0, 0)),
        pl.BlockSpec(halo.shape, lambda a: (0, 0, 0)),
    ]
    operands = [blocks, rows, top, bottom, halo]
    aliases = {}
    if previous is not None:
        in_specs.append(pl.BlockSpec(memory_space=pl.ANY))
        operands.append(previous)
        aliases = {len(operands) - 1: 0}
    return pl.pallas_call(
        functools.partial(stiff_kernel, degrees=degrees, first=first),
        grid=(count,),
        in_specs=in_specs,
        out_specs=pl.BlockSpec((1, band_rows, vectors), lambda a: (a + first, 0, 0)),
        out_shape=jax.ShapeDtypeStruct((axial_rows, band_rows, vectors), jnp.float32),
        scratch_shapes=[
            pltpu.VMEM((width, sel_cols), jnp.bfloat16),
            pltpu.VMEM((offsets, band_rows, band_cols), jnp.bfloat16),
        ],
        input_output_aliases=aliases,
    )(*operands)


def body(
    displacement,
    stiffness,
    kernel,
    areas,
    near_cells,
    source_owner,
    source_node,
    target_owner,
    target_node,
):
    axial_rows = displacement.shape[0]
    circum_rows = displacement.shape[1]
    degrees = displacement.shape[2]
    vectors = displacement.shape[3]
    sectors = lax.axis_size("circ")
    axial_total = axial_rows * lax.axis_size("ax")
    node_count = axial_rows * circum_rows

    radial = displacement[:, :, 0, :].reshape(node_count, vectors)
    table = lax.all_gather(radial, "circ", axis=0, tiled=True)

    node_rows = displacement.reshape(axial_rows, circum_rows * degrees, vectors)
    count_ax = lax.axis_size("ax")
    top = lax.ppermute(node_rows[-1:], "ax", [(i, (i + 1) % count_ax) for i in range(count_ax)])
    bottom = lax.ppermute(node_rows[:1], "ax", [((i + 1) % count_ax, i) for i in range(count_ax)])
    first_nodes = jnp.concatenate(
        [top[:, :degrees], node_rows[:, :degrees], bottom[:, :degrees]], axis=0
    )
    last_nodes = jnp.concatenate(
        [top[:, -degrees:], node_rows[:, -degrees:], bottom[:, -degrees:]], axis=0
    )
    left = lax.ppermute(last_nodes, "circ", [(i, (i + 1) % sectors) for i in range(sectors)])
    right = lax.ppermute(first_nodes, "circ", [((i + 1) % sectors, i) for i in range(sectors)])
    gap = jnp.zeros((axial_rows + 2, 128 - 2 * degrees, vectors), displacement.dtype)
    halo = jnp.concatenate([right, gap, left], axis=1)
    global_row = lax.axis_index("ax") * axial_rows + jnp.arange(axial_rows, dtype=jnp.int32)
    lane_step = jnp.arange(stiffness.shape[2], dtype=jnp.int32) // (3 * degrees * degrees) - 1
    inside = (global_row[:, None] + lane_step[None, :] >= 0) & (
        global_row[:, None] + lane_step[None, :] < axial_total
    )
    blocks = jnp.where(inside[:, None, :], stiffness, jnp.zeros_like(stiffness))
    half = axial_rows // 2
    force = banded_force(blocks, node_rows, top, bottom, halo, degrees, 0, half)

    force, table = lax.optimization_barrier((force, table))
    slot_index = source_owner[:, 0] * node_count + source_node
    velocity = jnp.take(table, slot_index, axis=0, mode="clip")

    panel_size = kernel.shape[3]
    source_cells = velocity.reshape(-1, panel_size, vectors)
    pressure, load_value = near_field(kernel, source_cells, areas, near_cells, 0)

    load_owner = target_owner[:, 0]
    target_count = load_owner.shape[0]
    load_capacity = 5 * target_count // (2 * sectors)
    load_slot = slot_positions(load_owner, sectors, load_capacity)
    gather_slot = (
        load_slot[None, :] == jnp.arange(sectors * load_capacity, dtype=jnp.int32)[:, None]
    ).astype(jnp.bfloat16)
    outgoing = jnp.dot(gather_slot, load_value, preferred_element_type=jnp.float32).astype(
        jnp.bfloat16
    )
    outgoing = outgoing.reshape(sectors, load_capacity, vectors)
    radix = 32
    digits = jnp.stack([target_node // radix, target_node % radix], axis=0).astype(jnp.bfloat16)
    slot_digits = lax.dot_general(
        digits, gather_slot, (((1,), (1,)), ((), ())), preferred_element_type=jnp.float32
    ).astype(jnp.bfloat16)
    slot_digits = jnp.transpose(slot_digits.reshape(2, sectors, load_capacity), (1, 0, 2))
    digit_rows = -(-2 * load_capacity // vectors)
    slot_digits = jnp.pad(
        slot_digits.reshape(sectors, 2 * load_capacity),
        ((0, 0), (0, digit_rows * vectors - 2 * load_capacity)),
    ).reshape(sectors, digit_rows, vectors)
    packet = jnp.concatenate([outgoing, slot_digits], axis=1)
    packet, force, pressure = lax.optimization_barrier((packet, force, pressure))
    arrived = lax.all_to_all(packet, "circ", split_axis=0, concat_axis=0, tiled=True)
    force = banded_force(
        blocks, node_rows, top, bottom, halo, degrees, half, axial_rows - half, force
    )
    pressure = near_field(kernel, source_cells, areas, near_cells, 1, pressure)[0]
    arrived_load = arrived[:, :load_capacity].reshape(-1, vectors)
    arrived_digits = (
        arrived[:, load_capacity:]
        .reshape(sectors, digit_rows * vectors)[:, : 2 * load_capacity]
        .reshape(sectors, 2, load_capacity)
        .astype(jnp.float32)
    )
    arrived_node = (arrived_digits[:, 0] * radix + arrived_digits[:, 1]).astype(jnp.int32)
    selector = (
        arrived_node.reshape(-1)[None, :] == jnp.arange(node_count, dtype=jnp.int32)[:, None]
    ).astype(jnp.bfloat16)
    fluid = jnp.dot(selector, arrived_load, preferred_element_type=jnp.float32)
    fluid = fluid.reshape(axial_rows, circum_rows, vectors)
    force = force.at[:, :circum_rows, :].add(-fluid)
    shell_force = jnp.transpose(
        force.reshape(axial_rows, degrees, circum_rows, vectors), (0, 2, 1, 3)
    )
    return (shell_force, pressure)


def solution(mesh):
    return jax.shard_map(
        body,
        mesh=mesh,
        in_specs=(
            P("ax", "circ", None, None),
            P("ax", "circ", None),
            P(("ax", "circ"), None, None, None, None),
            P(("ax", "circ")),
            P(("ax", "circ"), None),
            P(("ax", "circ"), None),
            P(("ax", "circ")),
            P(("ax", "circ"), None),
            P(("ax", "circ")),
        ),
        out_specs=(P("ax", "circ", None, None), P(None, ("ax", "circ"), None)),
        check_vma=False,
    )
```

```python
import functools

import jax
import jax.numpy as jnp
from jax import lax
from jax.experimental import pallas as pl
from jax.experimental.pallas import tpu as pltpu
from jax.sharding import PartitionSpec as P


def extended(cells, sides, width):
    for axis, dim in sides:
        count = lax.axis_size(axis)
        head = lax.slice_in_dim(cells, 0, width, axis=dim)
        tail = lax.slice_in_dim(cells, cells.shape[dim] - width, cells.shape[dim], axis=dim)
        cells = jnp.concatenate(
            [
                lax.ppermute(tail, axis, [(i, (i + 1) % count) for i in range(count)]),
                cells,
                lax.ppermute(head, axis, [((i + 1) % count, i) for i in range(count)]),
            ],
            axis=dim,
        )
    return cells


def slot_positions(owners, sectors, capacity):
    onehot = owners[:, None] == jnp.arange(sectors, dtype=jnp.int32)[None, :]
    count = owners.shape[0]
    order = jnp.arange(count, dtype=jnp.int32)
    earlier = (order[None, :] < order[:, None]).astype(jnp.bfloat16)
    before = jnp.dot(earlier, onehot.astype(jnp.bfloat16), preferred_element_type=jnp.float32)
    ranking = jnp.sum(jnp.where(onehot, before, 0.0), axis=1).astype(jnp.int32)
    return owners * capacity + ranking


def pressure_kernel(near_ref, kern_ref, vel_ref, area_ref, *rest, with_load):
    p_ref = rest[-2] if with_load else rest[-1]
    g = pl.program_id(0)
    near_count = kern_ref.shape[1]
    for n in range(near_count):
        m = near_ref[g, n]
        prod = jnp.dot(kern_ref[0, n, 0], vel_ref[m], preferred_element_type=jnp.float32)
        if n == 0:
            p_ref[0] = prod
        else:
            p_ref[0] += prod
    if with_load:
        load_ref = rest[-1]
        load_ref[...] = (area_ref[...] * p_ref[0]).astype(load_ref.dtype)


def near_field(kernel, source_cells, areas, near_cells, part, previous=None):
    cells_dev, near_count, _, panel, _ = kernel.shape
    src_cells, _, vectors = source_cells.shape
    targets = cells_dev * panel
    with_load = previous is None
    in_specs = [
        pl.BlockSpec((1, near_count, 1, panel, panel), lambda g, near: (g, 0, part, 0, 0)),
        pl.BlockSpec((src_cells, panel, vectors), lambda g, near: (0, 0, 0)),
        pl.BlockSpec((panel, 1), lambda g, near: (g, 0)),
    ]
    operands = [near_cells, kernel, source_cells, areas.reshape(targets, 1)]
    out_specs = [pl.BlockSpec((1, panel, vectors), lambda g, near: (part, g, 0))]
    out_shape = [jax.ShapeDtypeStruct((2, targets, vectors), jnp.float32)]
    aliases = {}
    if with_load:
        out_specs.append(pl.BlockSpec((panel, vectors), lambda g, near: (g, 0)))
        out_shape.append(jax.ShapeDtypeStruct((targets, vectors), jnp.bfloat16))
    else:
        in_specs.append(pl.BlockSpec(memory_space=pl.ANY))
        operands.append(previous)
        aliases = {len(operands) - 1: 0}
    grid_spec = pltpu.PrefetchScalarGridSpec(
        num_scalar_prefetch=1, grid=(cells_dev,), in_specs=in_specs, out_specs=out_specs
    )
    return pl.pallas_call(
        functools.partial(pressure_kernel, with_load=with_load),
        grid_spec=grid_spec,
        out_shape=out_shape,
        input_output_aliases=aliases,
    )(*operands)


def stiff_kernel(s_ref, rows_ref, top_ref, bottom_ref, halo_ref, *rest, degrees, first):
    out_ref, sel_ref, band_ref = rest[-3:]
    step = pl.program_id(0)
    a = step + first
    last = rows_ref.shape[0] - 1
    nodes = s_ref.shape[1]
    offsets = band_ref.shape[0]
    group = 128
    span = offsets * degrees
    wide = band_ref.shape[2]

    per_tile = group // span

    @pl.when(step == 0)
    def _():
        k = lax.broadcasted_iota(jnp.int32, sel_ref.shape, 0)
        y = lax.broadcasted_iota(jnp.int32, sel_ref.shape, 1)
        lane = y % group
        blk = (y // group) * per_tile + lane // span
        inner = lane % span
        target = (
            (blk // degrees) * (offsets * degrees * degrees)
            + (inner // degrees) * (degrees * degrees)
            + (blk % degrees) * degrees
            + inner % degrees
        )
        valid = (lane < per_tile * span) & (blk < offsets * degrees)
        sel_ref[...] = jnp.where(valid & (k == target), 1.0, 0.0).astype(sel_ref.dtype)
        band_ref[...] = jnp.zeros(band_ref.shape, band_ref.dtype)

    spread = jnp.dot(s_ref[0], sel_ref[...], preferred_element_type=jnp.float32)
    pad = jnp.zeros((8, group), jnp.float32)
    tiles = wide // group
    lane_id = lax.broadcasted_iota(jnp.int32, (nodes, group), 1)
    for d in range(offsets):
        for i in range(degrees):
            blk = d * degrees + i
            b, q = blk // per_tile, blk % per_tile
            piece = spread[:, b * group : (b + 1) * group]
            piece = jnp.where(
                (lane_id >= q * span) & (lane_id < (q + 1) * span), piece, jnp.zeros_like(piece)
            )
            for h in range(nodes // 16):
                base = 16 * h * degrees - degrees
                tile = base // group
                parts = []
                for g in (2 * h, 2 * h + 1):
                    rows = jnp.concatenate([piece[g * 8 : (g + 1) * 8], pad], axis=1)
                    shift = (8 * g * degrees - degrees - tile * group - q * span) % (2 * group)
                    rows = pltpu.roll(rows, shift, 1)
                    parts.append(pltpu.roll(rows, 0, 1, stride=degrees, stride_axis=0))
                window = jnp.concatenate(parts, axis=0).astype(band_ref.dtype)
                top_row = i * nodes + 16 * h
                for t in range(2):
                    lane = ((tile + t) % tiles) * group
                    band_ref[d, top_row : top_row + 16, lane : lane + group] = window[
                        :, t * group : (t + 1) * group
                    ]
    above = jnp.where(a == 0, top_ref[0], rows_ref[jnp.maximum(a - 1, 0)])
    below = jnp.where(a == last, bottom_ref[0], rows_ref[jnp.minimum(a + 1, last)])
    acc = None
    for d, rows in enumerate((above, rows_ref[a], below)):
        both = jnp.concatenate([rows, halo_ref[a + d]], axis=0)
        part = jnp.dot(band_ref[d], both, preferred_element_type=jnp.float32)
        acc = part if acc is None else acc + part
    out_ref[0] = acc


def banded_force(blocks, rows, top, bottom, halo, degrees, first, count, previous=None):
    axial_rows, nodes, width = blocks.shape
    offsets = 3
    vectors = rows.shape[-1]
    band_rows = degrees * nodes
    band_cols = band_rows + halo.shape[1]
    sel_cols = -(-offsets * degrees // (128 // (offsets * degrees))) * 128
    in_specs = [
        pl.BlockSpec((1, nodes, width), lambda a: (a + first, 0, 0)),
        pl.BlockSpec(rows.shape, lambda a: (0, 0, 0)),
        pl.BlockSpec(top.shape, lambda a: (0, 0, 0)),
        pl.BlockSpec(bottom.shape, lambda a: (0, 0, 0)),
        pl.BlockSpec(halo.shape, lambda a: (0, 0, 0)),
    ]
    operands = [blocks, rows, top, bottom, halo]
    aliases = {}
    if previous is not None:
        in_specs.append(pl.BlockSpec(memory_space=pl.ANY))
        operands.append(previous)
        aliases = {len(operands) - 1: 0}
    return pl.pallas_call(
        functools.partial(stiff_kernel, degrees=degrees, first=first),
        grid=(count,),
        in_specs=in_specs,
        out_specs=pl.BlockSpec((1, band_rows, vectors), lambda a: (a + first, 0, 0)),
        out_shape=jax.ShapeDtypeStruct((axial_rows, band_rows, vectors), jnp.float32),
        scratch_shapes=[
            pltpu.VMEM((width, sel_cols), jnp.bfloat16),
            pltpu.VMEM((offsets, band_rows, band_cols), jnp.bfloat16),
        ],
        input_output_aliases=aliases,
    )(*operands)


def body(
    displacement,
    stiffness,
    kernel,
    areas,
    near_cells,
    source_owner,
    source_node,
    target_owner,
    target_node,
):
    axial_rows = displacement.shape[0]
    circum_rows = displacement.shape[1]
    degrees = displacement.shape[2]
    vectors = displacement.shape[3]
    sectors = lax.axis_size("circ")
    axial_total = axial_rows * lax.axis_size("ax")
    node_count = axial_rows * circum_rows

    radial = displacement[:, :, 0, :].reshape(node_count, vectors)
    table = lax.all_gather(radial, "circ", axis=0, tiled=True)

    node_rows = displacement.reshape(axial_rows, circum_rows * degrees, vectors)
    count_ax = lax.axis_size("ax")
    top = lax.ppermute(node_rows[-1:], "ax", [(i, (i + 1) % count_ax) for i in range(count_ax)])
    bottom = lax.ppermute(node_rows[:1], "ax", [((i + 1) % count_ax, i) for i in range(count_ax)])
    first_nodes = jnp.concatenate(
        [top[:, :degrees], node_rows[:, :degrees], bottom[:, :degrees]], axis=0
    )
    last_nodes = jnp.concatenate(
        [top[:, -degrees:], node_rows[:, -degrees:], bottom[:, -degrees:]], axis=0
    )
    left = lax.ppermute(last_nodes, "circ", [(i, (i + 1) % sectors) for i in range(sectors)])
    right = lax.ppermute(first_nodes, "circ", [((i + 1) % sectors, i) for i in range(sectors)])
    gap = jnp.zeros((axial_rows + 2, 128 - 2 * degrees, vectors), displacement.dtype)
    halo = jnp.concatenate([right, gap, left], axis=1)
    global_row = lax.axis_index("ax") * axial_rows + jnp.arange(axial_rows, dtype=jnp.int32)
    lane_step = jnp.arange(stiffness.shape[2], dtype=jnp.int32) // (3 * degrees * degrees) - 1
    inside = (global_row[:, None] + lane_step[None, :] >= 0) & (
        global_row[:, None] + lane_step[None, :] < axial_total
    )
    blocks = jnp.where(inside[:, None, :], stiffness, jnp.zeros_like(stiffness))
    half = (axial_rows * 9) // 16
    force = banded_force(blocks, node_rows, top, bottom, halo, degrees, 0, half)

    force, table = lax.optimization_barrier((force, table))
    slot_index = source_owner[:, 0] * node_count + source_node
    velocity = jnp.take(table, slot_index, axis=0, mode="clip")

    panel_size = kernel.shape[3]
    source_cells = velocity.reshape(-1, panel_size, vectors)
    pressure, load_value = near_field(kernel, source_cells, areas, near_cells, 0)

    load_owner = target_owner[:, 0]
    target_count = load_owner.shape[0]
    load_capacity = 5 * target_count // (2 * sectors)
    load_slot = slot_positions(load_owner, sectors, load_capacity)
    gather_slot = (
        load_slot[None, :] == jnp.arange(sectors * load_capacity, dtype=jnp.int32)[:, None]
    ).astype(jnp.bfloat16)
    outgoing = jnp.dot(gather_slot, load_value, preferred_element_type=jnp.float32).astype(
        jnp.bfloat16
    )
    outgoing = outgoing.reshape(sectors, load_capacity, vectors)
    radix = 32
    digits = jnp.stack([target_node // radix, target_node % radix], axis=0).astype(jnp.bfloat16)
    slot_digits = lax.dot_general(
        digits, gather_slot, (((1,), (1,)), ((), ())), preferred_element_type=jnp.float32
    ).astype(jnp.bfloat16)
    slot_digits = jnp.transpose(slot_digits.reshape(2, sectors, load_capacity), (1, 0, 2))
    digit_rows = -(-2 * load_capacity // vectors)
    slot_digits = jnp.pad(
        slot_digits.reshape(sectors, 2 * load_capacity),
        ((0, 0), (0, digit_rows * vectors - 2 * load_capacity)),
    ).reshape(sectors, digit_rows, vectors)
    packet = jnp.concatenate([outgoing, slot_digits], axis=1)
    packet, force, pressure = lax.optimization_barrier((packet, force, pressure))
    arrived = lax.all_to_all(packet, "circ", split_axis=0, concat_axis=0, tiled=True)
    force = banded_force(
        blocks, node_rows, top, bottom, halo, degrees, half, axial_rows - half, force
    )
    pressure = near_field(kernel, source_cells, areas, near_cells, 1, pressure)[0]
    arrived_load = arrived[:, :load_capacity].reshape(-1, vectors)
    arrived_digits = (
        arrived[:, load_capacity:]
        .reshape(sectors, digit_rows * vectors)[:, : 2 * load_capacity]
        .reshape(sectors, 2, load_capacity)
        .astype(jnp.float32)
    )
    arrived_node = (arrived_digits[:, 0] * radix + arrived_digits[:, 1]).astype(jnp.int32)
    selector = (
        arrived_node.reshape(-1)[None, :] == jnp.arange(node_count, dtype=jnp.int32)[:, None]
    ).astype(jnp.bfloat16)
    fluid = jnp.dot(selector, arrived_load, preferred_element_type=jnp.float32)
    fluid = fluid.reshape(axial_rows, circum_rows, vectors)
    force = force.at[:, :circum_rows, :].add(-fluid)
    shell_force = jnp.transpose(
        force.reshape(axial_rows, degrees, circum_rows, vectors), (0, 2, 1, 3)
    )
    return (shell_force, pressure)


def solution(mesh):
    return jax.shard_map(
        body,
        mesh=mesh,
        in_specs=(
            P("ax", "circ", None, None),
            P("ax", "circ", None),
            P(("ax", "circ"), None, None, None, None),
            P(("ax", "circ")),
            P(("ax", "circ"), None),
            P(("ax", "circ"), None),
            P(("ax", "circ")),
            P(("ax", "circ"), None),
            P(("ax", "circ")),
        ),
        out_specs=(P("ax", "circ", None, None), P(None, ("ax", "circ"), None)),
        check_vma=False,
    )
```

```python
import functools

import jax
import jax.numpy as jnp
from jax import lax
from jax.experimental import pallas as pl
from jax.experimental.pallas import tpu as pltpu
from jax.sharding import PartitionSpec as P


def extended(cells, sides, width):
    for axis, dim in sides:
        count = lax.axis_size(axis)
        head = lax.slice_in_dim(cells, 0, width, axis=dim)
        tail = lax.slice_in_dim(cells, cells.shape[dim] - width, cells.shape[dim], axis=dim)
        cells = jnp.concatenate(
            [
                lax.ppermute(tail, axis, [(i, (i + 1) % count) for i in range(count)]),
                cells,
                lax.ppermute(head, axis, [((i + 1) % count, i) for i in range(count)]),
            ],
            axis=dim,
        )
    return cells


def slot_positions(owners, sectors, capacity):
    onehot = owners[:, None] == jnp.arange(sectors, dtype=jnp.int32)[None, :]
    count = owners.shape[0]
    order = jnp.arange(count, dtype=jnp.int32)
    earlier = (order[None, :] < order[:, None]).astype(jnp.bfloat16)
    before = jnp.dot(earlier, onehot.astype(jnp.bfloat16), preferred_element_type=jnp.float32)
    ranking = jnp.sum(jnp.where(onehot, before, 0.0), axis=1).astype(jnp.int32)
    return owners * capacity + ranking


def pressure_kernel(near_ref, kern_ref, vel_ref, area_ref, *rest, with_load):
    p_ref = rest[-2] if with_load else rest[-1]
    g = pl.program_id(0)
    near_count = kern_ref.shape[1]
    for n in range(near_count):
        m = near_ref[g, n]
        prod = jnp.dot(kern_ref[0, n, 0], vel_ref[m], preferred_element_type=jnp.float32)
        if n == 0:
            p_ref[0] = prod
        else:
            p_ref[0] += prod
    if with_load:
        load_ref = rest[-1]
        load_ref[...] = (area_ref[...] * p_ref[0]).astype(load_ref.dtype)


def near_field(kernel, source_cells, areas, near_cells, part, previous=None):
    cells_dev, near_count, _, panel, _ = kernel.shape
    src_cells, _, vectors = source_cells.shape
    targets = cells_dev * panel
    with_load = previous is None
    in_specs = [
        pl.BlockSpec((1, near_count, 1, panel, panel), lambda g, near: (g, 0, part, 0, 0)),
        pl.BlockSpec((src_cells, panel, vectors), lambda g, near: (0, 0, 0)),
        pl.BlockSpec((panel, 1), lambda g, near: (g, 0)),
    ]
    operands = [near_cells, kernel, source_cells, areas.reshape(targets, 1)]
    out_specs = [pl.BlockSpec((1, panel, vectors), lambda g, near: (part, g, 0))]
    out_shape = [jax.ShapeDtypeStruct((2, targets, vectors), jnp.float32)]
    aliases = {}
    if with_load:
        out_specs.append(pl.BlockSpec((panel, vectors), lambda g, near: (g, 0)))
        out_shape.append(jax.ShapeDtypeStruct((targets, vectors), jnp.bfloat16))
    else:
        in_specs.append(pl.BlockSpec(memory_space=pl.ANY))
        operands.append(previous)
        aliases = {len(operands) - 1: 0}
    grid_spec = pltpu.PrefetchScalarGridSpec(
        num_scalar_prefetch=1, grid=(cells_dev,), in_specs=in_specs, out_specs=out_specs
    )
    return pl.pallas_call(
        functools.partial(pressure_kernel, with_load=with_load),
        grid_spec=grid_spec,
        out_shape=out_shape,
        input_output_aliases=aliases,
    )(*operands)


def stiff_kernel(s_ref, rows_ref, top_ref, bottom_ref, halo_ref, *rest, degrees, first):
    out_ref, sel_ref, band_ref = rest[-3:]
    step = pl.program_id(0)
    a = step + first
    last = rows_ref.shape[0] - 1
    nodes = s_ref.shape[1]
    offsets = band_ref.shape[0]
    group = 128
    span = offsets * degrees
    wide = band_ref.shape[2]

    per_tile = group // span

    @pl.when(step == 0)
    def _():
        k = lax.broadcasted_iota(jnp.int32, sel_ref.shape, 0)
        y = lax.broadcasted_iota(jnp.int32, sel_ref.shape, 1)
        lane = y % group
        blk = (y // group) * per_tile + lane // span
        inner = lane % span
        target = (
            (blk // degrees) * (offsets * degrees * degrees)
            + (inner // degrees) * (degrees * degrees)
            + (blk % degrees) * degrees
            + inner % degrees
        )
        valid = (lane < per_tile * span) & (blk < offsets * degrees)
        sel_ref[...] = jnp.where(valid & (k == target), 1.0, 0.0).astype(sel_ref.dtype)
        band_ref[...] = jnp.zeros(band_ref.shape, band_ref.dtype)

    spread = jnp.dot(s_ref[0], sel_ref[...], preferred_element_type=jnp.float32)
    pad = jnp.zeros((8, group), jnp.float32)
    tiles = wide // group
    lane_id = lax.broadcasted_iota(jnp.int32, (nodes, group), 1)
    for d in range(offsets):
        for i in range(degrees):
            blk = d * degrees + i
            b, q = blk // per_tile, blk % per_tile
            piece = spread[:, b * group : (b + 1) * group]
            piece = jnp.where(
                (lane_id >= q * span) & (lane_id < (q + 1) * span), piece, jnp.zeros_like(piece)
            )
            for h in range(nodes // 16):
                base = 16 * h * degrees - degrees
                tile = base // group
                parts = []
                for g in (2 * h, 2 * h + 1):
                    rows = jnp.concatenate([piece[g * 8 : (g + 1) * 8], pad], axis=1)
                    shift = (8 * g * degrees - degrees - tile * group - q * span) % (2 * group)
                    rows = pltpu.roll(rows, shift, 1)
                    parts.append(pltpu.roll(rows, 0, 1, stride=degrees, stride_axis=0))
                window = jnp.concatenate(parts, axis=0).astype(band_ref.dtype)
                top_row = i * nodes + 16 * h
                for t in range(2):
                    lane = ((tile + t) % tiles) * group
                    band_ref[d, top_row : top_row + 16, lane : lane + group] = window[
                        :, t * group : (t + 1) * group
                    ]
    above = jnp.where(a == 0, top_ref[0], rows_ref[jnp.maximum(a - 1, 0)])
    below = jnp.where(a == last, bottom_ref[0], rows_ref[jnp.minimum(a + 1, last)])
    acc = None
    for d, rows in enumerate((above, rows_ref[a], below)):
        both = jnp.concatenate([rows, halo_ref[a + d]], axis=0)
        part = jnp.dot(band_ref[d], both, preferred_element_type=jnp.float32)
        acc = part if acc is None else acc + part
    out_ref[0] = acc


def banded_force(blocks, rows, top, bottom, halo, degrees, first, count, previous=None):
    axial_rows, nodes, width = blocks.shape
    offsets = 3
    vectors = rows.shape[-1]
    band_rows = degrees * nodes
    band_cols = band_rows + halo.shape[1]
    sel_cols = -(-offsets * degrees // (128 // (offsets * degrees))) * 128
    in_specs = [
        pl.BlockSpec((1, nodes, width), lambda a: (a + first, 0, 0)),
        pl.BlockSpec(rows.shape, lambda a: (0, 0, 0)),
        pl.BlockSpec(top.shape, lambda a: (0, 0, 0)),
        pl.BlockSpec(bottom.shape, lambda a: (0, 0, 0)),
        pl.BlockSpec(halo.shape, lambda a: (0, 0, 0)),
    ]
    operands = [blocks, rows, top, bottom, halo]
    aliases = {}
    if previous is not None:
        in_specs.append(pl.BlockSpec(memory_space=pl.ANY))
        operands.append(previous)
        aliases = {len(operands) - 1: 0}
    return pl.pallas_call(
        functools.partial(stiff_kernel, degrees=degrees, first=first),
        grid=(count,),
        in_specs=in_specs,
        out_specs=pl.BlockSpec((1, band_rows, vectors), lambda a: (a + first, 0, 0)),
        out_shape=jax.ShapeDtypeStruct((axial_rows, band_rows, vectors), jnp.float32),
        scratch_shapes=[
            pltpu.VMEM((width, sel_cols), jnp.bfloat16),
            pltpu.VMEM((offsets, band_rows, band_cols), jnp.bfloat16),
        ],
        input_output_aliases=aliases,
    )(*operands)


def body(
    displacement,
    stiffness,
    kernel,
    areas,
    near_cells,
    source_owner,
    source_node,
    target_owner,
    target_node,
):
    axial_rows = displacement.shape[0]
    circum_rows = displacement.shape[1]
    degrees = displacement.shape[2]
    vectors = displacement.shape[3]
    sectors = lax.axis_size("circ")
    axial_total = axial_rows * lax.axis_size("ax")
    node_count = axial_rows * circum_rows

    radial = displacement[:, :, 0, :].reshape(node_count, vectors)
    table = lax.all_gather(radial, "circ", axis=0, tiled=True)

    node_rows = displacement.reshape(axial_rows, circum_rows * degrees, vectors)
    count_ax = lax.axis_size("ax")
    top = lax.ppermute(node_rows[-1:], "ax", [(i, (i + 1) % count_ax) for i in range(count_ax)])
    bottom = lax.ppermute(node_rows[:1], "ax", [((i + 1) % count_ax, i) for i in range(count_ax)])
    first_nodes = jnp.concatenate(
        [top[:, :degrees], node_rows[:, :degrees], bottom[:, :degrees]], axis=0
    )
    last_nodes = jnp.concatenate(
        [top[:, -degrees:], node_rows[:, -degrees:], bottom[:, -degrees:]], axis=0
    )
    left = lax.ppermute(last_nodes, "circ", [(i, (i + 1) % sectors) for i in range(sectors)])
    right = lax.ppermute(first_nodes, "circ", [((i + 1) % sectors, i) for i in range(sectors)])
    gap = jnp.zeros((axial_rows + 2, 128 - 2 * degrees, vectors), displacement.dtype)
    halo = jnp.concatenate([right, gap, left], axis=1)
    global_row = lax.axis_index("ax") * axial_rows + jnp.arange(axial_rows, dtype=jnp.int32)
    lane_step = jnp.arange(stiffness.shape[2], dtype=jnp.int32) // (3 * degrees * degrees) - 1
    inside = (global_row[:, None] + lane_step[None, :] >= 0) & (
        global_row[:, None] + lane_step[None, :] < axial_total
    )
    blocks = jnp.where(inside[:, None, :], stiffness, jnp.zeros_like(stiffness))
    half = axial_rows // 2
    force = banded_force(blocks, node_rows, top, bottom, halo, degrees, 0, half)

    force, table = lax.optimization_barrier((force, table))
    slot_index = source_owner[:, 0] * node_count + source_node
    velocity = table.at[slot_index].get(mode="promise_in_bounds")

    panel_size = kernel.shape[3]
    source_cells = velocity.reshape(-1, panel_size, vectors)
    pressure, load_value = near_field(kernel, source_cells, areas, near_cells, 0)

    load_owner = target_owner[:, 0]
    target_count = load_owner.shape[0]
    load_capacity = 5 * target_count // (2 * sectors)
    load_slot = slot_positions(load_owner, sectors, load_capacity)
    gather_slot = (
        load_slot[None, :] == jnp.arange(sectors * load_capacity, dtype=jnp.int32)[:, None]
    ).astype(jnp.bfloat16)
    outgoing = jnp.dot(gather_slot, load_value, preferred_element_type=jnp.float32).astype(
        jnp.bfloat16
    )
    outgoing = outgoing.reshape(sectors, load_capacity, vectors)
    radix = 32
    digits = jnp.stack([target_node // radix, target_node % radix], axis=0).astype(jnp.bfloat16)
    slot_digits = lax.dot_general(
        digits, gather_slot, (((1,), (1,)), ((), ())), preferred_element_type=jnp.float32
    ).astype(jnp.bfloat16)
    slot_digits = jnp.transpose(slot_digits.reshape(2, sectors, load_capacity), (1, 0, 2))
    digit_rows = -(-2 * load_capacity // vectors)
    slot_digits = jnp.pad(
        slot_digits.reshape(sectors, 2 * load_capacity),
        ((0, 0), (0, digit_rows * vectors - 2 * load_capacity)),
    ).reshape(sectors, digit_rows, vectors)
    packet = jnp.concatenate([outgoing, slot_digits], axis=1)
    packet, force, pressure = lax.optimization_barrier((packet, force, pressure))
    arrived = lax.all_to_all(packet, "circ", split_axis=0, concat_axis=0, tiled=True)
    force = banded_force(
        blocks, node_rows, top, bottom, halo, degrees, half, axial_rows - half, force
    )
    pressure = near_field(kernel, source_cells, areas, near_cells, 1, pressure)[0]
    arrived_load = arrived[:, :load_capacity].reshape(-1, vectors)
    arrived_digits = (
        arrived[:, load_capacity:]
        .reshape(sectors, digit_rows * vectors)[:, : 2 * load_capacity]
        .reshape(sectors, 2, load_capacity)
        .astype(jnp.float32)
    )
    arrived_node = (arrived_digits[:, 0] * radix + arrived_digits[:, 1]).astype(jnp.int32)
    selector = (
        arrived_node.reshape(-1)[None, :] == jnp.arange(node_count, dtype=jnp.int32)[:, None]
    ).astype(jnp.bfloat16)
    fluid = jnp.dot(selector, arrived_load, preferred_element_type=jnp.float32)
    fluid = fluid.reshape(axial_rows, circum_rows, vectors)
    force = force.at[:, :circum_rows, :].add(-fluid)
    shell_force = jnp.transpose(
        force.reshape(axial_rows, degrees, circum_rows, vectors), (0, 2, 1, 3)
    )
    return (shell_force, pressure)


def solution(mesh):
    return jax.shard_map(
        body,
        mesh=mesh,
        in_specs=(
            P("ax", "circ", None, None),
            P("ax", "circ", None),
            P(("ax", "circ"), None, None, None, None),
            P(("ax", "circ")),
            P(("ax", "circ"), None),
            P(("ax", "circ"), None),
            P(("ax", "circ")),
            P(("ax", "circ"), None),
            P(("ax", "circ")),
        ),
        out_specs=(P("ax", "circ", None, None), P(None, ("ax", "circ"), None)),
        check_vma=False,
    )
```
